32 devices in a mesh: basin: 8 (over z, y), band: 4 (over x, core).
Axes of the slice: x: 2, y: 2, z: 4, core: 2. Of those that a mesh axis runs over, the one named last changes fastest.
Arguments:
- precip: float32 [6144, 8, 128], P(('basin', 'band')), may hold values from 0.002 to 0.02
- soil_water: float32 [6144, 128], P(('basin', 'band')), may hold values from 0.1 to 1
- capacity: float32 [6144, 128], P(('basin', 'band')), may hold values from 0.1 to 1
- evap_rate: float32 [6144, 128], P(('basin', 'band')), may hold values from 0.01 to 0.1
- tile_dest: int32 [6144], P(('basin', 'band')), may hold values from 0 to 31, as said below
- tile_block: int32 [6144], P(('basin', 'band')), may hold values from 0 to 7
- trib_op: float32 [256, 128, 128], P(('basin', 'band')), may hold values from 0 to 1
- trib_keep: float32 [256, 128], P(('basin', 'band')), may hold values from 0.01 to 0.6
- trib_prev: float32 [256, 128], P(('basin', 'band')), may hold values from 0 to 0.5
- trib_river: int32 [256], P(('basin', 'band')), may hold values from 0 to 3, as said below
- trib_reach: int32 [256], P(('basin', 'band')), may hold values from 0 to 127
- main_op: float32 [4, 8, 128, 128], P('band', 'basin'), may hold values from 0 to 1
- main_keep: float32 [4, 8, 128], P('band', 'basin'), may hold values from 0.002 to 0.1
- main_prev: float32 [4, 8, 128], P('band', 'basin'), may hold values from 0 to 4
- head_inflow: float32 [4, 8], P('band'), may hold values from 0.5 to 2
Outputs:
- soil_final: float32 [6144, 128], P(('basin', 'band'))
- trib_final: float32 [256, 128], P(('basin', 'band'))
- main_flow: float32 [4, 8, 8, 128], P('band', 'basin')
The draws below stay inside these ranges and needn't reach their ends.
Inputs may be any that keep to these rules, and one draw needn't show every extreme that they name: `tile_dest`: among the 192 tiles of one device, at most 12 name the same owner. `trib_river`: among the 8 tributary blocks of one device, at most 4 name the same river.
All inputs are finite; a program needn't handle non-finite values.
Results may differ from the reference program's by a relative error of at most 0.00016.
Values sent between devices are 32-bit elements; how exact they have to be, the bound alone decides.
No kernel may reach another device: no remote copies, remote signals or barrier semaphores. Data moves between devices by JAX's collectives and lax.ppermute only.
A program may use at most 64 MiB of HBM per device.

```python
import math
import jax
import jax.numpy as jnp
from jax import lax

R = 128
SUB = 8
TILE_DEV = 192
BLK_DEV = 8
CHAIN = 8
RIVERS = 4
SHARDS = 32
TILES = 6144
NBLK = 256
CAP = 12
BRANCH_CAP = 4


def pick_peers(key, groups, members, peer_count, slot_cap, wanted):
    keys = jax.random.split(key, 4)
    slot_total = peer_count * slot_cap
    slot_ids = jnp.arange(slot_total, dtype=jnp.int32)
    owner_ids = slot_ids // slot_cap
    preference = jax.random.randint(keys[0], (groups, 1, peer_count), 0, 4096, dtype=jnp.int32)
    jitter = jax.random.randint(keys[1], (groups, members, slot_total), 0, 4096, dtype=jnp.int32)
    hot_peer = jax.random.randint(keys[2], (groups, 1, 1), 0, peer_count, dtype=jnp.int32)
    scores = (jnp.take(preference, owner_ids, axis=2) + jitter) * slot_total + slot_ids
    scores = scores + jnp.where(owner_ids == hot_peer, 268435456, 0).astype(jnp.int32)
    chosen = lax.top_k(scores, wanted)[1]
    peer_ids = (chosen // slot_cap).astype(jnp.int32)
    return jax.random.permutation(keys[3], peer_ids, axis=2, independent=True)


def draw_tile_dest(key, part):
    peer_ids = pick_peers(jax.random.fold_in(key, 11), 1, SHARDS, SHARDS, CAP, TILE_DEV)
    return peer_ids.reshape(TILES)


def draw_trib_river(key, part):
    peer_ids = pick_peers(jax.random.fold_in(key, 12), CHAIN, RIVERS, RIVERS, BRANCH_CAP, BLK_DEV)
    return peer_ids.reshape(NBLK)


def draw_trib_op(key, part):
    off_diag = jax.random.uniform(jax.random.fold_in(key, 13), (NBLK, R, R), jnp.float32, 0.0, 2.0) / R
    lower_mask = jnp.tril(jnp.ones((R, R), jnp.float32), -1)
    return off_diag * lower_mask + jnp.eye(R, dtype=jnp.float32)


def draw_main_op(key, part):
    keys = jax.random.split(jax.random.fold_in(key, 14), 2)
    off_diag = jax.random.uniform(keys[0], (RIVERS, CHAIN, R, R), jnp.float32, 0.0, 2.0) / R
    first_col = jax.random.uniform(keys[1], (RIVERS, CHAIN, R, 1), jnp.float32, 1.0 - 3.0 / CHAIN, 1.0)
    lower_mask = jnp.tril(jnp.ones((R, R), jnp.float32), -1)
    column_zero = (jnp.arange(R) == 0)[None, :]
    return jnp.where(column_zero, first_col, off_diag) * lower_mask + jnp.eye(R, dtype=jnp.float32)


def with_ends(values, stream_key, low, top_value):
    shape = values.shape
    spot = [jax.random.randint(jax.random.fold_in(stream_key, axis), (), 0, shape[axis]) for axis in range(len(shape))]
    values = values.at[tuple(spot)].set(low)
    longest = shape.index(max(shape))
    spot[longest] = (spot[longest] + 1) % shape[longest]
    return values.at[tuple(spot)].set(top_value)


def shard_levels(stream_key, dims, cuts, smallest, high):
    gain, own = 1.0, jax.random.fold_in(stream_key, 6)
    for position, blocks in cuts:
        heights = jnp.exp(jax.random.uniform(jax.random.fold_in(own, position), (blocks,), jnp.float32, smallest / len(cuts), high / len(cuts)))
        gain = gain * jnp.repeat(heights, dims[position] // blocks).reshape([-1 if axis == position else 1 for axis in range(len(dims))])
    return gain


def setup_inputs(seed: int = 0) -> dict:
    streams_of = jax.random.split(jax.random.key(seed), 16)
    precip = jnp.clip(jnp.exp(math.log(0.02) - 2.30258502 * jax.random.uniform(streams_of[0], (TILES, SUB, R), jnp.float32) ** shard_levels(streams_of[0], (TILES, SUB, R), ((0, 32),), -0.2, 0.2)), 0.002, 0.02)
    soil_water = jnp.clip(0.1 + 0.9 * jax.random.uniform(streams_of[1], (TILES, R), jnp.float32) ** shard_levels(streams_of[1], (TILES, R), ((0, 32),), -0.2, 0.2), 0.1, 1.0)
    capacity = jnp.clip(jnp.exp(math.log(1.0) - 2.3025851 * jax.random.uniform(streams_of[2], (TILES, R), jnp.float32) ** shard_levels(streams_of[2], (TILES, R), ((0, 32),), -0.2, 0.2)), 0.1, 1.0)
    evap_rate = jnp.clip(jnp.exp(math.log(0.1) - 2.3025851 * jax.random.uniform(streams_of[3], (TILES, R), jnp.float32) ** shard_levels(streams_of[3], (TILES, R), ((0, 32),), -0.2, 0.2)), 0.01, 0.1)
    tile_dest = draw_tile_dest(jax.random.fold_in(streams_of[15], 71), 0)
    tile_block = with_ends(jax.random.randint(streams_of[5], (TILES,), 0, BLK_DEV), jax.random.fold_in(streams_of[5], 1), 0, BLK_DEV - 1).astype(jnp.int32)
    trib_op = draw_trib_op(jax.random.fold_in(streams_of[15], 71), 0)
    trib_keep = jnp.clip(jnp.exp(math.log(0.6) - 4.0943446 * jax.random.uniform(streams_of[7], (NBLK, R), jnp.float32) ** shard_levels(streams_of[7], (NBLK, R), ((0, 32),), -0.2, 0.2)), 0.01, 0.6)
    trib_prev = jnp.clip(0.5 * jax.random.uniform(streams_of[8], (NBLK, R), jnp.float32) ** shard_levels(streams_of[8], (NBLK, R), ((0, 32),), -0.2, 0.2), 0.0, 0.5)
    trib_river = draw_trib_river(jax.random.fold_in(streams_of[15], 71), 0)
    trib_reach = with_ends(jax.random.randint(streams_of[10], (NBLK,), 0, R), jax.random.fold_in(streams_of[10], 1), 0, R - 1).astype(jnp.int32)
    main_op = draw_main_op(jax.random.fold_in(streams_of[15], 71), 0)
    main_keep = jnp.clip(jnp.exp(math.log(0.1) - 3.912023 * jax.random.uniform(streams_of[12], (RIVERS, CHAIN, R), jnp.float32) ** shard_levels(streams_of[12], (RIVERS, CHAIN, R), ((0, 4), (1, 8)), -0.2, 0.2)), 0.002, 0.1)
    main_prev = jnp.clip(4.0 * jax.random.uniform(streams_of[13], (RIVERS, CHAIN, R), jnp.float32) ** shard_levels(streams_of[13], (RIVERS, CHAIN, R), ((0, 4), (1, 8)), -0.2, 0.2), 0.0, 4.0)
    head_inflow = jnp.clip(0.5 + 1.5 * jax.random.uniform(streams_of[14], (RIVERS, SUB), jnp.float32) ** shard_levels(streams_of[14], (RIVERS, SUB), ((0, 4),), -0.2, 0.2), 0.5, 2.0)
    return {"precip": precip, "soil_water": soil_water, "capacity": capacity, "evap_rate": evap_rate, "tile_dest": tile_dest, "tile_block": tile_block, "trib_op": trib_op, "trib_keep": trib_keep, "trib_prev": trib_prev, "trib_river": trib_river, "trib_reach": trib_reach, "main_op": main_op, "main_keep": main_keep, "main_prev": main_prev, "head_inflow": head_inflow}


def land_update_steps(precip, soil_water, capacity, evap_rate):
    water = soil_water
    runoff_steps = []
    for sub_step in range(precip.shape[1]):
        rain_now = precip[:, sub_step]
        runoff_now = rain_now * water / (water + capacity)
        water = (1.0 - evap_rate) * water + rain_now - runoff_now
        runoff_steps.append(runoff_now)
    return runoff_steps, water


def route_series(mixed, keep, previous):
    flow = previous
    flows = []
    for sub_step in range(mixed.shape[-2]):
        flow = keep * flow + (1.0 - keep) * mixed[..., sub_step, :]
        flows.append(flow)
    return jnp.stack(flows, axis=-2)


def reference(precip, soil_water, capacity, evap_rate, tile_dest, tile_block, trib_op, trib_keep, trib_prev, trib_river, trib_reach, main_op, main_keep, main_prev, head_inflow):
    runoff_steps, water = land_update_steps(precip, soil_water, capacity, evap_rate)
    block_ids = (tile_dest * BLK_DEV + tile_block).astype(jnp.int32)
    lateral = jnp.stack([jax.ops.segment_sum(piece, block_ids, num_segments=NBLK) for piece in runoff_steps], axis=1)
    trib_mixed = jnp.einsum("brc,btc->btr", trib_op, lateral, precision=lax.Precision.HIGHEST)
    trib_flows = route_series(trib_mixed, trib_keep, trib_prev)
    outlet = trib_flows[:, :, R - 1]
    section = (jnp.arange(NBLK, dtype=jnp.int32) // BLK_DEV) // RIVERS
    join_ids = ((trib_river * CHAIN + section) * R + trib_reach).astype(jnp.int32)
    branch_in = jax.ops.segment_sum(outlet, join_ids, num_segments=RIVERS * CHAIN * R)
    branch_in = jnp.transpose(branch_in.reshape(RIVERS, CHAIN, R, SUB), (0, 1, 3, 2))
    first_reach = (jnp.arange(R) == 0).astype(jnp.float32)

    def river_chain(head, operators, keeps, previous_flows, inflows):
        def advance(entry, piece):
            operator, keep, previous, inflow = piece
            fed = inflow + entry[:, None] * first_reach[None, :]
            mixed = jnp.einsum("rc,tc->tr", operator, fed, precision=lax.Precision.HIGHEST)
            flows = route_series(mixed, keep, previous)
            return flows[:, R - 1], flows

        last_exit, flows = lax.scan(advance, head, (operators, keeps, previous_flows, inflows))
        return flows

    main_flow = jax.vmap(river_chain)(head_inflow, main_op, main_keep, main_prev, branch_in)
    return water, trib_flows[:, SUB - 1], main_flow
```

```python
import jax
import jax.numpy as jnp
from jax import lax
from jax.sharding import PartitionSpec as P


def land_update(precip, soil_water, capacity, evap_rate):
    water = soil_water
    runoff_steps = []
    for sub_step in range(precip.shape[1]):
        rain_now = precip[:, sub_step]
        runoff_now = rain_now * water / (water + capacity)
        water = (1.0 - evap_rate) * water + rain_now - runoff_now
        runoff_steps.append(runoff_now)
    return (jnp.stack(runoff_steps, axis=1), water)


def route_series(mixed, keep, previous):
    flow = previous
    flows = []
    for sub_step in range(mixed.shape[-2]):
        flow = keep * flow + (1.0 - keep) * mixed[..., sub_step, :]
        flows.append(flow)
    return jnp.stack(flows, axis=-2)


def pack_slots(values, labels, targets, peer_count, slot_cap):
    entries = targets.shape[0]
    position = jnp.arange(entries, dtype=jnp.int32)
    earlier = (targets[:, None] == targets[None, :]) & (position[None, :] < position[:, None])
    ranking = jnp.sum(earlier.astype(jnp.int32), axis=1)
    target_slot = targets * slot_cap + ranking
    buffer = (
        jnp.zeros((peer_count * slot_cap, values.shape[1]), values.dtype)
        .at[target_slot]
        .set(values)
    )
    slot_labels = jnp.zeros((peer_count * slot_cap,), jnp.int32).at[target_slot].set(labels)
    return (buffer, slot_labels)


def gather_lateral(runoff, tile_dest, tile_block, blocks, shards):
    tile_count, width = runoff.shape
    tile_cap = max(2, 2 * tile_count // shards)
    grid = ("basin", "band")
    if tile_cap >= blocks:
        block_ids = tile_dest * blocks + tile_block
        pick = (
            block_ids[None, :] == jnp.arange(shards * blocks, dtype=jnp.int32)[:, None]
        ).astype(jnp.float32)
        dense = jnp.dot(pick, runoff, precision=lax.Precision.HIGHEST)
        arrived = lax.all_to_all(
            dense.reshape(shards, blocks, width), grid, split_axis=0, concat_axis=0, tiled=True
        )
        return jnp.sum(arrived, axis=0)
    buffer, slot_labels = pack_slots(runoff, tile_block, tile_dest, shards, tile_cap)
    arrived = lax.all_to_all(
        buffer.reshape(shards, tile_cap, width), grid, split_axis=0, concat_axis=0, tiled=True
    )
    arrived_ids = lax.all_to_all(
        slot_labels.reshape(shards, tile_cap), grid, split_axis=0, concat_axis=0, tiled=True
    )
    block_pick = (
        arrived_ids.reshape(-1)[:, None] == jnp.arange(blocks, dtype=jnp.int32)[None, :]
    ).astype(jnp.float32)
    return jnp.einsum(
        "sk,sx->kx", block_pick, arrived.reshape(-1, width), precision=lax.Precision.HIGHEST
    )


def local(
    precip,
    soil_water,
    capacity,
    evap_rate,
    tile_dest,
    tile_block,
    trib_op,
    trib_keep,
    trib_prev,
    trib_river,
    trib_reach,
    main_op,
    main_keep,
    main_prev,
    head_inflow,
):
    tile_count = precip.shape[0]
    sub_steps = precip.shape[1]
    reaches = precip.shape[2]
    blocks = trib_op.shape[0]
    chains = lax.axis_size("basin")
    rivers = lax.axis_size("band")
    shards = chains * rivers
    grid = ("basin", "band")
    operator = main_op[0, 0]
    keep_main = main_keep[0, 0]
    prev_main = main_prev[0, 0]

    runoff, water = land_update(precip, soil_water, capacity, evap_rate)
    lateral = gather_lateral(
        runoff.reshape(tile_count, sub_steps * reaches), tile_dest, tile_block, blocks, shards
    )
    trib_mixed = jnp.einsum(
        "brc,btc->btr",
        trib_op,
        lateral.reshape(blocks, sub_steps, reaches),
        precision=lax.Precision.HIGHEST,
    )
    trib_flows = route_series(trib_mixed, trib_keep, trib_prev)
    outlet = trib_flows[:, :, reaches - 1]

    payload = jnp.concatenate(
        [
            outlet.reshape(-1),
            trib_river.astype(jnp.float32),
            trib_reach.astype(jnp.float32),
            operator[reaches - 1],
            keep_main[reaches - 1 :],
            prev_main[reaches - 1 :],
        ]
    )
    width = payload.shape[0]
    padded = -(-width // 128) * 128
    payload = jnp.pad(payload, (0, padded - width))
    every = lax.all_gather(payload, grid, axis=0, tiled=False)

    mine = lax.axis_index("band")
    me = lax.axis_index("basin")
    at = 0
    outlets = every[:, at : at + blocks * sub_steps].reshape(chains, rivers * blocks, sub_steps)
    at += blocks * sub_steps
    river_of = every[:, at : at + blocks].reshape(chains, rivers * blocks)
    at += blocks
    reach_of = every[:, at : at + blocks].reshape(chains, rivers * blocks)
    at += blocks
    exit_rows = lax.dynamic_index_in_dim(
        every[:, at : at + reaches].reshape(chains, rivers, reaches), mine, axis=1, keepdims=False
    )
    at += reaches
    keeps = lax.dynamic_index_in_dim(
        every[:, at].reshape(chains, rivers), mine, axis=1, keepdims=False
    )
    starts = lax.dynamic_index_in_dim(
        every[:, at + 1].reshape(chains, rivers), mine, axis=1, keepdims=False
    )

    joins = (river_of == mine.astype(jnp.float32))[:, :, None] & (
        reach_of[:, :, None] == jnp.arange(reaches, dtype=jnp.float32)[None, None, :]
    )
    weight = joins.astype(jnp.float32)
    branch_all = jnp.sum(weight[:, :, None, :] * outlets[:, :, :, None], axis=1)
    branch_exit = jnp.sum(branch_all * exit_rows[:, None, :], axis=2)

    flow = starts
    free_exit = []
    for sub_step in range(sub_steps):
        flow = keeps * flow + (1.0 - keeps) * branch_exit[:, sub_step]
        free_exit.append(flow)
    free_exit = jnp.stack(free_exit, axis=1)
    lag = jnp.arange(sub_steps)[:, None] - jnp.arange(sub_steps)[None, :]
    lag_f = jnp.maximum(lag, 0).astype(jnp.float32)
    response = jnp.where(
        lag[None] >= 0,
        (exit_rows[:, 0] * (1.0 - keeps))[:, None, None] * keeps[:, None, None] ** lag_f[None],
        0.0,
    )

    def advance(section, entry):
        moved = jnp.sum(response[section] * entry[None, :], axis=1) + free_exit[section]
        return jnp.where(section < me, moved, entry)

    entry = lax.fori_loop(0, chains, advance, head_inflow[0], unroll=chains <= 16)

    branch_in = lax.dynamic_index_in_dim(branch_all, me, axis=0, keepdims=False)
    first_reach = (jnp.arange(reaches) == 0).astype(jnp.float32)
    fed = branch_in + entry[:, None] * first_reach[None, :]
    main_mixed = jnp.einsum("rc,tc->tr", operator, fed, precision=lax.Precision.HIGHEST)
    main_flows = route_series(main_mixed, keep_main, prev_main)
    return (water, trib_flows[:, sub_steps - 1], main_flows[None, None])


def solution(mesh):
    return jax.shard_map(
        local,
        mesh=mesh,
        in_specs=(
            P(("basin", "band"), None, None),
            P(("basin", "band"), None),
            P(("basin", "band"), None),
            P(("basin", "band"), None),
            P(("basin", "band")),
            P(("basin", "band")),
            P(("basin", "band"), None, None),
            P(("basin", "band"), None),
            P(("basin", "band"), None),
            P(("basin", "band")),
            P(("basin", "band")),
            P("band", "basin", None, None),
            P("band", "basin", None),
            P("band", "basin", None),
            P("band", None),
        ),
        out_specs=(
            P(("basin", "band"), None),
            P(("basin", "band"), None),
            P("band", "basin", None, None),
        ),
        check_vma=False,
    )
```

```python
import jax
import jax.numpy as jnp
from jax import lax
from jax.sharding import PartitionSpec as P


def land_update(precip, soil_water, capacity, evap_rate):
    water = soil_water
    runoff_steps = []
    for sub_step in range(precip.shape[1]):
        rain_now = precip[:, sub_step]
        runoff_now = rain_now * water / (water + capacity)
        water = (1.0 - evap_rate) * water + rain_now - runoff_now
        runoff_steps.append(runoff_now)
    return (jnp.stack(runoff_steps, axis=1), water)


def route_series(mixed, keep, previous):
    flow = previous
    flows = []
    for sub_step in range(mixed.shape[-2]):
        flow = keep * flow + (1.0 - keep) * mixed[..., sub_step, :]
        flows.append(flow)
    return jnp.stack(flows, axis=-2)


def pack_slots(values, labels, targets, peer_count, slot_cap):
    entries = targets.shape[0]
    position = jnp.arange(entries, dtype=jnp.int32)
    earlier = (targets[:, None] == targets[None, :]) & (position[None, :] < position[:, None])
    ranking = jnp.sum(earlier.astype(jnp.int32), axis=1)
    target_slot = targets * slot_cap + ranking
    buffer = (
        jnp.zeros((peer_count * slot_cap, values.shape[1]), values.dtype)
        .at[target_slot]
        .set(values)
    )
    slot_labels = jnp.zeros((peer_count * slot_cap,), jnp.int32).at[target_slot].set(labels)
    return (buffer, slot_labels)


def gather_lateral(runoff, tile_dest, tile_block, blocks, shards):
    tile_count, width = runoff.shape
    tile_cap = max(2, 2 * tile_count // shards)
    grid = ("basin", "band")
    if tile_cap >= blocks:
        block_ids = tile_dest * blocks + tile_block
        pick = (
            block_ids[None, :] == jnp.arange(shards * blocks, dtype=jnp.int32)[:, None]
        ).astype(jnp.float32)
        dense = jnp.dot(pick, runoff, precision=lax.Precision.HIGHEST)
        arrived = lax.all_to_all(
            dense.reshape(shards, blocks, width), grid, split_axis=0, concat_axis=0, tiled=True
        )
        return jnp.sum(arrived, axis=0)
    buffer, slot_labels = pack_slots(runoff, tile_block, tile_dest, shards, tile_cap)
    arrived = lax.all_to_all(
        buffer.reshape(shards, tile_cap, width), grid, split_axis=0, concat_axis=0, tiled=True
    )
    arrived_ids = lax.all_to_all(
        slot_labels.reshape(shards, tile_cap), grid, split_axis=0, concat_axis=0, tiled=True
    )
    block_pick = (
        arrived_ids.reshape(-1)[:, None] == jnp.arange(blocks, dtype=jnp.int32)[None, :]
    ).astype(jnp.float32)
    return jnp.einsum(
        "sk,sx->kx", block_pick, arrived.reshape(-1, width), precision=lax.Precision.HIGHEST
    )


def local(
    precip,
    soil_water,
    capacity,
    evap_rate,
    tile_dest,
    tile_block,
    trib_op,
    trib_keep,
    trib_prev,
    trib_river,
    trib_reach,
    main_op,
    main_keep,
    main_prev,
    head_inflow,
):
    tile_count = precip.shape[0]
    sub_steps = precip.shape[1]
    reaches = precip.shape[2]
    blocks = trib_op.shape[0]
    chains = lax.axis_size("basin")
    rivers = lax.axis_size("band")
    shards = chains * rivers
    grid = ("basin", "band")
    operator = main_op[0, 0]
    keep_main = main_keep[0, 0]
    prev_main = main_prev[0, 0]

    runoff, water = land_update(precip, soil_water, capacity, evap_rate)
    lateral = gather_lateral(
        runoff.reshape(tile_count, sub_steps * reaches), tile_dest, tile_block, blocks, shards
    )
    trib_mixed = jnp.einsum(
        "brc,btc->btr",
        trib_op,
        lateral.reshape(blocks, sub_steps, reaches),
        precision=lax.Precision.HIGHEST,
    )
    trib_flows = route_series(trib_mixed, trib_keep, trib_prev)
    outlet = trib_flows[:, :, reaches - 1]

    payload = jnp.concatenate(
        [
            outlet.reshape(-1),
            trib_river.astype(jnp.float32),
            trib_reach.astype(jnp.float32),
            operator[reaches - 1],
            keep_main[reaches - 1 :],
            prev_main[reaches - 1 :],
        ]
    )
    width = payload.shape[0]
    padded = -(-width // 128) * 128
    payload = jnp.pad(payload, (0, padded - width))
    every = lax.all_to_all(
        jnp.broadcast_to(payload[None], (shards, padded)), grid, split_axis=0, concat_axis=0, tiled=True
    )

    mine = lax.axis_index("band")
    me = lax.axis_index("basin")
    at = 0
    outlets = every[:, at : at + blocks * sub_steps].reshape(chains, rivers * blocks, sub_steps)
    at += blocks * sub_steps
    river_of = every[:, at : at + blocks].reshape(chains, rivers * blocks)
    at += blocks
    reach_of = every[:, at : at + blocks].reshape(chains, rivers * blocks)
    at += blocks
    exit_rows = lax.dynamic_index_in_dim(
        every[:, at : at + reaches].reshape(chains, rivers, reaches), mine, axis=1, keepdims=False
    )
    at += reaches
    keeps = lax.dynamic_index_in_dim(
        every[:, at].reshape(chains, rivers), mine, axis=1, keepdims=False
    )
    starts = lax.dynamic_index_in_dim(
        every[:, at + 1].reshape(chains, rivers), mine, axis=1, keepdims=False
    )

    joins = (river_of == mine.astype(jnp.float32))[:, :, None] & (
        reach_of[:, :, None] == jnp.arange(reaches, dtype=jnp.float32)[None, None, :]
    )
    weight = joins.astype(jnp.float32)
    branch_all = jnp.sum(weight[:, :, None, :] * outlets[:, :, :, None], axis=1)
    branch_exit = jnp.sum(branch_all * exit_rows[:, None, :], axis=2)

    flow = starts
    free_exit = []
    for sub_step in range(sub_steps):
        flow = keeps * flow + (1.0 - keeps) * branch_exit[:, sub_step]
        free_exit.append(flow)
    free_exit = jnp.stack(free_exit, axis=1)
    lag = jnp.arange(sub_steps)[:, None] - jnp.arange(sub_steps)[None, :]
    lag_f = jnp.maximum(lag, 0).astype(jnp.float32)
    response = jnp.where(
        lag[None] >= 0,
        (exit_rows[:, 0] * (1.0 - keeps))[:, None, None] * keeps[:, None, None] ** lag_f[None],
        0.0,
    )

    def advance(section, entry):
        moved = jnp.sum(response[section] * entry[None, :], axis=1) + free_exit[section]
        return jnp.where(section < me, moved, entry)

    entry = lax.fori_loop(0, chains, advance, head_inflow[0], unroll=chains <= 16)

    branch_in = lax.dynamic_index_in_dim(branch_all, me, axis=0, keepdims=False)
    first_reach = (jnp.arange(reaches) == 0).astype(jnp.float32)
    fed = branch_in + entry[:, None] * first_reach[None, :]
    main_mixed = jnp.einsum("rc,tc->tr", operator, fed, precision=lax.Precision.HIGHEST)
    main_flows = route_series(main_mixed, keep_main, prev_main)
    return (water, trib_flows[:, sub_steps - 1], main_flows[None, None])


def solution(mesh):
    return jax.shard_map(
        local,
        mesh=mesh,
        in_specs=(
            P(("basin", "band"), None, None),
            P(("basin", "band"), None),
            P(("basin", "band"), None),
            P(("basin", "band"), None),
            P(("basin", "band")),
            P(("basin", "band")),
            P(("basin", "band"), None, None),
            P(("basin", "band"), None),
            P(("basin", "band"), None),
            P(("basin", "band")),
            P(("basin", "band")),
            P("band", "basin", None, None),
            P("band", "basin", None),
            P("band", "basin", None),
            P("band", None),
        ),
        out_specs=(
            P(("basin", "band"), None),
            P(("basin", "band"), None),
            P("band", "basin", None, None),
        ),
        check_vma=False,
    )
```

```python
import jax
import jax.numpy as jnp
from jax import lax
from jax.sharding import PartitionSpec as P


def land_update(precip, soil_water, capacity, evap_rate):
    water = soil_water
    runoff_steps = []
    for sub_step in range(precip.shape[1]):
        rain_now = precip[:, sub_step]
        runoff_now = rain_now * water / (water + capacity)
        water = (1.0 - evap_rate) * water + rain_now - runoff_now
        runoff_steps.append(runoff_now)
    return (jnp.stack(runoff_steps, axis=1), water)


def route_series(mixed, keep, previous):
    flow = previous
    flows = []
    for sub_step in range(mixed.shape[-2]):
        flow = keep * flow + (1.0 - keep) * mixed[..., sub_step, :]
        flows.append(flow)
    return jnp.stack(flows, axis=-2)


def pack_slots(values, labels, targets, peer_count, slot_cap):
    entries = targets.shape[0]
    position = jnp.arange(entries, dtype=jnp.int32)
    earlier = (targets[:, None] == targets[None, :]) & (position[None, :] < position[:, None])
    ranking = jnp.sum(earlier.astype(jnp.int32), axis=1)
    target_slot = targets * slot_cap + ranking
    buffer = (
        jnp.zeros((peer_count * slot_cap, values.shape[1]), values.dtype)
        .at[target_slot]
        .set(values)
    )
    slot_labels = jnp.zeros((peer_count * slot_cap,), jnp.int32).at[target_slot].set(labels)
    return (buffer, slot_labels)


def gather_lateral(runoff, tile_dest, tile_block, blocks, shards):
    tile_count, width = runoff.shape
    tile_cap = max(2, 2 * tile_count // shards)
    grid = ("basin", "band")
    if tile_cap >= blocks:
        block_ids = tile_dest * blocks + tile_block
        pick = (
            block_ids[None, :] == jnp.arange(shards * blocks, dtype=jnp.int32)[:, None]
        ).astype(jnp.float32)
        dense = jnp.dot(pick, runoff, precision=lax.Precision.HIGHEST)
        return lax.psum_scatter(dense, grid, scatter_dimension=0, tiled=True)
    buffer, slot_labels = pack_slots(runoff, tile_block, tile_dest, shards, tile_cap)
    arrived = lax.all_to_all(
        buffer.reshape(shards, tile_cap, width), grid, split_axis=0, concat_axis=0, tiled=True
    )
    arrived_ids = lax.all_to_all(
        slot_labels.reshape(shards, tile_cap), grid, split_axis=0, concat_axis=0, tiled=True
    )
    block_pick = (
        arrived_ids.reshape(-1)[:, None] == jnp.arange(blocks, dtype=jnp.int32)[None, :]
    ).astype(jnp.float32)
    return jnp.einsum(
        "sk,sx->kx", block_pick, arrived.reshape(-1, width), precision=lax.Precision.HIGHEST
    )


def local(
    precip,
    soil_water,
    capacity,
    evap_rate,
    tile_dest,
    tile_block,
    trib_op,
    trib_keep,
    trib_prev,
    trib_river,
    trib_reach,
    main_op,
    main_keep,
    main_prev,
    head_inflow,
):
    tile_count = precip.shape[0]
    sub_steps = precip.shape[1]
    reaches = precip.shape[2]
    blocks = trib_op.shape[0]
    chains = lax.axis_size("basin")
    rivers = lax.axis_size("band")
    shards = chains * rivers
    grid = ("basin", "band")
    operator = main_op[0, 0]
    keep_main = main_keep[0, 0]
    prev_main = main_prev[0, 0]

    runoff, water = land_update(precip, soil_water, capacity, evap_rate)
    lateral = gather_lateral(
        runoff.reshape(tile_count, sub_steps * reaches), tile_dest, tile_block, blocks, shards
    )
    trib_mixed = jnp.einsum(
        "brc,btc->btr",
        trib_op,
        lateral.reshape(blocks, sub_steps, reaches),
        precision=lax.Precision.HIGHEST,
    )
    trib_flows = route_series(trib_mixed, trib_keep, trib_prev)
    outlet = trib_flows[:, :, reaches - 1]

    payload = jnp.concatenate(
        [
            outlet.reshape(-1),
            trib_river.astype(jnp.float32),
            trib_reach.astype(jnp.float32),
            operator[reaches - 1],
            keep_main[reaches - 1 :],
            prev_main[reaches - 1 :],
        ]
    )
    width = payload.shape[0]
    padded = -(-width // 128) * 128
    payload = jnp.pad(payload, (0, padded - width))
    every = lax.all_to_all(
        jnp.broadcast_to(payload[None], (shards, padded)), grid, split_axis=0, concat_axis=0, tiled=True
    )

    mine = lax.axis_index("band")
    me = lax.axis_index("basin")
    at = 0
    outlets = every[:, at : at + blocks * sub_steps].reshape(chains, rivers * blocks, sub_steps)
    at += blocks * sub_steps
    river_of = every[:, at : at + blocks].reshape(chains, rivers * blocks)
    at += blocks
    reach_of = every[:, at : at + blocks].reshape(chains, rivers * blocks)
    at += blocks
    exit_rows = lax.dynamic_index_in_dim(
        every[:, at : at + reaches].reshape(chains, rivers, reaches), mine, axis=1, keepdims=False
    )
    at += reaches
    keeps = lax.dynamic_index_in_dim(
        every[:, at].reshape(chains, rivers), mine, axis=1, keepdims=False
    )
    starts = lax.dynamic_index_in_dim(
        every[:, at + 1].reshape(chains, rivers), mine, axis=1, keepdims=False
    )

    joins = (river_of == mine.astype(jnp.float32))[:, :, None] & (
        reach_of[:, :, None] == jnp.arange(reaches, dtype=jnp.float32)[None, None, :]
    )
    weight = joins.astype(jnp.float32)
    branch_all = jnp.sum(weight[:, :, None, :] * outlets[:, :, :, None], axis=1)
    branch_exit = jnp.sum(branch_all * exit_rows[:, None, :], axis=2)

    flow = starts
    free_exit = []
    for sub_step in range(sub_steps):
        flow = keeps * flow + (1.0 - keeps) * branch_exit[:, sub_step]
        free_exit.append(flow)
    free_exit = jnp.stack(free_exit, axis=1)
    lag = jnp.arange(sub_steps)[:, None] - jnp.arange(sub_steps)[None, :]
    lag_f = jnp.maximum(lag, 0).astype(jnp.float32)
    response = jnp.where(
        lag[None] >= 0,
        (exit_rows[:, 0] * (1.0 - keeps))[:, None, None] * keeps[:, None, None] ** lag_f[None],
        0.0,
    )

    def advance(section, entry):
        moved = jnp.sum(response[section] * entry[None, :], axis=1) + free_exit[section]
        return jnp.where(section < me, moved, entry)

    entry = lax.fori_loop(0, chains, advance, head_inflow[0], unroll=chains <= 16)

    branch_in = lax.dynamic_index_in_dim(branch_all, me, axis=0, keepdims=False)
    first_reach = (jnp.arange(reaches) == 0).astype(jnp.float32)
    fed = branch_in + entry[:, None] * first_reach[None, :]
    main_mixed = jnp.einsum("rc,tc->tr", operator, fed, precision=lax.Precision.HIGHEST)
    main_flows = route_series(main_mixed, keep_main, prev_main)
    return (water, trib_flows[:, sub_steps - 1], main_flows[None, None])


def solution(mesh):
    return jax.shard_map(
        local,
        mesh=mesh,
        in_specs=(
            P(("basin", "band"), None, None),
            P(("basin", "band"), None),
            P(("basin", "band"), None),
            P(("basin", "band"), None),
            P(("basin", "band")),
            P(("basin", "band")),
            P(("basin", "band"), None, None),
            P(("basin", "band"), None),
            P(("basin", "band"), None),
            P(("basin", "band")),
            P(("basin", "band")),
            P("band", "basin", None, None),
            P("band", "basin", None),
            P("band", "basin", None),
            P("band", None),
        ),
        out_specs=(
            P(("basin", "band"), None),
            P(("basin", "band"), None),
            P("band", "basin", None, None),
        ),
        check_vma=False,
    )
```

```python
import jax
import jax.numpy as jnp
from jax import lax
from jax.sharding import PartitionSpec as P


def land_update(precip, soil_water, capacity, evap_rate):
    water = soil_water
    runoff_steps = []
    for sub_step in range(precip.shape[1]):
        rain_now = precip[:, sub_step]
        runoff_now = rain_now * water / (water + capacity)
        water = (1.0 - evap_rate) * water + rain_now - runoff_now
        runoff_steps.append(runoff_now)
    return (jnp.stack(runoff_steps, axis=1), water)


def route_series(mixed, keep, previous):
    flow = previous
    flows = []
    for sub_step in range(mixed.shape[-2]):
        flow = keep * flow + (1.0 - keep) * mixed[..., sub_step, :]
        flows.append(flow)
    return jnp.stack(flows, axis=-2)


def pack_slots(values, labels, targets, peer_count, slot_cap):
    entries = targets.shape[0]
    position = jnp.arange(entries, dtype=jnp.int32)
    earlier = (targets[:, None] == targets[None, :]) & (position[None, :] < position[:, None])
    ranking = jnp.sum(earlier.astype(jnp.int32), axis=1)
    target_slot = targets * slot_cap + ranking
    buffer = (
        jnp.zeros((peer_count * slot_cap, values.shape[1]), values.dtype)
        .at[target_slot]
        .set(values)
    )
    slot_labels = jnp.zeros((peer_count * slot_cap,), jnp.int32).at[target_slot].set(labels)
    return (buffer, slot_labels)


def gather_lateral(runoff, tile_dest, tile_block, blocks, shards):
    tile_count, width = runoff.shape
    tile_cap = max(2, 2 * tile_count // shards)
    grid = ("basin", "band")
    if tile_cap >= blocks:
        block_ids = tile_dest * blocks + tile_block
        pick = (
            block_ids[None, :] == jnp.arange(shards * blocks, dtype=jnp.int32)[:, None]
        ).astype(jnp.float32)
        dense = jnp.dot(pick, runoff, precision=lax.Precision.HIGHEST)
        chains = lax.axis_size("basin")
        rivers = shards // chains
        across = lax.all_to_all(
            dense.reshape(chains, rivers, blocks, width), "band", split_axis=1, concat_axis=1, tiled=True
        )
        arrived = lax.all_to_all(
            jnp.sum(across, axis=1), "basin", split_axis=0, concat_axis=0, tiled=True
        )
        return jnp.sum(arrived, axis=0)
    buffer, slot_labels = pack_slots(runoff, tile_block, tile_dest, shards, tile_cap)
    arrived = lax.all_to_all(
        buffer.reshape(shards, tile_cap, width), grid, split_axis=0, concat_axis=0, tiled=True
    )
    arrived_ids = lax.all_to_all(
        slot_labels.reshape(shards, tile_cap), grid, split_axis=0, concat_axis=0, tiled=True
    )
    block_pick = (
        arrived_ids.reshape(-1)[:, None] == jnp.arange(blocks, dtype=jnp.int32)[None, :]
    ).astype(jnp.float32)
    return jnp.einsum(
        "sk,sx->kx", block_pick, arrived.reshape(-1, width), precision=lax.Precision.HIGHEST
    )


def local(
    precip,
    soil_water,
    capacity,
    evap_rate,
    tile_dest,
    tile_block,
    trib_op,
    trib_keep,
    trib_prev,
    trib_river,
    trib_reach,
    main_op,
    main_keep,
    main_prev,
    head_inflow,
):
    tile_count = precip.shape[0]
    sub_steps = precip.shape[1]
    reaches = precip.shape[2]
    blocks = trib_op.shape[0]
    chains = lax.axis_size("basin")
    rivers = lax.axis_size("band")
    shards = chains * rivers
    grid = ("basin", "band")
    operator = main_op[0, 0]
    keep_main = main_keep[0, 0]
    prev_main = main_prev[0, 0]

    runoff, water = land_update(precip, soil_water, capacity, evap_rate)
    lateral = gather_lateral(
        runoff.reshape(tile_count, sub_steps * reaches), tile_dest, tile_block, blocks, shards
    )
    trib_mixed = jnp.einsum(
        "brc,btc->btr",
        trib_op,
        lateral.reshape(blocks, sub_steps, reaches),
        precision=lax.Precision.HIGHEST,
    )
    trib_flows = route_series(trib_mixed, trib_keep, trib_prev)
    outlet = trib_flows[:, :, reaches - 1]

    payload = jnp.concatenate(
        [
            outlet.reshape(-1),
            trib_river.astype(jnp.float32),
            trib_reach.astype(jnp.float32),
            operator[reaches - 1],
            keep_main[reaches - 1 :],
            prev_main[reaches - 1 :],
        ]
    )
    width = payload.shape[0]
    padded = -(-width // 128) * 128
    payload = jnp.pad(payload, (0, padded - width))
    every = lax.all_to_all(
        jnp.broadcast_to(payload[None], (shards, padded)), grid, split_axis=0, concat_axis=0, tiled=True
    )

    mine = lax.axis_index("band")
    me = lax.axis_index("basin")
    at = 0
    outlets = every[:, at : at + blocks * sub_steps].reshape(chains, rivers * blocks, sub_steps)
    at += blocks * sub_steps
    river_of = every[:, at : at + blocks].reshape(chains, rivers * blocks)
    at += blocks
    reach_of = every[:, at : at + blocks].reshape(chains, rivers * blocks)
    at += blocks
    exit_rows = lax.dynamic_index_in_dim(
        every[:, at : at + reaches].reshape(chains, rivers, reaches), mine, axis=1, keepdims=False
    )
    at += reaches
    keeps = lax.dynamic_index_in_dim(
        every[:, at].reshape(chains, rivers), mine, axis=1, keepdims=False
    )
    starts = lax.dynamic_index_in_dim(
        every[:, at + 1].reshape(chains, rivers), mine, axis=1, keepdims=False
    )

    joins = (river_of == mine.astype(jnp.float32))[:, :, None] & (
        reach_of[:, :, None] == jnp.arange(reaches, dtype=jnp.float32)[None, None, :]
    )
    weight = joins.astype(jnp.float32)
    branch_all = jnp.sum(weight[:, :, None, :] * outlets[:, :, :, None], axis=1)
    branch_exit = jnp.sum(branch_all * exit_rows[:, None, :], axis=2)

    flow = starts
    free_exit = []
    for sub_step in range(sub_steps):
        flow = keeps * flow + (1.0 - keeps) * branch_exit[:, sub_step]
        free_exit.append(flow)
    free_exit = jnp.stack(free_exit, axis=1)
    lag = jnp.arange(sub_steps)[:, None] - jnp.arange(sub_steps)[None, :]
    lag_f = jnp.maximum(lag, 0).astype(jnp.float32)
    response = jnp.where(
        lag[None] >= 0,
        (exit_rows[:, 0] * (1.0 - keeps))[:, None, None] * keeps[:, None, None] ** lag_f[None],
        0.0,
    )

    def advance(section, entry):
        moved = jnp.sum(response[section] * entry[None, :], axis=1) + free_exit[section]
        return jnp.where(section < me, moved, entry)

    entry = lax.fori_loop(0, chains, advance, head_inflow[0], unroll=chains <= 16)

    branch_in = lax.dynamic_index_in_dim(branch_all, me, axis=0, keepdims=False)
    first_reach = (jnp.arange(reaches) == 0).astype(jnp.float32)
    fed = branch_in + entry[:, None] * first_reach[None, :]
    main_mixed = jnp.einsum("rc,tc->tr", operator, fed, precision=lax.Precision.HIGHEST)
    main_flows = route_series(main_mixed, keep_main, prev_main)
    return (water, trib_flows[:, sub_steps - 1], main_flows[None, None])


def solution(mesh):
    return jax.shard_map(
        local,
        mesh=mesh,
        in_specs=(
            P(("basin", "band"), None, None),
            P(("basin", "band"), None),
            P(("basin", "band"), None),
            P(("basin", "band"), None),
            P(("basin", "band")),
            P(("basin", "band")),
            P(("basin", "band"), None, None),
            P(("basin", "band"), None),
            P(("basin", "band"), None),
            P(("basin", "band")),
            P(("basin", "band")),
            P("band", "basin", None, None),
            P("band", "basin", None),
            P("band", "basin", None),
            P("band", None),
        ),
        out_specs=(
            P(("basin", "band"), None),
            P(("basin", "band"), None),
            P("band", "basin", None, None),
        ),
        check_vma=False,
    )
```

```python
import jax
import jax.numpy as jnp
from jax import lax
from jax.sharding import PartitionSpec as P


def land_update(precip, soil_water, capacity, evap_rate):
    water = soil_water
    runoff_steps = []
    for sub_step in range(precip.shape[1]):
        rain_now = precip[:, sub_step]
        runoff_now = rain_now * water / (water + capacity)
        water = (1.0 - evap_rate) * water + rain_now - runoff_now
        runoff_steps.append(runoff_now)
    return (jnp.stack(runoff_steps, axis=1), water)


def route_series(mixed, keep, previous):
    flow = previous
    flows = []
    for sub_step in range(mixed.shape[-2]):
        flow = keep * flow + (1.0 - keep) * mixed[..., sub_step, :]
        flows.append(flow)
    return jnp.stack(flows, axis=-2)


def pack_slots(values, labels, targets, peer_count, slot_cap):
    entries = targets.shape[0]
    position = jnp.arange(entries, dtype=jnp.int32)
    earlier = (targets[:, None] == targets[None, :]) & (position[None, :] < position[:, None])
    ranking = jnp.sum(earlier.astype(jnp.int32), axis=1)
    target_slot = targets * slot_cap + ranking
    buffer = (
        jnp.zeros((peer_count * slot_cap, values.shape[1]), values.dtype)
        .at[target_slot]
        .set(values)
    )
    slot_labels = jnp.zeros((peer_count * slot_cap,), jnp.int32).at[target_slot].set(labels)
    return (buffer, slot_labels)


def gather_lateral(runoff, tile_dest, tile_block, blocks, shards):
    tile_count, width = runoff.shape
    tile_cap = max(2, 2 * tile_count // shards)
    grid = ("basin", "band")
    if tile_cap >= blocks:
        block_ids = tile_dest * blocks + tile_block
        pick = (
            block_ids[None, :] == jnp.arange(shards * blocks, dtype=jnp.int32)[:, None]
        ).astype(jnp.float32)
        dense = jnp.dot(pick, runoff, precision=lax.Precision.HIGHEST)
        arrived = lax.all_to_all(
            dense.reshape(shards, blocks, width), grid, split_axis=0, concat_axis=0, tiled=True
        )
        return jnp.sum(arrived, axis=0)
    buffer, slot_labels = pack_slots(runoff, tile_block, tile_dest, shards, tile_cap)
    arrived = lax.all_to_all(
        buffer.reshape(shards, tile_cap, width), grid, split_axis=0, concat_axis=0, tiled=True
    )
    arrived_ids = lax.all_to_all(
        slot_labels.reshape(shards, tile_cap), grid, split_axis=0, concat_axis=0, tiled=True
    )
    block_pick = (
        arrived_ids.reshape(-1)[:, None] == jnp.arange(blocks, dtype=jnp.int32)[None, :]
    ).astype(jnp.float32)
    return jnp.einsum(
        "sk,sx->kx", block_pick, arrived.reshape(-1, width), precision=lax.Precision.HIGHEST
    )


def spread(value, shards):
    grid = ("basin", "band")
    copies = jnp.broadcast_to(value[None], (shards,) + value.shape)
    return lax.all_to_all(copies, grid, split_axis=0, concat_axis=0, tiled=True)


def local_two_rounds(
    precip,
    soil_water,
    capacity,
    evap_rate,
    tile_dest,
    tile_block,
    trib_op,
    trib_keep,
    trib_prev,
    trib_river,
    trib_reach,
    main_op,
    main_keep,
    main_prev,
    head_inflow,
):
    tile_count = precip.shape[0]
    sub_steps = precip.shape[1]
    reaches = precip.shape[2]
    blocks = trib_op.shape[0]
    chains = lax.axis_size("basin")
    rivers = lax.axis_size("band")
    shards = chains * rivers
    grid = ("basin", "band")
    operator = main_op[0, 0]
    keep_main = main_keep[0, 0]
    prev_main = main_prev[0, 0]

    runoff, water = land_update(precip, soil_water, capacity, evap_rate)
    lateral = gather_lateral(
        runoff.reshape(tile_count, sub_steps * reaches), tile_dest, tile_block, blocks, shards
    )
    trib_mixed = jnp.einsum(
        "brc,btc->btr",
        trib_op,
        lateral.reshape(blocks, sub_steps, reaches),
        precision=lax.Precision.HIGHEST,
    )
    trib_flows = route_series(trib_mixed, trib_keep, trib_prev)
    outlet = trib_flows[:, :, reaches - 1]

    payload = jnp.concatenate(
        [
            outlet.reshape(-1),
            trib_river.astype(jnp.float32),
            trib_reach.astype(jnp.float32),
            operator[reaches - 1],
            keep_main[reaches - 1 :],
            prev_main[reaches - 1 :],
        ]
    )
    width = payload.shape[0]
    padded = -(-width // 128) * 128
    payload = jnp.pad(payload, (0, padded - width))
    every = lax.all_to_all(
        jnp.broadcast_to(payload[None], (shards, padded)), grid, split_axis=0, concat_axis=0, tiled=True
    )

    mine = lax.axis_index("band")
    me = lax.axis_index("basin")
    at = 0
    outlets = every[:, at : at + blocks * sub_steps].reshape(chains, rivers * blocks, sub_steps)
    at += blocks * sub_steps
    river_of = every[:, at : at + blocks].reshape(chains, rivers * blocks)
    at += blocks
    reach_of = every[:, at : at + blocks].reshape(chains, rivers * blocks)
    at += blocks
    exit_rows = lax.dynamic_index_in_dim(
        every[:, at : at + reaches].reshape(chains, rivers, reaches), mine, axis=1, keepdims=False
    )
    at += reaches
    keeps = lax.dynamic_index_in_dim(
        every[:, at].reshape(chains, rivers), mine, axis=1, keepdims=False
    )
    starts = lax.dynamic_index_in_dim(
        every[:, at + 1].reshape(chains, rivers), mine, axis=1, keepdims=False
    )

    joins = (river_of == mine.astype(jnp.float32))[:, :, None] & (
        reach_of[:, :, None] == jnp.arange(reaches, dtype=jnp.float32)[None, None, :]
    )
    weight = joins.astype(jnp.float32)
    branch_all = jnp.sum(weight[:, :, None, :] * outlets[:, :, :, None], axis=1)
    branch_exit = jnp.sum(branch_all * exit_rows[:, None, :], axis=2)

    flow = starts
    free_exit = []
    for sub_step in range(sub_steps):
        flow = keeps * flow + (1.0 - keeps) * branch_exit[:, sub_step]
        free_exit.append(flow)
    free_exit = jnp.stack(free_exit, axis=1)
    lag = jnp.arange(sub_steps)[:, None] - jnp.arange(sub_steps)[None, :]
    lag_f = jnp.maximum(lag, 0).astype(jnp.float32)
    response = jnp.where(
        lag[None] >= 0,
        (exit_rows[:, 0] * (1.0 - keeps))[:, None, None] * keeps[:, None, None] ** lag_f[None],
        0.0,
    )

    def advance(section, entry):
        moved = jnp.sum(response[section] * entry[None, :], axis=1) + free_exit[section]
        return jnp.where(section < me, moved, entry)

    entry = lax.fori_loop(0, chains, advance, head_inflow[0], unroll=chains <= 16)

    branch_in = lax.dynamic_index_in_dim(branch_all, me, axis=0, keepdims=False)
    first_reach = (jnp.arange(reaches) == 0).astype(jnp.float32)
    fed = branch_in + entry[:, None] * first_reach[None, :]
    main_mixed = jnp.einsum("rc,tc->tr", operator, fed, precision=lax.Precision.HIGHEST)
    main_flows = route_series(main_mixed, keep_main, prev_main)
    return (water, trib_flows[:, sub_steps - 1], main_flows[None, None])


def local_one_round(
    precip,
    soil_water,
    capacity,
    evap_rate,
    tile_dest,
    tile_block,
    trib_op,
    trib_keep,
    trib_prev,
    trib_river,
    trib_reach,
    main_op,
    main_keep,
    main_prev,
    head_inflow,
):
    tile_count = precip.shape[0]
    sub_steps = precip.shape[1]
    reaches = precip.shape[2]
    blocks = trib_op.shape[0]
    chains = lax.axis_size("basin")
    rivers = lax.axis_size("band")
    shards = chains * rivers
    grid = ("basin", "band")
    width = sub_steps * reaches
    operator = main_op[0, 0]
    keep_main = main_keep[0, 0]
    prev_main = main_prev[0, 0]
    last = reaches - 1

    facts = jnp.concatenate(
        [
            trib_keep[:, last],
            trib_prev[:, last],
            trib_river.astype(jnp.float32),
            trib_reach.astype(jnp.float32),
            keep_main[last:],
            prev_main[last:],
        ]
    )
    facts = jnp.pad(facts, (0, reaches - facts.shape[0]))
    static = jnp.concatenate([trib_op[:, last], facts[None], operator[last:]], axis=0)
    everyone = spread(static, shards)

    runoff, water = land_update(precip, soil_water, capacity, evap_rate)
    runoff = runoff.reshape(tile_count, width)
    block_ids = tile_dest * blocks + tile_block
    pick = (
        block_ids[None, :] == jnp.arange(shards * blocks, dtype=jnp.int32)[:, None]
    ).astype(jnp.float32)
    dense = jnp.dot(pick, runoff, precision=lax.Precision.HIGHEST)
    exit_rows_all = everyone[:, :blocks].reshape(shards * blocks, reaches)
    partial_exit = jnp.sum(
        dense.reshape(shards * blocks, sub_steps, reaches) * exit_rows_all[:, None, :], axis=2
    )
    extra = -(-(shards * blocks * sub_steps) // width)
    tail_rows = jnp.pad(partial_exit.reshape(-1), (0, extra * width - shards * blocks * sub_steps))
    send = jnp.concatenate(
        [
            dense.reshape(shards, blocks, width),
            jnp.broadcast_to(tail_rows.reshape(1, extra, width), (shards, extra, width)),
        ],
        axis=1,
    )
    arrived = jnp.sum(
        lax.all_to_all(send, grid, split_axis=0, concat_axis=0, tiled=True), axis=0
    )
    lateral = arrived[:blocks]
    exit_mix = arrived[blocks:].reshape(-1)[: shards * blocks * sub_steps].reshape(
        shards * blocks, sub_steps
    )

    trib_mixed = jnp.einsum(
        "brc,btc->btr",
        trib_op,
        lateral.reshape(blocks, sub_steps, reaches),
        precision=lax.Precision.HIGHEST,
    )
    trib_flows = route_series(trib_mixed, trib_keep, trib_prev)

    facts_all = everyone[:, blocks]
    at = 0
    keep_of = facts_all[:, at : at + blocks].reshape(-1)
    at += blocks
    prev_of = facts_all[:, at : at + blocks].reshape(-1)
    at += blocks
    river_of = facts_all[:, at : at + blocks].reshape(chains, rivers * blocks)
    at += blocks
    reach_of = facts_all[:, at : at + blocks].reshape(chains, rivers * blocks)
    at += blocks
    mine = lax.axis_index("band")
    me = lax.axis_index("basin")
    keeps = lax.dynamic_index_in_dim(
        facts_all[:, at].reshape(chains, rivers), mine, axis=1, keepdims=False
    )
    starts = lax.dynamic_index_in_dim(
        facts_all[:, at + 1].reshape(chains, rivers), mine, axis=1, keepdims=False
    )
    exit_rows = lax.dynamic_index_in_dim(
        everyone[:, blocks + 1].reshape(chains, rivers, reaches), mine, axis=1, keepdims=False
    )

    flow = prev_of
    outlet_steps = []
    for sub_step in range(sub_steps):
        flow = keep_of * flow + (1.0 - keep_of) * exit_mix[:, sub_step]
        outlet_steps.append(flow)
    outlets = jnp.stack(outlet_steps, axis=1).reshape(chains, rivers * blocks, sub_steps)

    joins = (river_of == mine.astype(jnp.float32))[:, :, None] & (
        reach_of[:, :, None] == jnp.arange(reaches, dtype=jnp.float32)[None, None, :]
    )
    weight = joins.astype(jnp.float32)
    branch_all = jnp.sum(weight[:, :, None, :] * outlets[:, :, :, None], axis=1)
    branch_exit = jnp.sum(branch_all * exit_rows[:, None, :], axis=2)

    flow = starts
    free_exit = []
    for sub_step in range(sub_steps):
        flow = keeps * flow + (1.0 - keeps) * branch_exit[:, sub_step]
        free_exit.append(flow)
    free_exit = jnp.stack(free_exit, axis=1)
    lag = jnp.arange(sub_steps)[:, None] - jnp.arange(sub_steps)[None, :]
    lag_f = jnp.maximum(lag, 0).astype(jnp.float32)
    response = jnp.where(
        lag[None] >= 0,
        (exit_rows[:, 0] * (1.0 - keeps))[:, None, None] * keeps[:, None, None] ** lag_f[None],
        0.0,
    )

    def advance(section, entry):
        moved = jnp.sum(response[section] * entry[None, :], axis=1) + free_exit[section]
        return jnp.where(section < me, moved, entry)

    entry = lax.fori_loop(0, chains, advance, head_inflow[0], unroll=chains <= 16)

    branch_in = lax.dynamic_index_in_dim(branch_all, me, axis=0, keepdims=False)
    first_reach = (jnp.arange(reaches) == 0).astype(jnp.float32)
    fed = branch_in + entry[:, None] * first_reach[None, :]
    main_mixed = jnp.einsum("rc,tc->tr", operator, fed, precision=lax.Precision.HIGHEST)
    main_flows = route_series(main_mixed, keep_main, prev_main)
    return (water, trib_flows[:, sub_steps - 1], main_flows[None, None])


def local(*args):
    precip, trib_op = args[0], args[6]
    tile_count, reaches = precip.shape[0], precip.shape[2]
    blocks = trib_op.shape[0]
    shards = lax.axis_size("basin") * lax.axis_size("band")
    if max(2, 2 * tile_count // shards) >= blocks and 4 * blocks + 2 <= reaches:
        return local_one_round(*args)
    return local_two_rounds(*args)


def solution(mesh):
    return jax.shard_map(
        local,
        mesh=mesh,
        in_specs=(
            P(("basin", "band"), None, None),
            P(("basin", "band"), None),
            P(("basin", "band"), None),
            P(("basin", "band"), None),
            P(("basin", "band")),
            P(("basin", "band")),
            P(("basin", "band"), None, None),
            P(("basin", "band"), None),
            P(("basin", "band"), None),
            P(("basin", "band")),
            P(("basin", "band")),
            P("band", "basin", None, None),
            P("band", "basin", None),
            P("band", "basin", None),
            P("band", None),
        ),
        out_specs=(
            P(("basin", "band"), None),
            P(("basin", "band"), None),
            P("band", "basin", None, None),
        ),
        check_vma=False,
    )
```

```python
import jax
import jax.numpy as jnp
from jax import lax
from jax.sharding import PartitionSpec as P


def land_update(precip, soil_water, capacity, evap_rate):
    water = soil_water
    runoff_steps = []
    for sub_step in range(precip.shape[1]):
        rain_now = precip[:, sub_step]
        runoff_now = rain_now * water / (water + capacity)
        water = (1.0 - evap_rate) * water + rain_now - runoff_now
        runoff_steps.append(runoff_now)
    return (jnp.stack(runoff_steps, axis=1), water)


def route_series(mixed, keep, previous):
    flow = previous
    flows = []
    for sub_step in range(mixed.shape[-2]):
        flow = keep * flow + (1.0 - keep) * mixed[..., sub_step, :]
        flows.append(flow)
    return jnp.stack(flows, axis=-2)


def pack_slots(values, labels, targets, peer_count, slot_cap):
    entries = targets.shape[0]
    position = jnp.arange(entries, dtype=jnp.int32)
    earlier = (targets[:, None] == targets[None, :]) & (position[None, :] < position[:, None])
    ranking = jnp.sum(earlier.astype(jnp.int32), axis=1)
    target_slot = targets * slot_cap + ranking
    buffer = (
        jnp.zeros((peer_count * slot_cap, values.shape[1]), values.dtype)
        .at[target_slot]
        .set(values)
    )
    slot_labels = jnp.zeros((peer_count * slot_cap,), jnp.int32).at[target_slot].set(labels)
    return (buffer, slot_labels)


def gather_lateral(runoff, tile_dest, tile_block, blocks, shards):
    tile_count, width = runoff.shape
    tile_cap = max(2, 2 * tile_count // shards)
    grid = ("basin", "band")
    if tile_cap >= blocks:
        block_ids = tile_dest * blocks + tile_block
        pick = (
            block_ids[None, :] == jnp.arange(shards * blocks, dtype=jnp.int32)[:, None]
        ).astype(jnp.float32)
        dense = jnp.dot(pick, runoff, precision=lax.Precision.HIGHEST)
        if not PAIRED or blocks % 2:
            arrived = lax.all_to_all(
                dense.reshape(shards, blocks, width), grid, split_axis=0, concat_axis=0, tiled=True
            )
            return jnp.sum(arrived, axis=0)
        return pair_exchange(dense, blocks, shards)
    buffer, slot_labels = pack_slots(runoff, tile_block, tile_dest, shards, tile_cap)
    arrived = lax.all_to_all(
        buffer.reshape(shards, tile_cap, width), grid, split_axis=0, concat_axis=0, tiled=True
    )
    arrived_ids = lax.all_to_all(
        slot_labels.reshape(shards, tile_cap), grid, split_axis=0, concat_axis=0, tiled=True
    )
    block_pick = (
        arrived_ids.reshape(-1)[:, None] == jnp.arange(blocks, dtype=jnp.int32)[None, :]
    ).astype(jnp.float32)
    return jnp.einsum(
        "sk,sx->kx", block_pick, arrived.reshape(-1, width), precision=lax.Precision.HIGHEST
    )


def pair_exchange(dense, blocks, shards):
    chains = lax.axis_size("basin")
    rivers = lax.axis_size("band")
    width = dense.shape[1]
    half = blocks // 2
    swap = [(m ^ 1, m) for m in range(rivers)]
    core = lax.axis_index("band") % 2
    parts = dense.reshape(chains, rivers // 2, 2, blocks, width)
    keep_side = lax.dynamic_index_in_dim(parts, core, axis=2, keepdims=False)
    give_side = lax.dynamic_index_in_dim(parts, 1 - core, axis=2, keepdims=False)
    chip_sum = keep_side + lax.ppermute(give_side, "band", swap)
    side = (jnp.arange(2) == core)[None, None, :, None, None]
    send = jnp.where(side, chip_sum[:, :, None, :half], chip_sum[:, :, None, half:])
    arrived = lax.all_to_all(
        send.reshape(shards, half, width), ("basin", "band"), split_axis=0, concat_axis=0, tiled=True
    ).reshape(chains, rivers // 2, 2, half, width)
    same = jnp.sum(jnp.where(side, arrived, 0.0), axis=(0, 1, 2))
    other = jnp.sum(jnp.where(side, 0.0, arrived), axis=(0, 1, 2))
    return jnp.concatenate([same, lax.ppermute(other, "band", swap)], axis=0)


def local(
    precip,
    soil_water,
    capacity,
    evap_rate,
    tile_dest,
    tile_block,
    trib_op,
    trib_keep,
    trib_prev,
    trib_river,
    trib_reach,
    main_op,
    main_keep,
    main_prev,
    head_inflow,
):
    tile_count = precip.shape[0]
    sub_steps = precip.shape[1]
    reaches = precip.shape[2]
    blocks = trib_op.shape[0]
    chains = lax.axis_size("basin")
    rivers = lax.axis_size("band")
    shards = chains * rivers
    grid = ("basin", "band")
    operator = main_op[0, 0]
    keep_main = main_keep[0, 0]
    prev_main = main_prev[0, 0]

    runoff, water = land_update(precip, soil_water, capacity, evap_rate)
    lateral = gather_lateral(
        runoff.reshape(tile_count, sub_steps * reaches), tile_dest, tile_block, blocks, shards
    )
    trib_mixed = jnp.einsum(
        "brc,btc->btr",
        trib_op,
        lateral.reshape(blocks, sub_steps, reaches),
        precision=lax.Precision.HIGHEST,
    )
    trib_flows = route_series(trib_mixed, trib_keep, trib_prev)
    outlet = trib_flows[:, :, reaches - 1]

    payload = jnp.concatenate(
        [
            outlet.reshape(-1),
            trib_river.astype(jnp.float32),
            trib_reach.astype(jnp.float32),
            operator[reaches - 1],
            keep_main[reaches - 1 :],
            prev_main[reaches - 1 :],
        ]
    )
    width = payload.shape[0]
    padded = -(-width // 128) * 128
    payload = jnp.pad(payload, (0, padded - width))
    every = lax.all_to_all(
        jnp.broadcast_to(payload[None], (shards, padded)), grid, split_axis=0, concat_axis=0, tiled=True
    )

    mine = lax.axis_index("band")
    me = lax.axis_index("basin")
    at = 0
    outlets = every[:, at : at + blocks * sub_steps].reshape(chains, rivers * blocks, sub_steps)
    at += blocks * sub_steps
    river_of = every[:, at : at + blocks].reshape(chains, rivers * blocks)
    at += blocks
    reach_of = every[:, at : at + blocks].reshape(chains, rivers * blocks)
    at += blocks
    exit_rows = lax.dynamic_index_in_dim(
        every[:, at : at + reaches].reshape(chains, rivers, reaches), mine, axis=1, keepdims=False
    )
    at += reaches
    keeps = lax.dynamic_index_in_dim(
        every[:, at].reshape(chains, rivers), mine, axis=1, keepdims=False
    )
    starts = lax.dynamic_index_in_dim(
        every[:, at + 1].reshape(chains, rivers), mine, axis=1, keepdims=False
    )

    joins = (river_of == mine.astype(jnp.float32))[:, :, None] & (
        reach_of[:, :, None] == jnp.arange(reaches, dtype=jnp.float32)[None, None, :]
    )
    weight = joins.astype(jnp.float32)
    branch_all = jnp.sum(weight[:, :, None, :] * outlets[:, :, :, None], axis=1)
    branch_exit = jnp.sum(branch_all * exit_rows[:, None, :], axis=2)

    flow = starts
    free_exit = []
    for sub_step in range(sub_steps):
        flow = keeps * flow + (1.0 - keeps) * branch_exit[:, sub_step]
        free_exit.append(flow)
    free_exit = jnp.stack(free_exit, axis=1)
    lag = jnp.arange(sub_steps)[:, None] - jnp.arange(sub_steps)[None, :]
    lag_f = jnp.maximum(lag, 0).astype(jnp.float32)
    response = jnp.where(
        lag[None] >= 0,
        (exit_rows[:, 0] * (1.0 - keeps))[:, None, None] * keeps[:, None, None] ** lag_f[None],
        0.0,
    )

    def advance(section, entry):
        moved = jnp.sum(response[section] * entry[None, :], axis=1) + free_exit[section]
        return jnp.where(section < me, moved, entry)

    entry = lax.fori_loop(0, chains, advance, head_inflow[0], unroll=chains <= 16)

    branch_in = lax.dynamic_index_in_dim(branch_all, me, axis=0, keepdims=False)
    first_reach = (jnp.arange(reaches) == 0).astype(jnp.float32)
    fed = branch_in + entry[:, None] * first_reach[None, :]
    main_mixed = jnp.einsum("rc,tc->tr", operator, fed, precision=lax.Precision.HIGHEST)
    main_flows = route_series(main_mixed, keep_main, prev_main)
    return (water, trib_flows[:, sub_steps - 1], main_flows[None, None])


def cores_paired(mesh):
    try:
        grid = mesh.devices
        if grid.ndim != 2 or grid.shape[1] % 2:
            return False
        for row in grid:
            for m in range(0, len(row), 2):
                a, b = row[m], row[m + 1]
                if tuple(a.coords) != tuple(b.coords) or a.core_on_chip == b.core_on_chip:
                    return False
        return True
    except AttributeError:
        return False


PAIRED = False


def solution(mesh):
    global PAIRED
    PAIRED = cores_paired(mesh)
    return jax.shard_map(
        local,
        mesh=mesh,
        in_specs=(
            P(("basin", "band"), None, None),
            P(("basin", "band"), None),
            P(("basin", "band"), None),
            P(("basin", "band"), None),
            P(("basin", "band")),
            P(("basin", "band")),
            P(("basin", "band"), None, None),
            P(("basin", "band"), None),
            P(("basin", "band"), None),
            P(("basin", "band")),
            P(("basin", "band")),
            P("band", "basin", None, None),
            P("band", "basin", None),
            P("band", "basin", None),
            P("band", None),
        ),
        out_specs=(
            P(("basin", "band"), None),
            P(("basin", "band"), None),
            P("band", "basin", None, None),
        ),
        check_vma=False,
    )
```

```python
import jax
import jax.numpy as jnp
from jax import lax
from jax.sharding import PartitionSpec as P


def land_update(precip, soil_water, capacity, evap_rate):
    water = soil_water
    runoff_steps = []
    for sub_step in range(precip.shape[1]):
        rain_now = precip[:, sub_step]
        runoff_now = rain_now * water / (water + capacity)
        water = (1.0 - evap_rate) * water + rain_now - runoff_now
        runoff_steps.append(runoff_now)
    return (jnp.stack(runoff_steps, axis=1), water)


def route_series(mixed, keep, previous):
    flow = previous
    flows = []
    for sub_step in range(mixed.shape[-2]):
        flow = keep * flow + (1.0 - keep) * mixed[..., sub_step, :]
        flows.append(flow)
    return jnp.stack(flows, axis=-2)


def pack_slots(values, labels, targets, peer_count, slot_cap):
    entries = targets.shape[0]
    position = jnp.arange(entries, dtype=jnp.int32)
    earlier = (targets[:, None] == targets[None, :]) & (position[None, :] < position[:, None])
    ranking = jnp.sum(earlier.astype(jnp.int32), axis=1)
    target_slot = targets * slot_cap + ranking
    buffer = (
        jnp.zeros((peer_count * slot_cap, values.shape[1]), values.dtype)
        .at[target_slot]
        .set(values)
    )
    slot_labels = jnp.zeros((peer_count * slot_cap,), jnp.int32).at[target_slot].set(labels)
    return (buffer, slot_labels)


def gather_lateral(runoff, tile_dest, tile_block, blocks, shards):
    tile_count, width = runoff.shape
    tile_cap = max(2, 2 * tile_count // shards)
    grid = ("basin", "band")
    if tile_cap >= blocks:
        block_ids = tile_dest * blocks + tile_block
        pick = (
            block_ids[None, :] == jnp.arange(shards * blocks, dtype=jnp.int32)[:, None]
        ).astype(jnp.float32)
        dense = jnp.dot(pick, runoff, precision=lax.Precision.HIGHEST)
        if not PAIRED or blocks % 2:
            arrived = lax.all_to_all(
                dense.reshape(shards, blocks, width), grid, split_axis=0, concat_axis=0, tiled=True
            )
            return jnp.sum(arrived, axis=0)
        return pair_exchange(dense, blocks, shards)
    buffer, slot_labels = pack_slots(runoff, tile_block, tile_dest, shards, tile_cap)
    arrived = lax.all_to_all(
        buffer.reshape(shards, tile_cap, width), grid, split_axis=0, concat_axis=0, tiled=True
    )
    arrived_ids = lax.all_to_all(
        slot_labels.reshape(shards, tile_cap), grid, split_axis=0, concat_axis=0, tiled=True
    )
    block_pick = (
        arrived_ids.reshape(-1)[:, None] == jnp.arange(blocks, dtype=jnp.int32)[None, :]
    ).astype(jnp.float32)
    return jnp.einsum(
        "sk,sx->kx", block_pick, arrived.reshape(-1, width), precision=lax.Precision.HIGHEST
    )


def pair_exchange(dense, blocks, shards):
    chains = lax.axis_size("basin")
    rivers = lax.axis_size("band")
    width = dense.shape[1]
    half = blocks // 2
    swap = [(m ^ 1, m) for m in range(rivers)]
    core = lax.axis_index("band") % 2
    parts = dense.reshape(chains, rivers // 2, 2, blocks, width)
    keep_side = lax.dynamic_index_in_dim(parts, core, axis=2, keepdims=False)
    give_side = lax.dynamic_index_in_dim(parts, 1 - core, axis=2, keepdims=False)
    chip_sum = keep_side + lax.ppermute(give_side, "band", swap)
    side = (jnp.arange(2) == core)[None, None, :, None, None]
    send = jnp.where(side, chip_sum[:, :, None, :half], chip_sum[:, :, None, half:])
    arrived = lax.all_to_all(
        send.reshape(shards, half, width), ("basin", "band"), split_axis=0, concat_axis=0, tiled=True
    ).reshape(chains, rivers // 2, 2, half, width)
    same = jnp.sum(jnp.where(side, arrived, 0.0), axis=(0, 1, 2))
    other = jnp.sum(jnp.where(side, 0.0, arrived), axis=(0, 1, 2))
    return jnp.concatenate([same, lax.ppermute(other, "band", swap)], axis=0)


def local(
    precip,
    soil_water,
    capacity,
    evap_rate,
    tile_dest,
    tile_block,
    trib_op,
    trib_keep,
    trib_prev,
    trib_river,
    trib_reach,
    main_op,
    main_keep,
    main_prev,
    head_inflow,
):
    tile_count = precip.shape[0]
    sub_steps = precip.shape[1]
    reaches = precip.shape[2]
    blocks = trib_op.shape[0]
    chains = lax.axis_size("basin")
    rivers = lax.axis_size("band")
    shards = chains * rivers
    grid = ("basin", "band")
    operator = main_op[0, 0]
    keep_main = main_keep[0, 0]
    prev_main = main_prev[0, 0]

    runoff, water = land_update(precip, soil_water, capacity, evap_rate)
    lateral = gather_lateral(
        runoff.reshape(tile_count, sub_steps * reaches), tile_dest, tile_block, blocks, shards
    )
    trib_mixed = jnp.einsum(
        "brc,btc->btr",
        trib_op,
        lateral.reshape(blocks, sub_steps, reaches),
        precision=lax.Precision.HIGHEST,
    )
    trib_flows = route_series(trib_mixed, trib_keep, trib_prev)
    outlet = trib_flows[:, :, reaches - 1]

    mine = lax.axis_index("band")
    me = lax.axis_index("basin")
    spread_lanes = reaches // blocks
    if reaches % blocks == 0 and sub_steps + 4 + spread_lanes <= reaches:
        column = lambda value: jnp.broadcast_to(value.reshape(-1, 1), (blocks, 1))
        tile = jnp.concatenate(
            [
                outlet,
                column(trib_river.astype(jnp.float32)),
                column(trib_reach.astype(jnp.float32)),
                column(keep_main[reaches - 1]),
                column(prev_main[reaches - 1]),
                operator[reaches - 1].reshape(blocks, spread_lanes),
            ],
            axis=1,
        )
        tile = jnp.pad(tile, ((0, 0), (0, reaches - tile.shape[1])))
        every = lax.all_to_all(
            jnp.broadcast_to(tile[None], (shards,) + tile.shape), grid, split_axis=0, concat_axis=0, tiled=True
        )
        outlets = every[:, :, :sub_steps].reshape(chains, rivers * blocks, sub_steps)
        river_of = every[:, :, sub_steps].reshape(chains, rivers * blocks)
        reach_of = every[:, :, sub_steps + 1].reshape(chains, rivers * blocks)
        facts = lax.dynamic_index_in_dim(
            every.reshape(chains, rivers, blocks, reaches), mine, axis=1, keepdims=False
        )
        keeps = facts[:, 0, sub_steps + 2]
        starts = facts[:, 0, sub_steps + 3]
        exit_rows = facts[:, :, sub_steps + 4 : sub_steps + 4 + spread_lanes].reshape(chains, reaches)
    else:
        payload = jnp.concatenate(
            [
                outlet.reshape(-1),
                trib_river.astype(jnp.float32),
                trib_reach.astype(jnp.float32),
                operator[reaches - 1],
                keep_main[reaches - 1 :],
                prev_main[reaches - 1 :],
            ]
        )
        width = payload.shape[0]
        padded = -(-width // 128) * 128
        payload = jnp.pad(payload, (0, padded - width))
        every = lax.all_to_all(
            jnp.broadcast_to(payload[None], (shards, padded)), grid, split_axis=0, concat_axis=0, tiled=True
        )
        at = 0
        outlets = every[:, at : at + blocks * sub_steps].reshape(chains, rivers * blocks, sub_steps)
        at += blocks * sub_steps
        river_of = every[:, at : at + blocks].reshape(chains, rivers * blocks)
        at += blocks
        reach_of = every[:, at : at + blocks].reshape(chains, rivers * blocks)
        at += blocks
        exit_rows = lax.dynamic_index_in_dim(
            every[:, at : at + reaches].reshape(chains, rivers, reaches), mine, axis=1, keepdims=False
        )
        at += reaches
        keeps = lax.dynamic_index_in_dim(
            every[:, at].reshape(chains, rivers), mine, axis=1, keepdims=False
        )
        starts = lax.dynamic_index_in_dim(
            every[:, at + 1].reshape(chains, rivers), mine, axis=1, keepdims=False
        )

    joins = (river_of == mine.astype(jnp.float32))[:, :, None] & (
        reach_of[:, :, None] == jnp.arange(reaches, dtype=jnp.float32)[None, None, :]
    )
    weight = joins.astype(jnp.float32)
    branch_all = jnp.sum(weight[:, :, None, :] * outlets[:, :, :, None], axis=1)
    branch_exit = jnp.sum(branch_all * exit_rows[:, None, :], axis=2)

    flow = starts
    free_exit = []
    for sub_step in range(sub_steps):
        flow = keeps * flow + (1.0 - keeps) * branch_exit[:, sub_step]
        free_exit.append(flow)
    free_exit = jnp.stack(free_exit, axis=1)
    lag = jnp.arange(sub_steps)[:, None] - jnp.arange(sub_steps)[None, :]
    lag_f = jnp.maximum(lag, 0).astype(jnp.float32)
    response = jnp.where(
        lag[None] >= 0,
        (exit_rows[:, 0] * (1.0 - keeps))[:, None, None] * keeps[:, None, None] ** lag_f[None],
        0.0,
    )

    def advance(section, entry):
        moved = jnp.sum(response[section] * entry[None, :], axis=1) + free_exit[section]
        return jnp.where(section < me, moved, entry)

    entry = lax.fori_loop(0, chains, advance, head_inflow[0], unroll=chains <= 16)

    branch_in = lax.dynamic_index_in_dim(branch_all, me, axis=0, keepdims=False)
    first_reach = (jnp.arange(reaches) == 0).astype(jnp.float32)
    fed = branch_in + entry[:, None] * first_reach[None, :]
    main_mixed = jnp.einsum("rc,tc->tr", operator, fed, precision=lax.Precision.HIGHEST)
    main_flows = route_series(main_mixed, keep_main, prev_main)
    return (water, trib_flows[:, sub_steps - 1], main_flows[None, None])


def cores_paired(mesh):
    try:
        grid = mesh.devices
        if grid.ndim != 2 or grid.shape[1] % 2:
            return False
        for row in grid:
            for m in range(0, len(row), 2):
                a, b = row[m], row[m + 1]
                if tuple(a.coords) != tuple(b.coords) or a.core_on_chip == b.core_on_chip:
                    return False
        return True
    except AttributeError:
        return False


PAIRED = False


def solution(mesh):
    global PAIRED
    PAIRED = cores_paired(mesh)
    return jax.shard_map(
        local,
        mesh=mesh,
        in_specs=(
            P(("basin", "band"), None, None),
            P(("basin", "band"), None),
            P(("basin", "band"), None),
            P(("basin", "band"), None),
            P(("basin", "band")),
            P(("basin", "band")),
            P(("basin", "band"), None, None),
            P(("basin", "band"), None),
            P(("basin", "band"), None),
            P(("basin", "band")),
            P(("basin", "band")),
            P("band", "basin", None, None),
            P("band", "basin", None),
            P("band", "basin", None),
            P("band", None),
        ),
        out_specs=(
            P(("basin", "band"), None),
            P(("basin", "band"), None),
            P("band", "basin", None, None),
        ),
        check_vma=False,
    )
```

```python
import jax
import jax.numpy as jnp
from jax import lax
from jax.sharding import PartitionSpec as P


def land_update(precip, soil_water, capacity, evap_rate):
    water = soil_water
    runoff_steps = []
    for sub_step in range(precip.shape[1]):
        rain_now = precip[:, sub_step]
        runoff_now = rain_now * water / (water + capacity)
        water = (1.0 - evap_rate) * water + rain_now - runoff_now
        runoff_steps.append(runoff_now)
    return (jnp.stack(runoff_steps, axis=1), water)


def route_series(mixed, keep, previous):
    flow = previous
    flows = []
    for sub_step in range(mixed.shape[-2]):
        flow = keep * flow + (1.0 - keep) * mixed[..., sub_step, :]
        flows.append(flow)
    return jnp.stack(flows, axis=-2)


def pack_slots(values, labels, targets, peer_count, slot_cap):
    entries = targets.shape[0]
    position = jnp.arange(entries, dtype=jnp.int32)
    earlier = (targets[:, None] == targets[None, :]) & (position[None, :] < position[:, None])
    ranking = jnp.sum(earlier.astype(jnp.int32), axis=1)
    target_slot = targets * slot_cap + ranking
    buffer = (
        jnp.zeros((peer_count * slot_cap, values.shape[1]), values.dtype)
        .at[target_slot]
        .set(values)
    )
    slot_labels = jnp.zeros((peer_count * slot_cap,), jnp.int32).at[target_slot].set(labels)
    return (buffer, slot_labels)


def gather_lateral(runoff, tile_dest, tile_block, blocks, shards):
    tile_count, width = runoff.shape
    tile_cap = max(2, 2 * tile_count // shards)
    grid = ("basin", "band")
    if tile_cap >= blocks:
        block_ids = tile_dest * blocks + tile_block
        pick = (
            block_ids[None, :] == jnp.arange(shards * blocks, dtype=jnp.int32)[:, None]
        ).astype(jnp.float32)
        dense = jnp.dot(pick, runoff, precision=lax.Precision.HIGHEST)
        if not PAIRED or blocks % 2:
            arrived = lax.all_to_all(
                dense.reshape(shards, blocks, width), grid, split_axis=0, concat_axis=0, tiled=True
            )
            return jnp.sum(arrived, axis=0)
        return pair_exchange(dense, blocks, shards)
    buffer, slot_labels = pack_slots(runoff, tile_block, tile_dest, shards, tile_cap)
    arrived = lax.all_to_all(
        buffer.reshape(shards, tile_cap, width), grid, split_axis=0, concat_axis=0, tiled=True
    )
    arrived_ids = lax.all_to_all(
        slot_labels.reshape(shards, tile_cap), grid, split_axis=0, concat_axis=0, tiled=True
    )
    block_pick = (
        arrived_ids.reshape(-1)[:, None] == jnp.arange(blocks, dtype=jnp.int32)[None, :]
    ).astype(jnp.float32)
    return jnp.einsum(
        "sk,sx->kx", block_pick, arrived.reshape(-1, width), precision=lax.Precision.HIGHEST
    )


def pair_exchange(dense, blocks, shards):
    chains = lax.axis_size("basin")
    rivers = lax.axis_size("band")
    width = dense.shape[1]
    half = blocks // 2
    swap = [(m ^ 1, m) for m in range(rivers)]
    core = lax.axis_index("band") % 2
    parts = dense.reshape(chains, rivers // 2, 2, blocks, width)
    keep_side = lax.dynamic_index_in_dim(parts, core, axis=2, keepdims=False)
    give_side = lax.dynamic_index_in_dim(parts, 1 - core, axis=2, keepdims=False)
    chip_sum = keep_side + lax.ppermute(give_side, "band", swap)
    side = (jnp.arange(2) == core)[None, None, :, None, None]
    send = jnp.where(side, chip_sum[:, :, None, :half], chip_sum[:, :, None, half:])
    arrived = lax.all_to_all(
        send.reshape(shards, half, width), ("basin", "band"), split_axis=0, concat_axis=0, tiled=True
    ).reshape(chains, rivers // 2, 2, half, width)
    same = jnp.sum(jnp.where(side, arrived, 0.0), axis=(0, 1, 2))
    other = jnp.sum(jnp.where(side, 0.0, arrived), axis=(0, 1, 2))
    return jnp.concatenate([same, lax.ppermute(other, "band", swap)], axis=0)


def local(
    precip,
    soil_water,
    capacity,
    evap_rate,
    tile_dest,
    tile_block,
    trib_op,
    trib_keep,
    trib_prev,
    trib_river,
    trib_reach,
    main_op,
    main_keep,
    main_prev,
    head_inflow,
):
    tile_count = precip.shape[0]
    sub_steps = precip.shape[1]
    reaches = precip.shape[2]
    blocks = trib_op.shape[0]
    chains = lax.axis_size("basin")
    rivers = lax.axis_size("band")
    shards = chains * rivers
    grid = ("basin", "band")
    operator = main_op[0, 0]
    keep_main = main_keep[0, 0]
    prev_main = main_prev[0, 0]

    runoff, water = land_update(precip, soil_water, capacity, evap_rate)
    lateral = gather_lateral(
        runoff.reshape(tile_count, sub_steps * reaches), tile_dest, tile_block, blocks, shards
    )
    trib_mixed = jnp.einsum(
        "brc,btc->btr",
        trib_op,
        lateral.reshape(blocks, sub_steps, reaches),
        precision=lax.Precision.HIGHEST,
    )
    trib_flows = route_series(trib_mixed, trib_keep, trib_prev)
    outlet = trib_flows[:, :, reaches - 1]

    mine = lax.axis_index("band")
    me = lax.axis_index("basin")
    spread_lanes = reaches // blocks
    if reaches % blocks == 0 and sub_steps + 4 + spread_lanes <= reaches:
        lane = lax.broadcasted_iota(jnp.int32, (blocks, reaches), 1)
        tile = jnp.pad(outlet, ((0, 0), (0, reaches - sub_steps)))
        columns = (
            trib_river.astype(jnp.float32)[:, None],
            trib_reach.astype(jnp.float32)[:, None],
            keep_main[reaches - 1 :][None, :],
            prev_main[reaches - 1 :][None, :],
        )
        for offset, value in enumerate(columns):
            tile = tile + jnp.where(lane == sub_steps + offset, value, 0.0)
        spread_row = operator[reaches - 1].reshape(blocks, spread_lanes)
        tile = tile + jnp.pad(
            spread_row, ((0, 0), (sub_steps + 4, reaches - sub_steps - 4 - spread_lanes))
        )
        every = lax.all_to_all(
            jnp.broadcast_to(tile[None], (shards,) + tile.shape), grid, split_axis=0, concat_axis=0, tiled=True
        )
        outlets = every[:, :, :sub_steps].reshape(chains, rivers * blocks, sub_steps)
        river_of = every[:, :, sub_steps].reshape(chains, rivers * blocks)
        reach_of = every[:, :, sub_steps + 1].reshape(chains, rivers * blocks)
        facts = lax.dynamic_index_in_dim(
            every.reshape(chains, rivers, blocks, reaches), mine, axis=1, keepdims=False
        )
        keeps = facts[:, 0, sub_steps + 2]
        starts = facts[:, 0, sub_steps + 3]
        exit_rows = facts[:, :, sub_steps + 4 : sub_steps + 4 + spread_lanes].reshape(chains, reaches)
    else:
        payload = jnp.concatenate(
            [
                outlet.reshape(-1),
                trib_river.astype(jnp.float32),
                trib_reach.astype(jnp.float32),
                operator[reaches - 1],
                keep_main[reaches - 1 :],
                prev_main[reaches - 1 :],
            ]
        )
        width = payload.shape[0]
        padded = -(-width // 128) * 128
        payload = jnp.pad(payload, (0, padded - width))
        every = lax.all_to_all(
            jnp.broadcast_to(payload[None], (shards, padded)), grid, split_axis=0, concat_axis=0, tiled=True
        )
        at = 0
        outlets = every[:, at : at + blocks * sub_steps].reshape(chains, rivers * blocks, sub_steps)
        at += blocks * sub_steps
        river_of = every[:, at : at + blocks].reshape(chains, rivers * blocks)
        at += blocks
        reach_of = every[:, at : at + blocks].reshape(chains, rivers * blocks)
        at += blocks
        exit_rows = lax.dynamic_index_in_dim(
            every[:, at : at + reaches].reshape(chains, rivers, reaches), mine, axis=1, keepdims=False
        )
        at += reaches
        keeps = lax.dynamic_index_in_dim(
            every[:, at].reshape(chains, rivers), mine, axis=1, keepdims=False
        )
        starts = lax.dynamic_index_in_dim(
            every[:, at + 1].reshape(chains, rivers), mine, axis=1, keepdims=False
        )

    joins = (river_of == mine.astype(jnp.float32))[:, :, None] & (
        reach_of[:, :, None] == jnp.arange(reaches, dtype=jnp.float32)[None, None, :]
    )
    weight = joins.astype(jnp.float32)
    branch_all = jnp.sum(weight[:, :, None, :] * outlets[:, :, :, None], axis=1)
    branch_exit = jnp.sum(branch_all * exit_rows[:, None, :], axis=2)

    flow = starts
    free_exit = []
    for sub_step in range(sub_steps):
        flow = keeps * flow + (1.0 - keeps) * branch_exit[:, sub_step]
        free_exit.append(flow)
    free_exit = jnp.stack(free_exit, axis=1)
    lag = jnp.arange(sub_steps)[:, None] - jnp.arange(sub_steps)[None, :]
    lag_f = jnp.maximum(lag, 0).astype(jnp.float32)
    response = jnp.where(
        lag[None] >= 0,
        (exit_rows[:, 0] * (1.0 - keeps))[:, None, None] * keeps[:, None, None] ** lag_f[None],
        0.0,
    )

    def advance(section, entry):
        moved = jnp.sum(response[section] * entry[None, :], axis=1) + free_exit[section]
        return jnp.where(section < me, moved, entry)

    entry = lax.fori_loop(0, chains, advance, head_inflow[0], unroll=chains <= 16)

    branch_in = lax.dynamic_index_in_dim(branch_all, me, axis=0, keepdims=False)
    first_reach = (jnp.arange(reaches) == 0).astype(jnp.float32)
    fed = branch_in + entry[:, None] * first_reach[None, :]
    main_mixed = jnp.einsum("rc,tc->tr", operator, fed, precision=lax.Precision.HIGHEST)
    main_flows = route_series(main_mixed, keep_main, prev_main)
    return (water, trib_flows[:, sub_steps - 1], main_flows[None, None])


def cores_paired(mesh):
    try:
        grid = mesh.devices
        if grid.ndim != 2 or grid.shape[1] % 2:
            return False
        for row in grid:
            for m in range(0, len(row), 2):
                a, b = row[m], row[m + 1]
                if tuple(a.coords) != tuple(b.coords) or a.core_on_chip == b.core_on_chip:
                    return False
        return True
    except AttributeError:
        return False


PAIRED = False


def solution(mesh):
    global PAIRED
    PAIRED = cores_paired(mesh)
    return jax.shard_map(
        local,
        mesh=mesh,
        in_specs=(
            P(("basin", "band"), None, None),
            P(("basin", "band"), None),
            P(("basin", "band"), None),
            P(("basin", "band"), None),
            P(("basin", "band")),
            P(("basin", "band")),
            P(("basin", "band"), None, None),
            P(("basin", "band"), None),
            P(("basin", "band"), None),
            P(("basin", "band")),
            P(("basin", "band")),
            P("band", "basin", None, None),
            P("band", "basin", None),
            P("band", "basin", None),
            P("band", None),
        ),
        out_specs=(
            P(("basin", "band"), None),
            P(("basin", "band"), None),
            P("band", "basin", None, None),
        ),
        check_vma=False,
    )
```

```python
import jax
import jax.numpy as jnp
from jax import lax
from jax.sharding import PartitionSpec as P


def land_update(precip, soil_water, capacity, evap_rate):
    water = soil_water
    runoff_steps = []
    for sub_step in range(precip.shape[1]):
        rain_now = precip[:, sub_step]
        runoff_now = rain_now * water / (water + capacity)
        water = (1.0 - evap_rate) * water + rain_now - runoff_now
        runoff_steps.append(runoff_now)
    return (jnp.stack(runoff_steps, axis=1), water)


def route_series(mixed, keep, previous):
    flow = previous
    flows = []
    for sub_step in range(mixed.shape[-2]):
        flow = keep * flow + (1.0 - keep) * mixed[..., sub_step, :]
        flows.append(flow)
    return jnp.stack(flows, axis=-2)


def pack_slots(values, labels, targets, peer_count, slot_cap):
    entries = targets.shape[0]
    position = jnp.arange(entries, dtype=jnp.int32)
    earlier = (targets[:, None] == targets[None, :]) & (position[None, :] < position[:, None])
    ranking = jnp.sum(earlier.astype(jnp.int32), axis=1)
    target_slot = targets * slot_cap + ranking
    buffer = (
        jnp.zeros((peer_count * slot_cap, values.shape[1]), values.dtype)
        .at[target_slot]
        .set(values)
    )
    slot_labels = jnp.zeros((peer_count * slot_cap,), jnp.int32).at[target_slot].set(labels)
    return (buffer, slot_labels)


def gather_lateral(runoff, tile_dest, tile_block, blocks, shards):
    tile_count, width = runoff.shape
    tile_cap = max(2, 2 * tile_count // shards)
    grid = ("basin", "band")
    if tile_cap >= blocks:
        block_ids = tile_dest * blocks + tile_block
        pick = (
            block_ids[None, :] == jnp.arange(shards * blocks, dtype=jnp.int32)[:, None]
        ).astype(jnp.float32)
        dense = jnp.dot(pick, runoff, precision=lax.Precision.HIGHEST)
        if not PAIRED or blocks % 2:
            arrived = lax.all_to_all(
                dense.reshape(shards, blocks, width), grid, split_axis=0, concat_axis=0, tiled=True
            )
            return jnp.sum(arrived, axis=0)
        return pair_exchange(dense, blocks, shards)
    buffer, slot_labels = pack_slots(runoff, tile_block, tile_dest, shards, tile_cap)
    arrived = lax.all_to_all(
        buffer.reshape(shards, tile_cap, width), grid, split_axis=0, concat_axis=0, tiled=True
    )
    arrived_ids = lax.all_to_all(
        slot_labels.reshape(shards, tile_cap), grid, split_axis=0, concat_axis=0, tiled=True
    )
    block_pick = (
        arrived_ids.reshape(-1)[:, None] == jnp.arange(blocks, dtype=jnp.int32)[None, :]
    ).astype(jnp.float32)
    return jnp.einsum(
        "sk,sx->kx", block_pick, arrived.reshape(-1, width), precision=lax.Precision.HIGHEST
    )


def pair_exchange(dense, blocks, shards):
    chains = lax.axis_size("basin")
    rivers = lax.axis_size("band")
    width = dense.shape[1]
    half = blocks // 2
    swap = [(m ^ 1, m) for m in range(rivers)]
    core = lax.axis_index("band") % 2
    parts = dense.reshape(chains, rivers // 2, 2, blocks, width)
    keep_side = lax.dynamic_index_in_dim(parts, core, axis=2, keepdims=False)
    give_side = lax.dynamic_index_in_dim(parts, 1 - core, axis=2, keepdims=False)
    chip_sum = keep_side + lax.ppermute(give_side, "band", swap)
    side = (jnp.arange(2) == core)[None, None, :, None, None]
    send = jnp.where(side, chip_sum[:, :, None, :half], chip_sum[:, :, None, half:])
    arrived = lax.all_to_all(
        send.reshape(shards, half, width), ("basin", "band"), split_axis=0, concat_axis=0, tiled=True
    ).reshape(chains, rivers // 2, 2, half, width)
    same = jnp.sum(jnp.where(side, arrived, 0.0), axis=(0, 1, 2))
    other = jnp.sum(jnp.where(side, 0.0, arrived), axis=(0, 1, 2))
    return jnp.concatenate([same, lax.ppermute(other, "band", swap)], axis=0)


def local(
    precip,
    soil_water,
    capacity,
    evap_rate,
    tile_dest,
    tile_block,
    trib_op,
    trib_keep,
    trib_prev,
    trib_river,
    trib_reach,
    main_op,
    main_keep,
    main_prev,
    head_inflow,
):
    tile_count = precip.shape[0]
    sub_steps = precip.shape[1]
    reaches = precip.shape[2]
    blocks = trib_op.shape[0]
    chains = lax.axis_size("basin")
    rivers = lax.axis_size("band")
    shards = chains * rivers
    grid = ("basin", "band")
    operator = main_op[0, 0]
    keep_main = main_keep[0, 0]
    prev_main = main_prev[0, 0]

    runoff, water = land_update(precip, soil_water, capacity, evap_rate)
    lateral = gather_lateral(
        runoff.reshape(tile_count, sub_steps * reaches), tile_dest, tile_block, blocks, shards
    )
    trib_mixed = jnp.einsum(
        "brc,btc->btr",
        trib_op,
        lateral.reshape(blocks, sub_steps, reaches),
        precision=lax.Precision.HIGHEST,
    )
    trib_flows = route_series(trib_mixed, trib_keep, trib_prev)
    exit_mixed = jnp.sum(
        lateral.reshape(blocks, sub_steps, reaches) * trib_op[:, reaches - 1][:, None, :], axis=2
    )
    outlet = route_series(
        exit_mixed[:, :, None], trib_keep[:, reaches - 1 :], trib_prev[:, reaches - 1 :]
    )[:, :, 0]

    mine = lax.axis_index("band")
    me = lax.axis_index("basin")
    spread_lanes = reaches // blocks
    if reaches % blocks == 0 and sub_steps + 4 + spread_lanes <= reaches:
        lane = lax.broadcasted_iota(jnp.int32, (blocks, reaches), 1)
        tile = jnp.pad(outlet, ((0, 0), (0, reaches - sub_steps)))
        columns = (
            trib_river.astype(jnp.float32)[:, None],
            trib_reach.astype(jnp.float32)[:, None],
            keep_main[reaches - 1 :][None, :],
            prev_main[reaches - 1 :][None, :],
        )
        for offset, value in enumerate(columns):
            tile = tile + jnp.where(lane == sub_steps + offset, value, 0.0)
        spread_row = operator[reaches - 1].reshape(blocks, spread_lanes)
        tile = tile + jnp.pad(
            spread_row, ((0, 0), (sub_steps + 4, reaches - sub_steps - 4 - spread_lanes))
        )
        every = lax.all_to_all(
            jnp.broadcast_to(tile[None], (shards,) + tile.shape), grid, split_axis=0, concat_axis=0, tiled=True
        )
        outlets = every[:, :, :sub_steps].reshape(chains, rivers * blocks, sub_steps)
        river_of = every[:, :, sub_steps].reshape(chains, rivers * blocks)
        reach_of = every[:, :, sub_steps + 1].reshape(chains, rivers * blocks)
        facts = lax.dynamic_index_in_dim(
            every.reshape(chains, rivers, blocks, reaches), mine, axis=1, keepdims=False
        )
        keeps = facts[:, 0, sub_steps + 2]
        starts = facts[:, 0, sub_steps + 3]
        exit_rows = facts[:, :, sub_steps + 4 : sub_steps + 4 + spread_lanes].reshape(chains, reaches)
    else:
        payload = jnp.concatenate(
            [
                outlet.reshape(-1),
                trib_river.astype(jnp.float32),
                trib_reach.astype(jnp.float32),
                operator[reaches - 1],
                keep_main[reaches - 1 :],
                prev_main[reaches - 1 :],
            ]
        )
        width = payload.shape[0]
        padded = -(-width // 128) * 128
        payload = jnp.pad(payload, (0, padded - width))
        every = lax.all_to_all(
            jnp.broadcast_to(payload[None], (shards, padded)), grid, split_axis=0, concat_axis=0, tiled=True
        )
        at = 0
        outlets = every[:, at : at + blocks * sub_steps].reshape(chains, rivers * blocks, sub_steps)
        at += blocks * sub_steps
        river_of = every[:, at : at + blocks].reshape(chains, rivers * blocks)
        at += blocks
        reach_of = every[:, at : at + blocks].reshape(chains, rivers * blocks)
        at += blocks
        exit_rows = lax.dynamic_index_in_dim(
            every[:, at : at + reaches].reshape(chains, rivers, reaches), mine, axis=1, keepdims=False
        )
        at += reaches
        keeps = lax.dynamic_index_in_dim(
            every[:, at].reshape(chains, rivers), mine, axis=1, keepdims=False
        )
        starts = lax.dynamic_index_in_dim(
            every[:, at + 1].reshape(chains, rivers), mine, axis=1, keepdims=False
        )

    joins = (river_of == mine.astype(jnp.float32))[:, :, None] & (
        reach_of[:, :, None] == jnp.arange(reaches, dtype=jnp.float32)[None, None, :]
    )
    weight = joins.astype(jnp.float32)
    branch_all = jnp.sum(weight[:, :, None, :] * outlets[:, :, :, None], axis=1)
    branch_exit = jnp.sum(branch_all * exit_rows[:, None, :], axis=2)

    flow = starts
    free_exit = []
    for sub_step in range(sub_steps):
        flow = keeps * flow + (1.0 - keeps) * branch_exit[:, sub_step]
        free_exit.append(flow)
    free_exit = jnp.stack(free_exit, axis=1)
    lag = jnp.arange(sub_steps)[:, None] - jnp.arange(sub_steps)[None, :]
    lag_f = jnp.maximum(lag, 0).astype(jnp.float32)
    response = jnp.where(
        lag[None] >= 0,
        (exit_rows[:, 0] * (1.0 - keeps))[:, None, None] * keeps[:, None, None] ** lag_f[None],
        0.0,
    )

    def advance(section, entry):
        moved = jnp.sum(response[section] * entry[None, :], axis=1) + free_exit[section]
        return jnp.where(section < me, moved, entry)

    entry = lax.fori_loop(0, chains, advance, head_inflow[0], unroll=chains <= 16)

    branch_in = lax.dynamic_index_in_dim(branch_all, me, axis=0, keepdims=False)
    first_reach = (jnp.arange(reaches) == 0).astype(jnp.float32)
    fed = branch_in + entry[:, None] * first_reach[None, :]
    main_mixed = jnp.einsum("rc,tc->tr", operator, fed, precision=lax.Precision.HIGHEST)
    main_flows = route_series(main_mixed, keep_main, prev_main)
    return (water, trib_flows[:, sub_steps - 1], main_flows[None, None])


def cores_paired(mesh):
    try:
        grid = mesh.devices
        if grid.ndim != 2 or grid.shape[1] % 2:
            return False
        for row in grid:
            for m in range(0, len(row), 2):
                a, b = row[m], row[m + 1]
                if tuple(a.coords) != tuple(b.coords) or a.core_on_chip == b.core_on_chip:
                    return False
        return True
    except AttributeError:
        return False


PAIRED = False


def solution(mesh):
    global PAIRED
    PAIRED = cores_paired(mesh)
    return jax.shard_map(
        local,
        mesh=mesh,
        in_specs=(
            P(("basin", "band"), None, None),
            P(("basin", "band"), None),
            P(("basin", "band"), None),
            P(("basin", "band"), None),
            P(("basin", "band")),
            P(("basin", "band")),
            P(("basin", "band"), None, None),
            P(("basin", "band"), None),
            P(("basin", "band"), None),
            P(("basin", "band")),
            P(("basin", "band")),
            P("band", "basin", None, None),
            P("band", "basin", None),
            P("band", "basin", None),
            P("band", None),
        ),
        out_specs=(
            P(("basin", "band"), None),
            P(("basin", "band"), None),
            P("band", "basin", None, None),
        ),
        check_vma=False,
    )
```

```python
import jax
import jax.numpy as jnp
from jax import lax
from jax.sharding import PartitionSpec as P


def land_update(precip, soil_water, capacity, evap_rate):
    water = soil_water
    runoff_steps = []
    for sub_step in range(precip.shape[1]):
        rain_now = precip[:, sub_step]
        runoff_now = rain_now * water / (water + capacity)
        water = (1.0 - evap_rate) * water + rain_now - runoff_now
        runoff_steps.append(runoff_now)
    return (jnp.stack(runoff_steps, axis=1), water)


def route_series(mixed, keep, previous):
    flow = previous
    flows = []
    for sub_step in range(mixed.shape[-2]):
        flow = keep * flow + (1.0 - keep) * mixed[..., sub_step, :]
        flows.append(flow)
    return jnp.stack(flows, axis=-2)


def pack_slots(values, labels, targets, peer_count, slot_cap):
    entries = targets.shape[0]
    position = jnp.arange(entries, dtype=jnp.int32)
    earlier = (targets[:, None] == targets[None, :]) & (position[None, :] < position[:, None])
    ranking = jnp.sum(earlier.astype(jnp.int32), axis=1)
    target_slot = targets * slot_cap + ranking
    buffer = (
        jnp.zeros((peer_count * slot_cap, values.shape[1]), values.dtype)
        .at[target_slot]
        .set(values)
    )
    slot_labels = jnp.zeros((peer_count * slot_cap,), jnp.int32).at[target_slot].set(labels)
    return (buffer, slot_labels)


def gather_lateral(runoff, tile_dest, tile_block, blocks, shards):
    tile_count, width = runoff.shape
    tile_cap = max(2, 2 * tile_count // shards)
    grid = ("basin", "band")
    if tile_cap >= blocks:
        block_ids = tile_dest * blocks + tile_block
        pick = (
            block_ids[None, :] == jnp.arange(shards * blocks, dtype=jnp.int32)[:, None]
        ).astype(jnp.float32)
        dense = jnp.dot(pick, runoff, precision=lax.Precision.HIGHEST)
        if not PAIRED or blocks % 2:
            arrived = lax.all_to_all(
                dense.reshape(shards, blocks, width), grid, split_axis=0, concat_axis=0, tiled=True
            )
            return jnp.sum(arrived, axis=0)
        return pair_exchange(dense, blocks, shards)
    buffer, slot_labels = pack_slots(runoff, tile_block, tile_dest, shards, tile_cap)
    arrived = lax.all_to_all(
        buffer.reshape(shards, tile_cap, width), grid, split_axis=0, concat_axis=0, tiled=True
    )
    arrived_ids = lax.all_to_all(
        slot_labels.reshape(shards, tile_cap), grid, split_axis=0, concat_axis=0, tiled=True
    )
    block_pick = (
        arrived_ids.reshape(-1)[:, None] == jnp.arange(blocks, dtype=jnp.int32)[None, :]
    ).astype(jnp.float32)
    return jnp.einsum(
        "sk,sx->kx", block_pick, arrived.reshape(-1, width), precision=lax.Precision.HIGHEST
    )


def pair_exchange(dense, blocks, shards):
    chains = lax.axis_size("basin")
    rivers = lax.axis_size("band")
    width = dense.shape[1]
    half = blocks // 2
    swap = [(m ^ 1, m) for m in range(rivers)]
    core = lax.axis_index("band") % 2
    parts = dense.reshape(chains, rivers // 2, 2, blocks, width)
    keep_side = lax.dynamic_index_in_dim(parts, core, axis=2, keepdims=False)
    give_side = lax.dynamic_index_in_dim(parts, 1 - core, axis=2, keepdims=False)
    chip_sum = keep_side + lax.ppermute(give_side, "band", swap)
    side = (jnp.arange(2) == core)[None, None, :, None, None]
    send = jnp.where(side, chip_sum[:, :, None, :half], chip_sum[:, :, None, half:])
    arrived = lax.all_to_all(
        send.reshape(shards, half, width), ("basin", "band"), split_axis=0, concat_axis=0, tiled=True
    ).reshape(chains, rivers // 2, 2, half, width)
    same = jnp.sum(jnp.where(side, arrived, 0.0), axis=(0, 1, 2))
    other = jnp.sum(jnp.where(side, 0.0, arrived), axis=(0, 1, 2))
    return jnp.concatenate([same, lax.ppermute(other, "band", swap)], axis=0)


def local(
    precip,
    soil_water,
    capacity,
    evap_rate,
    tile_dest,
    tile_block,
    trib_op,
    trib_keep,
    trib_prev,
    trib_river,
    trib_reach,
    main_op,
    main_keep,
    main_prev,
    head_inflow,
):
    tile_count = precip.shape[0]
    sub_steps = precip.shape[1]
    reaches = precip.shape[2]
    blocks = trib_op.shape[0]
    chains = lax.axis_size("basin")
    rivers = lax.axis_size("band")
    shards = chains * rivers
    grid = ("basin", "band")
    operator = main_op[0, 0]
    keep_main = main_keep[0, 0]
    prev_main = main_prev[0, 0]

    runoff, water = land_update(precip, soil_water, capacity, evap_rate)
    lateral = gather_lateral(
        runoff.reshape(tile_count, sub_steps * reaches), tile_dest, tile_block, blocks, shards
    )
    trib_mixed = jnp.einsum(
        "brc,btc->btr",
        trib_op,
        lateral.reshape(blocks, sub_steps, reaches),
        precision=lax.Precision.HIGHEST,
    )
    trib_flows = route_series(trib_mixed, trib_keep, trib_prev)
    exit_mixed = jnp.sum(
        lateral.reshape(blocks, sub_steps, reaches) * trib_op[:, reaches - 1][:, None, :], axis=2
    )
    outlet = route_series(
        exit_mixed[:, :, None], trib_keep[:, reaches - 1 :], trib_prev[:, reaches - 1 :]
    )[:, :, 0]

    mine = lax.axis_index("band")
    me = lax.axis_index("basin")
    spread_lanes = reaches // blocks
    if reaches % blocks == 0 and sub_steps + 4 + spread_lanes <= reaches:
        lane = lax.broadcasted_iota(jnp.int32, (blocks, reaches), 1)
        columns = (
            trib_river.astype(jnp.float32)[:, None],
            trib_reach.astype(jnp.float32)[:, None],
            keep_main[reaches - 1 :][None, :],
            prev_main[reaches - 1 :][None, :],
        )
        spread_row = operator[reaches - 1].reshape(blocks, spread_lanes)
        static_tile = jnp.pad(
            spread_row, ((0, 0), (sub_steps + 4, reaches - sub_steps - 4 - spread_lanes))
        )
        for offset, value in enumerate(columns):
            static_tile = static_tile + jnp.where(lane == sub_steps + offset, value, 0.0)
        static_tile = lax.optimization_barrier(static_tile)
        tile = jnp.pad(outlet, ((0, 0), (0, reaches - sub_steps))) + static_tile
        every = lax.all_to_all(
            jnp.broadcast_to(tile[None], (shards,) + tile.shape), grid, split_axis=0, concat_axis=0, tiled=True
        )
        outlets = every[:, :, :sub_steps].reshape(chains, rivers * blocks, sub_steps)
        river_of = every[:, :, sub_steps].reshape(chains, rivers * blocks)
        reach_of = every[:, :, sub_steps + 1].reshape(chains, rivers * blocks)
        facts = lax.dynamic_index_in_dim(
            every.reshape(chains, rivers, blocks, reaches), mine, axis=1, keepdims=False
        )
        keeps = facts[:, 0, sub_steps + 2]
        starts = facts[:, 0, sub_steps + 3]
        exit_rows = facts[:, :, sub_steps + 4 : sub_steps + 4 + spread_lanes].reshape(chains, reaches)
    else:
        payload = jnp.concatenate(
            [
                outlet.reshape(-1),
                trib_river.astype(jnp.float32),
                trib_reach.astype(jnp.float32),
                operator[reaches - 1],
                keep_main[reaches - 1 :],
                prev_main[reaches - 1 :],
            ]
        )
        width = payload.shape[0]
        padded = -(-width // 128) * 128
        payload = jnp.pad(payload, (0, padded - width))
        every = lax.all_to_all(
            jnp.broadcast_to(payload[None], (shards, padded)), grid, split_axis=0, concat_axis=0, tiled=True
        )
        at = 0
        outlets = every[:, at : at + blocks * sub_steps].reshape(chains, rivers * blocks, sub_steps)
        at += blocks * sub_steps
        river_of = every[:, at : at + blocks].reshape(chains, rivers * blocks)
        at += blocks
        reach_of = every[:, at : at + blocks].reshape(chains, rivers * blocks)
        at += blocks
        exit_rows = lax.dynamic_index_in_dim(
            every[:, at : at + reaches].reshape(chains, rivers, reaches), mine, axis=1, keepdims=False
        )
        at += reaches
        keeps = lax.dynamic_index_in_dim(
            every[:, at].reshape(chains, rivers), mine, axis=1, keepdims=False
        )
        starts = lax.dynamic_index_in_dim(
            every[:, at + 1].reshape(chains, rivers), mine, axis=1, keepdims=False
        )

    joins = (river_of == mine.astype(jnp.float32))[:, :, None] & (
        reach_of[:, :, None] == jnp.arange(reaches, dtype=jnp.float32)[None, None, :]
    )
    weight = joins.astype(jnp.float32)
    branch_all = jnp.sum(weight[:, :, None, :] * outlets[:, :, :, None], axis=1)
    branch_exit = jnp.sum(branch_all * exit_rows[:, None, :], axis=2)

    flow = starts
    free_exit = []
    for sub_step in range(sub_steps):
        flow = keeps * flow + (1.0 - keeps) * branch_exit[:, sub_step]
        free_exit.append(flow)
    free_exit = jnp.stack(free_exit, axis=1)
    lag = jnp.arange(sub_steps)[:, None] - jnp.arange(sub_steps)[None, :]
    lag_f = jnp.maximum(lag, 0).astype(jnp.float32)
    response = jnp.where(
        lag[None] >= 0,
        (exit_rows[:, 0] * (1.0 - keeps))[:, None, None] * keeps[:, None, None] ** lag_f[None],
        0.0,
    )

    def advance(section, entry):
        moved = jnp.sum(response[section] * entry[None, :], axis=1) + free_exit[section]
        return jnp.where(section < me, moved, entry)

    entry = lax.fori_loop(0, chains, advance, head_inflow[0], unroll=chains <= 16)

    branch_in = lax.dynamic_index_in_dim(branch_all, me, axis=0, keepdims=False)
    first_reach = (jnp.arange(reaches) == 0).astype(jnp.float32)
    fed = branch_in + entry[:, None] * first_reach[None, :]
    main_mixed = jnp.einsum("rc,tc->tr", operator, fed, precision=lax.Precision.HIGHEST)
    main_flows = route_series(main_mixed, keep_main, prev_main)
    return (water, trib_flows[:, sub_steps - 1], main_flows[None, None])


def cores_paired(mesh):
    try:
        grid = mesh.devices
        if grid.ndim != 2 or grid.shape[1] % 2:
            return False
        for row in grid:
            for m in range(0, len(row), 2):
                a, b = row[m], row[m + 1]
                if tuple(a.coords) != tuple(b.coords) or a.core_on_chip == b.core_on_chip:
                    return False
        return True
    except AttributeError:
        return False


PAIRED = False


def solution(mesh):
    global PAIRED
    PAIRED = cores_paired(mesh)
    return jax.shard_map(
        local,
        mesh=mesh,
        in_specs=(
            P(("basin", "band"), None, None),
            P(("basin", "band"), None),
            P(("basin", "band"), None),
            P(("basin", "band"), None),
            P(("basin", "band")),
            P(("basin", "band")),
            P(("basin", "band"), None, None),
            P(("basin", "band"), None),
            P(("basin", "band"), None),
            P(("basin", "band")),
            P(("basin", "band")),
            P("band", "basin", None, None),
            P("band", "basin", None),
            P("band", "basin", None),
            P("band", None),
        ),
        out_specs=(
            P(("basin", "band"), None),
            P(("basin", "band"), None),
            P("band", "basin", None, None),
        ),
        check_vma=False,
    )
```

```python
import jax
import jax.numpy as jnp
from jax import lax
from jax.sharding import Mesh, PartitionSpec as P


def land_update(precip, soil_water, capacity, evap_rate):
    water = soil_water
    runoff_steps = []
    for sub_step in range(precip.shape[1]):
        rain_now = precip[:, sub_step]
        runoff_now = rain_now * water / (water + capacity)
        water = (1.0 - evap_rate) * water + rain_now - runoff_now
        runoff_steps.append(runoff_now)
    return (jnp.stack(runoff_steps, axis=1), water)


def route_series(mixed, keep, previous):
    flow = previous
    flows = []
    for sub_step in range(mixed.shape[-2]):
        flow = keep * flow + (1.0 - keep) * mixed[..., sub_step, :]
        flows.append(flow)
    return jnp.stack(flows, axis=-2)


def pack_slots(values, labels, targets, peer_count, slot_cap):
    entries = targets.shape[0]
    position = jnp.arange(entries, dtype=jnp.int32)
    earlier = (targets[:, None] == targets[None, :]) & (position[None, :] < position[:, None])
    ranking = jnp.sum(earlier.astype(jnp.int32), axis=1)
    target_slot = targets * slot_cap + ranking
    buffer = (
        jnp.zeros((peer_count * slot_cap, values.shape[1]), values.dtype)
        .at[target_slot]
        .set(values)
    )
    slot_labels = jnp.zeros((peer_count * slot_cap,), jnp.int32).at[target_slot].set(labels)
    return (buffer, slot_labels)


def gather_lateral(runoff, tile_dest, tile_block, blocks, shards):
    tile_count, width = runoff.shape
    tile_cap = max(2, 2 * tile_count // shards)
    grid = GRID
    if tile_cap >= blocks:
        block_ids = tile_dest * blocks + tile_block
        pick = (
            block_ids[None, :] == jnp.arange(shards * blocks, dtype=jnp.int32)[:, None]
        ).astype(jnp.float32)
        dense = jnp.dot(pick, runoff, precision=lax.Precision.HIGHEST)
        if not PAIRED or blocks % 2:
            arrived = lax.all_to_all(
                dense.reshape(shards, blocks, width), grid, split_axis=0, concat_axis=0, tiled=True
            )
            return jnp.sum(arrived, axis=0)
        return pair_exchange(dense, blocks, shards)
    buffer, slot_labels = pack_slots(runoff, tile_block, tile_dest, shards, tile_cap)
    arrived = lax.all_to_all(
        buffer.reshape(shards, tile_cap, width), grid, split_axis=0, concat_axis=0, tiled=True
    )
    arrived_ids = lax.all_to_all(
        slot_labels.reshape(shards, tile_cap), grid, split_axis=0, concat_axis=0, tiled=True
    )
    block_pick = (
        arrived_ids.reshape(-1)[:, None] == jnp.arange(blocks, dtype=jnp.int32)[None, :]
    ).astype(jnp.float32)
    return jnp.einsum(
        "sk,sx->kx", block_pick, arrived.reshape(-1, width), precision=lax.Precision.HIGHEST
    )


def pair_exchange(dense, blocks, shards):
    chains = lax.axis_size("basin")
    across = lax.axis_size("x")
    width = dense.shape[1]
    core = lax.axis_index("core")
    parts = dense.reshape(chains, across, 2, blocks, width)
    keep_side = lax.dynamic_index_in_dim(parts, core, axis=2, keepdims=False)
    give_side = lax.dynamic_index_in_dim(parts, 1 - core, axis=2, keepdims=False)
    chip_sum = keep_side + lax.ppermute(give_side, "core", [(0, 1), (1, 0)])
    arrived = lax.all_to_all(
        chip_sum.reshape(chains * across, blocks, width), ("basin", "x"), split_axis=0, concat_axis=0, tiled=True
    )
    return jnp.sum(arrived, axis=0)


def local(
    precip,
    soil_water,
    capacity,
    evap_rate,
    tile_dest,
    tile_block,
    trib_op,
    trib_keep,
    trib_prev,
    trib_river,
    trib_reach,
    main_op,
    main_keep,
    main_prev,
    head_inflow,
):
    tile_count = precip.shape[0]
    sub_steps = precip.shape[1]
    reaches = precip.shape[2]
    blocks = trib_op.shape[0]
    chains = lax.axis_size("basin")
    rivers = lax.axis_size(BAND)
    shards = chains * rivers
    grid = GRID
    operator = main_op[0, 0]
    keep_main = main_keep[0, 0]
    prev_main = main_prev[0, 0]

    runoff, water = land_update(precip, soil_water, capacity, evap_rate)
    lateral = gather_lateral(
        runoff.reshape(tile_count, sub_steps * reaches), tile_dest, tile_block, blocks, shards
    )
    trib_mixed = jnp.einsum(
        "brc,btc->btr",
        trib_op,
        lateral.reshape(blocks, sub_steps, reaches),
        precision=lax.Precision.HIGHEST,
    )
    trib_flows = route_series(trib_mixed, trib_keep, trib_prev)
    exit_mixed = jnp.sum(
        lateral.reshape(blocks, sub_steps, reaches) * trib_op[:, reaches - 1][:, None, :], axis=2
    )
    outlet = route_series(
        exit_mixed[:, :, None], trib_keep[:, reaches - 1 :], trib_prev[:, reaches - 1 :]
    )[:, :, 0]

    mine = lax.axis_index(BAND)
    me = lax.axis_index("basin")
    spread_lanes = reaches // blocks
    if reaches % blocks == 0 and sub_steps + 4 + spread_lanes <= reaches:
        lane = lax.broadcasted_iota(jnp.int32, (blocks, reaches), 1)
        columns = (
            trib_river.astype(jnp.float32)[:, None],
            trib_reach.astype(jnp.float32)[:, None],
            keep_main[reaches - 1 :][None, :],
            prev_main[reaches - 1 :][None, :],
        )
        spread_row = operator[reaches - 1].reshape(blocks, spread_lanes)
        static_tile = jnp.pad(
            spread_row, ((0, 0), (sub_steps + 4, reaches - sub_steps - 4 - spread_lanes))
        )
        for offset, value in enumerate(columns):
            static_tile = static_tile + jnp.where(lane == sub_steps + offset, value, 0.0)
        static_tile = lax.optimization_barrier(static_tile)
        tile = jnp.pad(outlet, ((0, 0), (0, reaches - sub_steps))) + static_tile
        every = lax.all_to_all(
            jnp.broadcast_to(tile[None], (shards,) + tile.shape), grid, split_axis=0, concat_axis=0, tiled=True
        )
        outlets = every[:, :, :sub_steps].reshape(chains, rivers * blocks, sub_steps)
        river_of = every[:, :, sub_steps].reshape(chains, rivers * blocks)
        reach_of = every[:, :, sub_steps + 1].reshape(chains, rivers * blocks)
        facts = lax.dynamic_index_in_dim(
            every.reshape(chains, rivers, blocks, reaches), mine, axis=1, keepdims=False
        )
        keeps = facts[:, 0, sub_steps + 2]
        starts = facts[:, 0, sub_steps + 3]
        exit_rows = facts[:, :, sub_steps + 4 : sub_steps + 4 + spread_lanes].reshape(chains, reaches)
    else:
        payload = jnp.concatenate(
            [
                outlet.reshape(-1),
                trib_river.astype(jnp.float32),
                trib_reach.astype(jnp.float32),
                operator[reaches - 1],
                keep_main[reaches - 1 :],
                prev_main[reaches - 1 :],
            ]
        )
        width = payload.shape[0]
        padded = -(-width // 128) * 128
        payload = jnp.pad(payload, (0, padded - width))
        every = lax.all_to_all(
            jnp.broadcast_to(payload[None], (shards, padded)), grid, split_axis=0, concat_axis=0, tiled=True
        )
        at = 0
        outlets = every[:, at : at + blocks * sub_steps].reshape(chains, rivers * blocks, sub_steps)
        at += blocks * sub_steps
        river_of = every[:, at : at + blocks].reshape(chains, rivers * blocks)
        at += blocks
        reach_of = every[:, at : at + blocks].reshape(chains, rivers * blocks)
        at += blocks
        exit_rows = lax.dynamic_index_in_dim(
            every[:, at : at + reaches].reshape(chains, rivers, reaches), mine, axis=1, keepdims=False
        )
        at += reaches
        keeps = lax.dynamic_index_in_dim(
            every[:, at].reshape(chains, rivers), mine, axis=1, keepdims=False
        )
        starts = lax.dynamic_index_in_dim(
            every[:, at + 1].reshape(chains, rivers), mine, axis=1, keepdims=False
        )

    joins = (river_of == mine.astype(jnp.float32))[:, :, None] & (
        reach_of[:, :, None] == jnp.arange(reaches, dtype=jnp.float32)[None, None, :]
    )
    weight = joins.astype(jnp.float32)
    branch_all = jnp.sum(weight[:, :, None, :] * outlets[:, :, :, None], axis=1)
    branch_exit = jnp.sum(branch_all * exit_rows[:, None, :], axis=2)

    flow = starts
    free_exit = []
    for sub_step in range(sub_steps):
        flow = keeps * flow + (1.0 - keeps) * branch_exit[:, sub_step]
        free_exit.append(flow)
    free_exit = jnp.stack(free_exit, axis=1)
    lag = jnp.arange(sub_steps)[:, None] - jnp.arange(sub_steps)[None, :]
    lag_f = jnp.maximum(lag, 0).astype(jnp.float32)
    response = jnp.where(
        lag[None] >= 0,
        (exit_rows[:, 0] * (1.0 - keeps))[:, None, None] * keeps[:, None, None] ** lag_f[None],
        0.0,
    )

    def advance(section, entry):
        moved = jnp.sum(response[section] * entry[None, :], axis=1) + free_exit[section]
        return jnp.where(section < me, moved, entry)

    entry = lax.fori_loop(0, chains, advance, head_inflow[0], unroll=chains <= 16)

    branch_in = lax.dynamic_index_in_dim(branch_all, me, axis=0, keepdims=False)
    first_reach = (jnp.arange(reaches) == 0).astype(jnp.float32)
    fed = branch_in + entry[:, None] * first_reach[None, :]
    main_mixed = jnp.einsum("rc,tc->tr", operator, fed, precision=lax.Precision.HIGHEST)
    main_flows = route_series(main_mixed, keep_main, prev_main)
    return (water, trib_flows[:, sub_steps - 1], main_flows[None, None])


def cores_paired(mesh):
    try:
        grid = mesh.devices
        if grid.ndim != 2 or grid.shape[1] % 2:
            return False
        for row in grid:
            for m in range(0, len(row), 2):
                a, b = row[m], row[m + 1]
                if tuple(a.coords) != tuple(b.coords) or a.core_on_chip == b.core_on_chip:
                    return False
        return True
    except AttributeError:
        return False


PAIRED = False
BAND = "band"
GRID = ("basin", "band")


def solution(mesh):
    global PAIRED, BAND, GRID
    PAIRED = cores_paired(mesh)
    if PAIRED:
        grid = mesh.devices
        mesh = Mesh(grid.reshape(grid.shape[0], grid.shape[1] // 2, 2), ("basin", "x", "core"))
        BAND, GRID = ("x", "core"), ("basin", "x", "core")
    else:
        BAND, GRID = "band", ("basin", "band")
    return jax.shard_map(
        local,
        mesh=mesh,
        in_specs=(
            P(GRID, None, None),
            P(GRID, None),
            P(GRID, None),
            P(GRID, None),
            P(GRID),
            P(GRID),
            P(GRID, None, None),
            P(GRID, None),
            P(GRID, None),
            P(GRID),
            P(GRID),
            P(BAND, "basin", None, None),
            P(BAND, "basin", None),
            P(BAND, "basin", None),
            P(BAND, None),
        ),
        out_specs=(
            P(GRID, None),
            P(GRID, None),
            P(BAND, "basin", None, None),
        ),
        check_vma=False,
    )
```

```python
import jax
import jax.numpy as jnp
from jax import lax
from jax.sharding import Mesh, PartitionSpec as P


def land_update(precip, soil_water, capacity, evap_rate):
    water = soil_water
    runoff_steps = []
    for sub_step in range(precip.shape[1]):
        rain_now = precip[:, sub_step]
        runoff_now = rain_now * water / (water + capacity)
        water = (1.0 - evap_rate) * water + rain_now - runoff_now
        runoff_steps.append(runoff_now)
    return (jnp.stack(runoff_steps, axis=1), water)


def land_update_t(precip_t, soil_water, capacity, evap_rate):
    water = soil_water
    runoff_steps = []
    for sub_step in range(precip_t.shape[0]):
        rain_now = precip_t[sub_step]
        runoff_now = rain_now * water / (water + capacity)
        water = (1.0 - evap_rate) * water + rain_now - runoff_now
        runoff_steps.append(runoff_now)
    return (jnp.stack(runoff_steps, axis=0), water)


def route_series(mixed, keep, previous):
    flow = previous
    flows = []
    for sub_step in range(mixed.shape[-2]):
        flow = keep * flow + (1.0 - keep) * mixed[..., sub_step, :]
        flows.append(flow)
    return jnp.stack(flows, axis=-2)


def pack_slots(values, labels, targets, peer_count, slot_cap):
    entries = targets.shape[0]
    position = jnp.arange(entries, dtype=jnp.int32)
    earlier = (targets[:, None] == targets[None, :]) & (position[None, :] < position[:, None])
    ranking = jnp.sum(earlier.astype(jnp.int32), axis=1)
    target_slot = targets * slot_cap + ranking
    buffer = (
        jnp.zeros((peer_count * slot_cap, values.shape[1]), values.dtype)
        .at[target_slot]
        .set(values)
    )
    slot_labels = jnp.zeros((peer_count * slot_cap,), jnp.int32).at[target_slot].set(labels)
    return (buffer, slot_labels)


def gather_lateral(runoff_t, tile_dest, tile_block, blocks, shards):
    sub_steps, tile_count, reaches = runoff_t.shape
    width = sub_steps * reaches
    tile_cap = max(2, 2 * tile_count // shards)
    grid = GRID
    if tile_cap >= blocks:
        block_ids = tile_dest * blocks + tile_block
        pick = (
            block_ids[None, :] == jnp.arange(shards * blocks, dtype=jnp.int32)[:, None]
        ).astype(jnp.float32)
        dense = jnp.einsum(
            "gk,tkc->gtc", pick, runoff_t, precision=lax.Precision.HIGHEST
        ).reshape(shards * blocks, width)
        if not PAIRED or blocks % 2:
            arrived = lax.all_to_all(
                dense.reshape(shards, blocks, width), grid, split_axis=0, concat_axis=0, tiled=True
            )
            return jnp.sum(arrived, axis=0)
        return pair_exchange(dense, blocks, shards)
    runoff = jnp.transpose(runoff_t, (1, 0, 2)).reshape(tile_count, width)
    buffer, slot_labels = pack_slots(runoff, tile_block, tile_dest, shards, tile_cap)
    arrived = lax.all_to_all(
        buffer.reshape(shards, tile_cap, width), grid, split_axis=0, concat_axis=0, tiled=True
    )
    arrived_ids = lax.all_to_all(
        slot_labels.reshape(shards, tile_cap), grid, split_axis=0, concat_axis=0, tiled=True
    )
    block_pick = (
        arrived_ids.reshape(-1)[:, None] == jnp.arange(blocks, dtype=jnp.int32)[None, :]
    ).astype(jnp.float32)
    return jnp.einsum(
        "sk,sx->kx", block_pick, arrived.reshape(-1, width), precision=lax.Precision.HIGHEST
    )


def pair_exchange(dense, blocks, shards):
    chains = lax.axis_size("basin")
    across = lax.axis_size("x")
    width = dense.shape[1]
    core = lax.axis_index("core")
    parts = dense.reshape(chains, across, 2, blocks, width)
    keep_side = lax.dynamic_index_in_dim(parts, core, axis=2, keepdims=False)
    give_side = lax.dynamic_index_in_dim(parts, 1 - core, axis=2, keepdims=False)
    chip_sum = keep_side + lax.ppermute(give_side, "core", [(0, 1), (1, 0)])
    arrived = lax.all_to_all(
        chip_sum.reshape(chains * across, blocks, width), ("basin", "x"), split_axis=0, concat_axis=0, tiled=True
    )
    return jnp.sum(arrived, axis=0)


def local(
    precip,
    soil_water,
    capacity,
    evap_rate,
    tile_dest,
    tile_block,
    trib_op,
    trib_keep,
    trib_prev,
    trib_river,
    trib_reach,
    main_op,
    main_keep,
    main_prev,
    head_inflow,
):
    tile_count = precip.shape[0]
    sub_steps = precip.shape[1]
    reaches = precip.shape[2]
    blocks = trib_op.shape[0]
    chains = lax.axis_size("basin")
    rivers = lax.axis_size(BAND)
    shards = chains * rivers
    grid = GRID
    operator = main_op[0, 0]
    keep_main = main_keep[0, 0]
    prev_main = main_prev[0, 0]

    runoff_t, water = land_update_t(jnp.transpose(precip, (1, 0, 2)), soil_water, capacity, evap_rate)
    lateral = gather_lateral(runoff_t, tile_dest, tile_block, blocks, shards)
    trib_mixed = jnp.einsum(
        "brc,btc->btr",
        trib_op,
        lateral.reshape(blocks, sub_steps, reaches),
        precision=lax.Precision.HIGHEST,
    )
    trib_flows = route_series(trib_mixed, trib_keep, trib_prev)
    exit_mixed = jnp.sum(
        lateral.reshape(blocks, sub_steps, reaches) * trib_op[:, reaches - 1][:, None, :], axis=2
    )
    outlet = route_series(
        exit_mixed[:, :, None], trib_keep[:, reaches - 1 :], trib_prev[:, reaches - 1 :]
    )[:, :, 0]

    mine = lax.axis_index(BAND)
    me = lax.axis_index("basin")
    spread_lanes = reaches // blocks
    if reaches % blocks == 0 and sub_steps + 4 + spread_lanes <= reaches:
        lane = lax.broadcasted_iota(jnp.int32, (blocks, reaches), 1)
        columns = (
            trib_river.astype(jnp.float32)[:, None],
            trib_reach.astype(jnp.float32)[:, None],
            keep_main[reaches - 1 :][None, :],
            prev_main[reaches - 1 :][None, :],
        )
        spread_row = operator[reaches - 1].reshape(blocks, spread_lanes)
        static_tile = jnp.pad(
            spread_row, ((0, 0), (sub_steps + 4, reaches - sub_steps - 4 - spread_lanes))
        )
        for offset, value in enumerate(columns):
            static_tile = static_tile + jnp.where(lane == sub_steps + offset, value, 0.0)
        static_tile = lax.optimization_barrier(static_tile)
        tile = jnp.pad(outlet, ((0, 0), (0, reaches - sub_steps))) + static_tile
        every = lax.all_to_all(
            jnp.broadcast_to(tile[None], (shards,) + tile.shape), grid, split_axis=0, concat_axis=0, tiled=True
        )
        outlets = every[:, :, :sub_steps].reshape(chains, rivers * blocks, sub_steps)
        river_of = every[:, :, sub_steps].reshape(chains, rivers * blocks)
        reach_of = every[:, :, sub_steps + 1].reshape(chains, rivers * blocks)
        facts = lax.dynamic_index_in_dim(
            every.reshape(chains, rivers, blocks, reaches), mine, axis=1, keepdims=False
        )
        keeps = facts[:, 0, sub_steps + 2]
        starts = facts[:, 0, sub_steps + 3]
        exit_rows = facts[:, :, sub_steps + 4 : sub_steps + 4 + spread_lanes].reshape(chains, reaches)
    else:
        payload = jnp.concatenate(
            [
                outlet.reshape(-1),
                trib_river.astype(jnp.float32),
                trib_reach.astype(jnp.float32),
                operator[reaches - 1],
                keep_main[reaches - 1 :],
                prev_main[reaches - 1 :],
            ]
        )
        width = payload.shape[0]
        padded = -(-width // 128) * 128
        payload = jnp.pad(payload, (0, padded - width))
        every = lax.all_to_all(
            jnp.broadcast_to(payload[None], (shards, padded)), grid, split_axis=0, concat_axis=0, tiled=True
        )
        at = 0
        outlets = every[:, at : at + blocks * sub_steps].reshape(chains, rivers * blocks, sub_steps)
        at += blocks * sub_steps
        river_of = every[:, at : at + blocks].reshape(chains, rivers * blocks)
        at += blocks
        reach_of = every[:, at : at + blocks].reshape(chains, rivers * blocks)
        at += blocks
        exit_rows = lax.dynamic_index_in_dim(
            every[:, at : at + reaches].reshape(chains, rivers, reaches), mine, axis=1, keepdims=False
        )
        at += reaches
        keeps = lax.dynamic_index_in_dim(
            every[:, at].reshape(chains, rivers), mine, axis=1, keepdims=False
        )
        starts = lax.dynamic_index_in_dim(
            every[:, at + 1].reshape(chains, rivers), mine, axis=1, keepdims=False
        )

    joins = (river_of == mine.astype(jnp.float32))[:, :, None] & (
        reach_of[:, :, None] == jnp.arange(reaches, dtype=jnp.float32)[None, None, :]
    )
    weight = joins.astype(jnp.float32)
    branch_all = jnp.sum(weight[:, :, None, :] * outlets[:, :, :, None], axis=1)
    branch_exit = jnp.sum(branch_all * exit_rows[:, None, :], axis=2)

    flow = starts
    free_exit = []
    for sub_step in range(sub_steps):
        flow = keeps * flow + (1.0 - keeps) * branch_exit[:, sub_step]
        free_exit.append(flow)
    free_exit = jnp.stack(free_exit, axis=1)
    lag = jnp.arange(sub_steps)[:, None] - jnp.arange(sub_steps)[None, :]
    lag_f = jnp.maximum(lag, 0).astype(jnp.float32)
    response = jnp.where(
        lag[None] >= 0,
        (exit_rows[:, 0] * (1.0 - keeps))[:, None, None] * keeps[:, None, None] ** lag_f[None],
        0.0,
    )

    def advance(section, entry):
        moved = jnp.sum(response[section] * entry[None, :], axis=1) + free_exit[section]
        return jnp.where(section < me, moved, entry)

    entry = lax.fori_loop(0, chains, advance, head_inflow[0], unroll=chains <= 16)

    branch_in = lax.dynamic_index_in_dim(branch_all, me, axis=0, keepdims=False)
    first_reach = (jnp.arange(reaches) == 0).astype(jnp.float32)
    fed = branch_in + entry[:, None] * first_reach[None, :]
    main_mixed = jnp.einsum("rc,tc->tr", operator, fed, precision=lax.Precision.HIGHEST)
    main_flows = route_series(main_mixed, keep_main, prev_main)
    return (water, trib_flows[:, sub_steps - 1], main_flows[None, None])


def cores_paired(mesh):
    try:
        grid = mesh.devices
        if grid.ndim != 2 or grid.shape[1] % 2:
            return False
        for row in grid:
            for m in range(0, len(row), 2):
                a, b = row[m], row[m + 1]
                if tuple(a.coords) != tuple(b.coords) or a.core_on_chip == b.core_on_chip:
                    return False
        return True
    except AttributeError:
        return False


PAIRED = False
BAND = "band"
GRID = ("basin", "band")


def solution(mesh):
    global PAIRED, BAND, GRID
    PAIRED = cores_paired(mesh)
    if PAIRED:
        grid = mesh.devices
        mesh = Mesh(grid.reshape(grid.shape[0], grid.shape[1] // 2, 2), ("basin", "x", "core"))
        BAND, GRID = ("x", "core"), ("basin", "x", "core")
    else:
        BAND, GRID = "band", ("basin", "band")
    return jax.shard_map(
        local,
        mesh=mesh,
        in_specs=(
            P(GRID, None, None),
            P(GRID, None),
            P(GRID, None),
            P(GRID, None),
            P(GRID),
            P(GRID),
            P(GRID, None, None),
            P(GRID, None),
            P(GRID, None),
            P(GRID),
            P(GRID),
            P(BAND, "basin", None, None),
            P(BAND, "basin", None),
            P(BAND, "basin", None),
            P(BAND, None),
        ),
        out_specs=(
            P(GRID, None),
            P(GRID, None),
            P(BAND, "basin", None, None),
        ),
        check_vma=False,
    )
```

```python
import jax
import jax.numpy as jnp
from jax import lax
from jax.sharding import Mesh, PartitionSpec as P


def land_update(precip, soil_water, capacity, evap_rate):
    water = soil_water
    runoff_steps = []
    for sub_step in range(precip.shape[1]):
        rain_now = precip[:, sub_step]
        runoff_now = rain_now * water / (water + capacity)
        water = (1.0 - evap_rate) * water + rain_now - runoff_now
        runoff_steps.append(runoff_now)
    return (jnp.stack(runoff_steps, axis=1), water)


def land_update_t(precip_t, soil_water, capacity, evap_rate):
    water = soil_water
    runoff_steps = []
    for sub_step in range(precip_t.shape[0]):
        rain_now = precip_t[sub_step]
        runoff_now = rain_now * water / (water + capacity)
        water = (1.0 - evap_rate) * water + rain_now - runoff_now
        runoff_steps.append(runoff_now)
    return (jnp.stack(runoff_steps, axis=0), water)


def route_series(mixed, keep, previous):
    flow = previous
    flows = []
    for sub_step in range(mixed.shape[-2]):
        flow = keep * flow + (1.0 - keep) * mixed[..., sub_step, :]
        flows.append(flow)
    return jnp.stack(flows, axis=-2)


def pack_slots(values, labels, targets, peer_count, slot_cap):
    entries = targets.shape[0]
    position = jnp.arange(entries, dtype=jnp.int32)
    earlier = (targets[:, None] == targets[None, :]) & (position[None, :] < position[:, None])
    ranking = jnp.sum(earlier.astype(jnp.int32), axis=1)
    target_slot = targets * slot_cap + ranking
    buffer = (
        jnp.zeros((peer_count * slot_cap, values.shape[1]), values.dtype)
        .at[target_slot]
        .set(values)
    )
    slot_labels = jnp.zeros((peer_count * slot_cap,), jnp.int32).at[target_slot].set(labels)
    return (buffer, slot_labels)


def gather_lateral(runoff_t, tile_dest, tile_block, blocks, shards):
    sub_steps, tile_count, reaches = runoff_t.shape
    width = sub_steps * reaches
    tile_cap = max(2, 2 * tile_count // shards)
    grid = GRID
    if tile_cap >= blocks:
        block_ids = tile_dest * blocks + tile_block
        pick = (
            block_ids[None, :] == jnp.arange(shards * blocks, dtype=jnp.int32)[:, None]
        ).astype(jnp.float32)
        dense = jnp.einsum(
            "gk,tkc->gtc", pick, runoff_t, precision=lax.Precision.HIGHEST
        ).reshape(shards * blocks, width)
        if not PAIRED or blocks % 2:
            arrived = lax.all_to_all(
                dense.reshape(shards, blocks, width), grid, split_axis=0, concat_axis=0, tiled=True
            )
            return jnp.sum(arrived, axis=0)
        return pair_exchange(dense, blocks, shards)
    runoff = jnp.transpose(runoff_t, (1, 0, 2)).reshape(tile_count, width)
    buffer, slot_labels = pack_slots(runoff, tile_block, tile_dest, shards, tile_cap)
    arrived = lax.all_to_all(
        buffer.reshape(shards, tile_cap, width), grid, split_axis=0, concat_axis=0, tiled=True
    )
    arrived_ids = lax.all_to_all(
        slot_labels.reshape(shards, tile_cap), grid, split_axis=0, concat_axis=0, tiled=True
    )
    block_pick = (
        arrived_ids.reshape(-1)[:, None] == jnp.arange(blocks, dtype=jnp.int32)[None, :]
    ).astype(jnp.float32)
    return jnp.einsum(
        "sk,sx->kx", block_pick, arrived.reshape(-1, width), precision=lax.Precision.HIGHEST
    )


def pair_exchange(dense, blocks, shards):
    chains = lax.axis_size("basin")
    across = lax.axis_size("x")
    width = dense.shape[1]
    core = lax.axis_index("core")
    parts = dense.reshape(chains, across, 2, blocks, width)
    keep_side = lax.dynamic_index_in_dim(parts, core, axis=2, keepdims=False)
    give_side = lax.dynamic_index_in_dim(parts, 1 - core, axis=2, keepdims=False)
    chip_sum = keep_side + lax.ppermute(give_side, "core", [(0, 1), (1, 0)])
    arrived = lax.all_to_all(
        chip_sum.reshape(chains * across, blocks, width), ("basin", "x"), split_axis=0, concat_axis=0, tiled=True
    )
    return jnp.sum(arrived, axis=0)


def local(
    precip,
    soil_water,
    capacity,
    evap_rate,
    tile_dest,
    tile_block,
    trib_op,
    trib_keep,
    trib_prev,
    trib_river,
    trib_reach,
    main_op,
    main_keep,
    main_prev,
    head_inflow,
):
    tile_count = precip.shape[0]
    sub_steps = precip.shape[1]
    reaches = precip.shape[2]
    blocks = trib_op.shape[0]
    chains = lax.axis_size("basin")
    rivers = lax.axis_size(BAND)
    shards = chains * rivers
    grid = GRID
    operator = main_op[0, 0]
    keep_main = main_keep[0, 0]
    prev_main = main_prev[0, 0]

    runoff_t, water = land_update_t(jnp.transpose(precip, (1, 0, 2)), soil_water, capacity, evap_rate)
    lateral = gather_lateral(runoff_t, tile_dest, tile_block, blocks, shards)
    trib_mixed = jnp.einsum(
        "brc,btc->btr",
        trib_op,
        lateral.reshape(blocks, sub_steps, reaches),
        precision=lax.Precision.HIGHEST,
    )
    trib_flows = route_series(trib_mixed, trib_keep, trib_prev)
    exit_mixed = jnp.sum(
        lateral.reshape(blocks, sub_steps, reaches) * trib_op[:, reaches - 1][:, None, :], axis=2
    )
    outlet = route_series(
        exit_mixed[:, :, None], trib_keep[:, reaches - 1 :], trib_prev[:, reaches - 1 :]
    )[:, :, 0]

    mine = lax.axis_index(BAND)
    me = lax.axis_index("basin")
    spread_lanes = reaches // blocks
    if reaches % blocks == 0 and sub_steps + 4 + spread_lanes <= reaches:
        lane = lax.broadcasted_iota(jnp.int32, (blocks, reaches), 1)
        columns = (
            trib_river.astype(jnp.float32)[:, None],
            trib_reach.astype(jnp.float32)[:, None],
            keep_main[reaches - 1 :][None, :],
            prev_main[reaches - 1 :][None, :],
        )
        spread_row = operator[reaches - 1].reshape(blocks, spread_lanes)
        static_tile = jnp.pad(
            spread_row, ((0, 0), (sub_steps + 4, reaches - sub_steps - 4 - spread_lanes))
        )
        for offset, value in enumerate(columns):
            static_tile = static_tile + jnp.where(lane == sub_steps + offset, value, 0.0)
        tile = jnp.pad(outlet, ((0, 0), (0, reaches - sub_steps))) + static_tile
        every = lax.all_to_all(
            jnp.broadcast_to(tile[None], (shards,) + tile.shape), grid, split_axis=0, concat_axis=0, tiled=True
        )
        outlets = every[:, :, :sub_steps].reshape(chains, rivers * blocks, sub_steps)
        river_of = every[:, :, sub_steps].reshape(chains, rivers * blocks)
        reach_of = every[:, :, sub_steps + 1].reshape(chains, rivers * blocks)
        facts = lax.dynamic_index_in_dim(
            every.reshape(chains, rivers, blocks, reaches), mine, axis=1, keepdims=False
        )
        keeps = facts[:, 0, sub_steps + 2]
        starts = facts[:, 0, sub_steps + 3]
        exit_rows = facts[:, :, sub_steps + 4 : sub_steps + 4 + spread_lanes].reshape(chains, reaches)
    else:
        payload = jnp.concatenate(
            [
                outlet.reshape(-1),
                trib_river.astype(jnp.float32),
                trib_reach.astype(jnp.float32),
                operator[reaches - 1],
                keep_main[reaches - 1 :],
                prev_main[reaches - 1 :],
            ]
        )
        width = payload.shape[0]
        padded = -(-width // 128) * 128
        payload = jnp.pad(payload, (0, padded - width))
        every = lax.all_to_all(
            jnp.broadcast_to(payload[None], (shards, padded)), grid, split_axis=0, concat_axis=0, tiled=True
        )
        at = 0
        outlets = every[:, at : at + blocks * sub_steps].reshape(chains, rivers * blocks, sub_steps)
        at += blocks * sub_steps
        river_of = every[:, at : at + blocks].reshape(chains, rivers * blocks)
        at += blocks
        reach_of = every[:, at : at + blocks].reshape(chains, rivers * blocks)
        at += blocks
        exit_rows = lax.dynamic_index_in_dim(
            every[:, at : at + reaches].reshape(chains, rivers, reaches), mine, axis=1, keepdims=False
        )
        at += reaches
        keeps = lax.dynamic_index_in_dim(
            every[:, at].reshape(chains, rivers), mine, axis=1, keepdims=False
        )
        starts = lax.dynamic_index_in_dim(
            every[:, at + 1].reshape(chains, rivers), mine, axis=1, keepdims=False
        )

    joins = (river_of == mine.astype(jnp.float32))[:, :, None] & (
        reach_of[:, :, None] == jnp.arange(reaches, dtype=jnp.float32)[None, None, :]
    )
    weight = joins.astype(jnp.float32)
    branch_all = jnp.sum(weight[:, :, None, :] * outlets[:, :, :, None], axis=1)
    branch_exit = jnp.sum(branch_all * exit_rows[:, None, :], axis=2)

    flow = starts
    free_exit = []
    for sub_step in range(sub_steps):
        flow = keeps * flow + (1.0 - keeps) * branch_exit[:, sub_step]
        free_exit.append(flow)
    free_exit = jnp.stack(free_exit, axis=1)
    lag = jnp.arange(sub_steps)[:, None] - jnp.arange(sub_steps)[None, :]
    lag_f = jnp.maximum(lag, 0).astype(jnp.float32)
    response = jnp.where(
        lag[None] >= 0,
        (exit_rows[:, 0] * (1.0 - keeps))[:, None, None] * keeps[:, None, None] ** lag_f[None],
        0.0,
    )

    def advance(section, entry):
        moved = jnp.sum(response[section] * entry[None, :], axis=1) + free_exit[section]
        return jnp.where(section < me, moved, entry)

    entry = lax.fori_loop(0, chains, advance, head_inflow[0], unroll=chains <= 16)

    branch_in = lax.dynamic_index_in_dim(branch_all, me, axis=0, keepdims=False)
    first_reach = (jnp.arange(reaches) == 0).astype(jnp.float32)
    fed = branch_in + entry[:, None] * first_reach[None, :]
    main_mixed = jnp.einsum("rc,tc->tr", operator, fed, precision=lax.Precision.HIGHEST)
    main_flows = route_series(main_mixed, keep_main, prev_main)
    return (water, trib_flows[:, sub_steps - 1], main_flows[None, None])


def cores_paired(mesh):
    try:
        grid = mesh.devices
        if grid.ndim != 2 or grid.shape[1] % 2:
            return False
        for row in grid:
            for m in range(0, len(row), 2):
                a, b = row[m], row[m + 1]
                if tuple(a.coords) != tuple(b.coords) or a.core_on_chip == b.core_on_chip:
                    return False
        return True
    except AttributeError:
        return False


PAIRED = False
BAND = "band"
GRID = ("basin", "band")


def solution(mesh):
    global PAIRED, BAND, GRID
    PAIRED = cores_paired(mesh)
    if PAIRED:
        grid = mesh.devices
        mesh = Mesh(grid.reshape(grid.shape[0], grid.shape[1] // 2, 2), ("basin", "x", "core"))
        BAND, GRID = ("x", "core"), ("basin", "x", "core")
    else:
        BAND, GRID = "band", ("basin", "band")
    return jax.shard_map(
        local,
        mesh=mesh,
        in_specs=(
            P(GRID, None, None),
            P(GRID, None),
            P(GRID, None),
            P(GRID, None),
            P(GRID),
            P(GRID),
            P(GRID, None, None),
            P(GRID, None),
            P(GRID, None),
            P(GRID),
            P(GRID),
            P(BAND, "basin", None, None),
            P(BAND, "basin", None),
            P(BAND, "basin", None),
            P(BAND, None),
        ),
        out_specs=(
            P(GRID, None),
            P(GRID, None),
            P(BAND, "basin", None, None),
        ),
        check_vma=False,
    )
```

```python
import functools

import jax
import jax.numpy as jnp
from jax import lax
from jax.experimental import pallas as pl
from jax.experimental.pallas import tpu as pltpu
from jax.sharding import Mesh, PartitionSpec as P


def land_update(precip, soil_water, capacity, evap_rate):
    water = soil_water
    runoff_steps = []
    for sub_step in range(precip.shape[1]):
        rain_now = precip[:, sub_step]
        runoff_now = rain_now * water / (water + capacity)
        water = (1.0 - evap_rate) * water + rain_now - runoff_now
        runoff_steps.append(runoff_now)
    return (jnp.stack(runoff_steps, axis=1), water)


def land_update_t(precip_t, soil_water, capacity, evap_rate):
    water = soil_water
    runoff_steps = []
    for sub_step in range(precip_t.shape[0]):
        rain_now = precip_t[sub_step]
        runoff_now = rain_now * water / (water + capacity)
        water = (1.0 - evap_rate) * water + rain_now - runoff_now
        runoff_steps.append(runoff_now)
    return (jnp.stack(runoff_steps, axis=0), water)


def land_kernel(sub_steps, rain_ref, soil_ref, capacity_ref, evap_ref, runoff_ref, water_ref):
    tiles = soil_ref.shape[0]
    water = soil_ref[...]
    capacity = capacity_ref[...]
    evap_rate = evap_ref[...]
    for sub_step in range(sub_steps):
        rain_now = rain_ref[pl.ds(sub_step, tiles, stride=sub_steps), :]
        runoff_now = rain_now * water / (water + capacity)
        water = (1.0 - evap_rate) * water + rain_now - runoff_now
        runoff_ref[sub_step] = runoff_now
    water_ref[...] = water


def land_update_kernel(precip, soil_water, capacity, evap_rate):
    tiles, sub_steps, reaches = precip.shape
    vmem = pl.BlockSpec(memory_space=pltpu.VMEM)
    return pl.pallas_call(
        functools.partial(land_kernel, sub_steps),
        out_shape=(
            jax.ShapeDtypeStruct((sub_steps, tiles, reaches), precip.dtype),
            jax.ShapeDtypeStruct((tiles, reaches), precip.dtype),
        ),
        in_specs=[vmem] * 4,
        out_specs=(vmem, vmem),
        cost_estimate=pl.CostEstimate(
            flops=10 * precip.size, transcendentals=0, bytes_accessed=4 * (2 * precip.size + 4 * soil_water.size)
        ),
    )(precip.reshape(tiles * sub_steps, reaches), soil_water, capacity, evap_rate)


def route_series(mixed, keep, previous):
    flow = previous
    flows = []
    for sub_step in range(mixed.shape[-2]):
        flow = keep * flow + (1.0 - keep) * mixed[..., sub_step, :]
        flows.append(flow)
    return jnp.stack(flows, axis=-2)


def pack_slots(values, labels, targets, peer_count, slot_cap):
    entries = targets.shape[0]
    position = jnp.arange(entries, dtype=jnp.int32)
    earlier = (targets[:, None] == targets[None, :]) & (position[None, :] < position[:, None])
    ranking = jnp.sum(earlier.astype(jnp.int32), axis=1)
    target_slot = targets * slot_cap + ranking
    buffer = (
        jnp.zeros((peer_count * slot_cap, values.shape[1]), values.dtype)
        .at[target_slot]
        .set(values)
    )
    slot_labels = jnp.zeros((peer_count * slot_cap,), jnp.int32).at[target_slot].set(labels)
    return (buffer, slot_labels)


def gather_lateral(runoff_t, tile_dest, tile_block, blocks, shards):
    sub_steps, tile_count, reaches = runoff_t.shape
    width = sub_steps * reaches
    tile_cap = max(2, 2 * tile_count // shards)
    grid = GRID
    if tile_cap >= blocks:
        block_ids = tile_dest * blocks + tile_block
        pick = (
            block_ids[None, :] == jnp.arange(shards * blocks, dtype=jnp.int32)[:, None]
        ).astype(jnp.float32)
        dense = jnp.einsum(
            "gk,tkc->gtc", pick, runoff_t, precision=lax.Precision.HIGHEST
        ).reshape(shards * blocks, width)
        if not PAIRED or blocks % 2:
            arrived = lax.all_to_all(
                dense.reshape(shards, blocks, width), grid, split_axis=0, concat_axis=0, tiled=True
            )
            return jnp.sum(arrived, axis=0)
        return pair_exchange(dense, blocks, shards)
    runoff = jnp.transpose(runoff_t, (1, 0, 2)).reshape(tile_count, width)
    buffer, slot_labels = pack_slots(runoff, tile_block, tile_dest, shards, tile_cap)
    arrived = lax.all_to_all(
        buffer.reshape(shards, tile_cap, width), grid, split_axis=0, concat_axis=0, tiled=True
    )
    arrived_ids = lax.all_to_all(
        slot_labels.reshape(shards, tile_cap), grid, split_axis=0, concat_axis=0, tiled=True
    )
    block_pick = (
        arrived_ids.reshape(-1)[:, None] == jnp.arange(blocks, dtype=jnp.int32)[None, :]
    ).astype(jnp.float32)
    return jnp.einsum(
        "sk,sx->kx", block_pick, arrived.reshape(-1, width), precision=lax.Precision.HIGHEST
    )


def pair_exchange(dense, blocks, shards):
    chains = lax.axis_size("basin")
    across = lax.axis_size("x")
    width = dense.shape[1]
    core = lax.axis_index("core")
    parts = dense.reshape(chains, across, 2, blocks, width)
    keep_side = lax.dynamic_index_in_dim(parts, core, axis=2, keepdims=False)
    give_side = lax.dynamic_index_in_dim(parts, 1 - core, axis=2, keepdims=False)
    chip_sum = keep_side + lax.ppermute(give_side, "core", [(0, 1), (1, 0)])
    arrived = lax.all_to_all(
        chip_sum.reshape(chains * across, blocks, width), ("basin", "x"), split_axis=0, concat_axis=0, tiled=True
    )
    return jnp.sum(arrived, axis=0)


def local(
    precip,
    soil_water,
    capacity,
    evap_rate,
    tile_dest,
    tile_block,
    trib_op,
    trib_keep,
    trib_prev,
    trib_river,
    trib_reach,
    main_op,
    main_keep,
    main_prev,
    head_inflow,
):
    tile_count = precip.shape[0]
    sub_steps = precip.shape[1]
    reaches = precip.shape[2]
    blocks = trib_op.shape[0]
    chains = lax.axis_size("basin")
    rivers = lax.axis_size(BAND)
    shards = chains * rivers
    grid = GRID
    operator = main_op[0, 0]
    keep_main = main_keep[0, 0]
    prev_main = main_prev[0, 0]

    runoff_t, water = land_update_kernel(precip, soil_water, capacity, evap_rate)
    lateral = gather_lateral(runoff_t, tile_dest, tile_block, blocks, shards)
    trib_mixed = jnp.einsum(
        "brc,btc->btr",
        trib_op,
        lateral.reshape(blocks, sub_steps, reaches),
        precision=lax.Precision.HIGHEST,
    )
    trib_flows = route_series(trib_mixed, trib_keep, trib_prev)
    exit_mixed = jnp.sum(
        lateral.reshape(blocks, sub_steps, reaches) * trib_op[:, reaches - 1][:, None, :], axis=2
    )
    outlet = route_series(
        exit_mixed[:, :, None], trib_keep[:, reaches - 1 :], trib_prev[:, reaches - 1 :]
    )[:, :, 0]

    mine = lax.axis_index(BAND)
    me = lax.axis_index("basin")
    spread_lanes = reaches // blocks
    if reaches % blocks == 0 and sub_steps + 4 + spread_lanes <= reaches:
        lane = lax.broadcasted_iota(jnp.int32, (blocks, reaches), 1)
        columns = (
            trib_river.astype(jnp.float32)[:, None],
            trib_reach.astype(jnp.float32)[:, None],
            keep_main[reaches - 1 :][None, :],
            prev_main[reaches - 1 :][None, :],
        )
        spread_row = operator[reaches - 1].reshape(blocks, spread_lanes)
        static_tile = jnp.pad(
            spread_row, ((0, 0), (sub_steps + 4, reaches - sub_steps - 4 - spread_lanes))
        )
        for offset, value in enumerate(columns):
            static_tile = static_tile + jnp.where(lane == sub_steps + offset, value, 0.0)
        tile = jnp.pad(outlet, ((0, 0), (0, reaches - sub_steps))) + static_tile
        every = lax.all_to_all(
            jnp.broadcast_to(tile[None], (shards,) + tile.shape), grid, split_axis=0, concat_axis=0, tiled=True
        )
        outlets = every[:, :, :sub_steps].reshape(chains, rivers * blocks, sub_steps)
        river_of = every[:, :, sub_steps].reshape(chains, rivers * blocks)
        reach_of = every[:, :, sub_steps + 1].reshape(chains, rivers * blocks)
        facts = lax.dynamic_index_in_dim(
            every.reshape(chains, rivers, blocks, reaches), mine, axis=1, keepdims=False
        )
        keeps = facts[:, 0, sub_steps + 2]
        starts = facts[:, 0, sub_steps + 3]
        exit_rows = facts[:, :, sub_steps + 4 : sub_steps + 4 + spread_lanes].reshape(chains, reaches)
    else:
        payload = jnp.concatenate(
            [
                outlet.reshape(-1),
                trib_river.astype(jnp.float32),
                trib_reach.astype(jnp.float32),
                operator[reaches - 1],
                keep_main[reaches - 1 :],
                prev_main[reaches - 1 :],
            ]
        )
        width = payload.shape[0]
        padded = -(-width // 128) * 128
        payload = jnp.pad(payload, (0, padded - width))
        every = lax.all_to_all(
            jnp.broadcast_to(payload[None], (shards, padded)), grid, split_axis=0, concat_axis=0, tiled=True
        )
        at = 0
        outlets = every[:, at : at + blocks * sub_steps].reshape(chains, rivers * blocks, sub_steps)
        at += blocks * sub_steps
        river_of = every[:, at : at + blocks].reshape(chains, rivers * blocks)
        at += blocks
        reach_of = every[:, at : at + blocks].reshape(chains, rivers * blocks)
        at += blocks
        exit_rows = lax.dynamic_index_in_dim(
            every[:, at : at + reaches].reshape(chains, rivers, reaches), mine, axis=1, keepdims=False
        )
        at += reaches
        keeps = lax.dynamic_index_in_dim(
            every[:, at].reshape(chains, rivers), mine, axis=1, keepdims=False
        )
        starts = lax.dynamic_index_in_dim(
            every[:, at + 1].reshape(chains, rivers), mine, axis=1, keepdims=False
        )

    joins = (river_of == mine.astype(jnp.float32))[:, :, None] & (
        reach_of[:, :, None] == jnp.arange(reaches, dtype=jnp.float32)[None, None, :]
    )
    weight = joins.astype(jnp.float32)
    branch_all = jnp.sum(weight[:, :, None, :] * outlets[:, :, :, None], axis=1)
    branch_exit = jnp.sum(branch_all * exit_rows[:, None, :], axis=2)

    flow = starts
    free_exit = []
    for sub_step in range(sub_steps):
        flow = keeps * flow + (1.0 - keeps) * branch_exit[:, sub_step]
        free_exit.append(flow)
    free_exit = jnp.stack(free_exit, axis=1)
    lag = jnp.arange(sub_steps)[:, None] - jnp.arange(sub_steps)[None, :]
    lag_f = jnp.maximum(lag, 0).astype(jnp.float32)
    response = jnp.where(
        lag[None] >= 0,
        (exit_rows[:, 0] * (1.0 - keeps))[:, None, None] * keeps[:, None, None] ** lag_f[None],
        0.0,
    )

    def advance(section, entry):
        moved = jnp.sum(response[section] * entry[None, :], axis=1) + free_exit[section]
        return jnp.where(section < me, moved, entry)

    entry = lax.fori_loop(0, chains, advance, head_inflow[0], unroll=chains <= 16)

    branch_in = lax.dynamic_index_in_dim(branch_all, me, axis=0, keepdims=False)
    first_reach = (jnp.arange(reaches) == 0).astype(jnp.float32)
    fed = branch_in + entry[:, None] * first_reach[None, :]
    main_mixed = jnp.einsum("rc,tc->tr", operator, fed, precision=lax.Precision.HIGHEST)
    main_flows = route_series(main_mixed, keep_main, prev_main)
    return (water, trib_flows[:, sub_steps - 1], main_flows[None, None])


def cores_paired(mesh):
    try:
        grid = mesh.devices
        if grid.ndim != 2 or grid.shape[1] % 2:
            return False
        for row in grid:
            for m in range(0, len(row), 2):
                a, b = row[m], row[m + 1]
                if tuple(a.coords) != tuple(b.coords) or a.core_on_chip == b.core_on_chip:
                    return False
        return True
    except AttributeError:
        return False


PAIRED = False
BAND = "band"
GRID = ("basin", "band")


def solution(mesh):
    global PAIRED, BAND, GRID
    PAIRED = cores_paired(mesh)
    if PAIRED:
        grid = mesh.devices
        mesh = Mesh(grid.reshape(grid.shape[0], grid.shape[1] // 2, 2), ("basin", "x", "core"))
        BAND, GRID = ("x", "core"), ("basin", "x", "core")
    else:
        BAND, GRID = "band", ("basin", "band")
    return jax.shard_map(
        local,
        mesh=mesh,
        in_specs=(
            P(GRID, None, None),
            P(GRID, None),
            P(GRID, None),
            P(GRID, None),
            P(GRID),
            P(GRID),
            P(GRID, None, None),
            P(GRID, None),
            P(GRID, None),
            P(GRID),
            P(GRID),
            P(BAND, "basin", None, None),
            P(BAND, "basin", None),
            P(BAND, "basin", None),
            P(BAND, None),
        ),
        out_specs=(
            P(GRID, None),
            P(GRID, None),
            P(BAND, "basin", None, None),
        ),
        check_vma=False,
    )
```

```python
import jax
import jax.numpy as jnp
from jax import lax
from jax.sharding import Mesh, PartitionSpec as P


def land_update(precip, soil_water, capacity, evap_rate):
    water = soil_water
    runoff_steps = []
    for sub_step in range(precip.shape[1]):
        rain_now = precip[:, sub_step]
        runoff_now = rain_now * water / (water + capacity)
        water = (1.0 - evap_rate) * water + rain_now - runoff_now
        runoff_steps.append(runoff_now)
    return (jnp.stack(runoff_steps, axis=1), water)


def land_update_t(precip_t, soil_water, capacity, evap_rate):
    water = soil_water
    runoff_steps = []
    for sub_step in range(precip_t.shape[0]):
        rain_now = precip_t[sub_step]
        runoff_now = rain_now * water / (water + capacity)
        water = (1.0 - evap_rate) * water + rain_now - runoff_now
        runoff_steps.append(runoff_now)
    return (jnp.stack(runoff_steps, axis=0), water)


def route_series(mixed, keep, previous):
    flow = previous
    flows = []
    for sub_step in range(mixed.shape[-2]):
        flow = keep * flow + (1.0 - keep) * mixed[..., sub_step, :]
        flows.append(flow)
    return jnp.stack(flows, axis=-2)


def pack_slots(values, labels, targets, peer_count, slot_cap):
    entries = targets.shape[0]
    position = jnp.arange(entries, dtype=jnp.int32)
    earlier = (targets[:, None] == targets[None, :]) & (position[None, :] < position[:, None])
    ranking = jnp.sum(earlier.astype(jnp.int32), axis=1)
    target_slot = targets * slot_cap + ranking
    buffer = (
        jnp.zeros((peer_count * slot_cap, values.shape[1]), values.dtype)
        .at[target_slot]
        .set(values)
    )
    slot_labels = jnp.zeros((peer_count * slot_cap,), jnp.int32).at[target_slot].set(labels)
    return (buffer, slot_labels)


def gather_lateral(runoff_t, tile_dest, tile_block, blocks, shards):
    sub_steps, tile_count, reaches = runoff_t.shape
    width = sub_steps * reaches
    tile_cap = max(2, 2 * tile_count // shards)
    grid = GRID
    if tile_cap >= blocks:
        block_ids = tile_dest * blocks + tile_block
        pick = (
            block_ids[None, :] == jnp.arange(shards * blocks, dtype=jnp.int32)[:, None]
        ).astype(jnp.float32)
        if PAIRED:
            return pair_exchange(runoff_t, block_ids, blocks, shards)
        dense = jnp.einsum(
            "gk,tkc->gtc", pick, runoff_t, precision=lax.Precision.HIGHEST
        ).reshape(shards * blocks, width)
        if not PAIRED or blocks % 2:
            arrived = lax.all_to_all(
                dense.reshape(shards, blocks, width), grid, split_axis=0, concat_axis=0, tiled=True
            )
            return jnp.sum(arrived, axis=0)
        return pair_exchange(dense, blocks, shards)
    runoff = jnp.transpose(runoff_t, (1, 0, 2)).reshape(tile_count, width)
    buffer, slot_labels = pack_slots(runoff, tile_block, tile_dest, shards, tile_cap)
    arrived = lax.all_to_all(
        buffer.reshape(shards, tile_cap, width), grid, split_axis=0, concat_axis=0, tiled=True
    )
    arrived_ids = lax.all_to_all(
        slot_labels.reshape(shards, tile_cap), grid, split_axis=0, concat_axis=0, tiled=True
    )
    block_pick = (
        arrived_ids.reshape(-1)[:, None] == jnp.arange(blocks, dtype=jnp.int32)[None, :]
    ).astype(jnp.float32)
    return jnp.einsum(
        "sk,sx->kx", block_pick, arrived.reshape(-1, width), precision=lax.Precision.HIGHEST
    )


def pair_exchange(runoff_t, block_ids, blocks, shards):
    chains = lax.axis_size("basin")
    across = lax.axis_size("x")
    sub_steps, tile_count, reaches = runoff_t.shape
    width = sub_steps * reaches
    core = lax.axis_index("core")
    owners = jnp.arange(chains * across, dtype=jnp.int32)[:, None] * 2
    slots = jnp.arange(blocks, dtype=jnp.int32)[None, :]

    def side_sums(side):
        wanted = ((owners + side) * blocks + slots).reshape(-1)
        pick = (block_ids[None, :] == wanted[:, None]).astype(jnp.float32)
        return jnp.einsum("gk,tkc->gtc", pick, runoff_t, precision=lax.Precision.HIGHEST)

    moved = lax.ppermute(side_sums(1 - core), "core", [(0, 1), (1, 0)])
    chip_sum = (side_sums(core) + moved).reshape(chains * across, blocks, width)
    arrived = lax.all_to_all(chip_sum, ("basin", "x"), split_axis=0, concat_axis=0, tiled=True)
    return jnp.sum(arrived, axis=0)


def local(
    precip,
    soil_water,
    capacity,
    evap_rate,
    tile_dest,
    tile_block,
    trib_op,
    trib_keep,
    trib_prev,
    trib_river,
    trib_reach,
    main_op,
    main_keep,
    main_prev,
    head_inflow,
):
    tile_count = precip.shape[0]
    sub_steps = precip.shape[1]
    reaches = precip.shape[2]
    blocks = trib_op.shape[0]
    chains = lax.axis_size("basin")
    rivers = lax.axis_size(BAND)
    shards = chains * rivers
    grid = GRID
    operator = main_op[0, 0]
    keep_main = main_keep[0, 0]
    prev_main = main_prev[0, 0]

    runoff_t, water = land_update_t(jnp.transpose(precip, (1, 0, 2)), soil_water, capacity, evap_rate)
    lateral = gather_lateral(runoff_t, tile_dest, tile_block, blocks, shards)
    trib_mixed = jnp.einsum(
        "brc,btc->btr",
        trib_op,
        lateral.reshape(blocks, sub_steps, reaches),
        precision=lax.Precision.HIGHEST,
    )
    trib_flows = route_series(trib_mixed, trib_keep, trib_prev)
    exit_mixed = jnp.sum(
        lateral.reshape(blocks, sub_steps, reaches) * trib_op[:, reaches - 1][:, None, :], axis=2
    )
    outlet = route_series(
        exit_mixed[:, :, None], trib_keep[:, reaches - 1 :], trib_prev[:, reaches - 1 :]
    )[:, :, 0]

    mine = lax.axis_index(BAND)
    me = lax.axis_index("basin")
    spread_lanes = reaches // blocks
    if reaches % blocks == 0 and sub_steps + 4 + spread_lanes <= reaches:
        lane = lax.broadcasted_iota(jnp.int32, (blocks, reaches), 1)
        columns = (
            trib_river.astype(jnp.float32)[:, None],
            trib_reach.astype(jnp.float32)[:, None],
            keep_main[reaches - 1 :][None, :],
            prev_main[reaches - 1 :][None, :],
        )
        spread_row = operator[reaches - 1].reshape(blocks, spread_lanes)
        static_tile = jnp.pad(
            spread_row, ((0, 0), (sub_steps + 4, reaches - sub_steps - 4 - spread_lanes))
        )
        for offset, value in enumerate(columns):
            static_tile = static_tile + jnp.where(lane == sub_steps + offset, value, 0.0)
        tile = jnp.pad(outlet, ((0, 0), (0, reaches - sub_steps))) + static_tile
        every = lax.all_to_all(
            jnp.broadcast_to(tile[None], (shards,) + tile.shape), grid, split_axis=0, concat_axis=0, tiled=True
        )
        outlets = every[:, :, :sub_steps].reshape(chains, rivers * blocks, sub_steps)
        river_of = every[:, :, sub_steps].reshape(chains, rivers * blocks)
        reach_of = every[:, :, sub_steps + 1].reshape(chains, rivers * blocks)
        facts = lax.dynamic_index_in_dim(
            every.reshape(chains, rivers, blocks, reaches), mine, axis=1, keepdims=False
        )
        keeps = facts[:, 0, sub_steps + 2]
        starts = facts[:, 0, sub_steps + 3]
        exit_rows = facts[:, :, sub_steps + 4 : sub_steps + 4 + spread_lanes].reshape(chains, reaches)
    else:
        payload = jnp.concatenate(
            [
                outlet.reshape(-1),
                trib_river.astype(jnp.float32),
                trib_reach.astype(jnp.float32),
                operator[reaches - 1],
                keep_main[reaches - 1 :],
                prev_main[reaches - 1 :],
            ]
        )
        width = payload.shape[0]
        padded = -(-width // 128) * 128
        payload = jnp.pad(payload, (0, padded - width))
        every = lax.all_to_all(
            jnp.broadcast_to(payload[None], (shards, padded)), grid, split_axis=0, concat_axis=0, tiled=True
        )
        at = 0
        outlets = every[:, at : at + blocks * sub_steps].reshape(chains, rivers * blocks, sub_steps)
        at += blocks * sub_steps
        river_of = every[:, at : at + blocks].reshape(chains, rivers * blocks)
        at += blocks
        reach_of = every[:, at : at + blocks].reshape(chains, rivers * blocks)
        at += blocks
        exit_rows = lax.dynamic_index_in_dim(
            every[:, at : at + reaches].reshape(chains, rivers, reaches), mine, axis=1, keepdims=False
        )
        at += reaches
        keeps = lax.dynamic_index_in_dim(
            every[:, at].reshape(chains, rivers), mine, axis=1, keepdims=False
        )
        starts = lax.dynamic_index_in_dim(
            every[:, at + 1].reshape(chains, rivers), mine, axis=1, keepdims=False
        )

    joins = (river_of == mine.astype(jnp.float32))[:, :, None] & (
        reach_of[:, :, None] == jnp.arange(reaches, dtype=jnp.float32)[None, None, :]
    )
    weight = joins.astype(jnp.float32)
    branch_all = jnp.sum(weight[:, :, None, :] * outlets[:, :, :, None], axis=1)
    branch_exit = jnp.sum(branch_all * exit_rows[:, None, :], axis=2)

    flow = starts
    free_exit = []
    for sub_step in range(sub_steps):
        flow = keeps * flow + (1.0 - keeps) * branch_exit[:, sub_step]
        free_exit.append(flow)
    free_exit = jnp.stack(free_exit, axis=1)
    lag = jnp.arange(sub_steps)[:, None] - jnp.arange(sub_steps)[None, :]
    lag_f = jnp.maximum(lag, 0).astype(jnp.float32)
    response = jnp.where(
        lag[None] >= 0,
        (exit_rows[:, 0] * (1.0 - keeps))[:, None, None] * keeps[:, None, None] ** lag_f[None],
        0.0,
    )

    def advance(section, entry):
        moved = jnp.sum(response[section] * entry[None, :], axis=1) + free_exit[section]
        return jnp.where(section < me, moved, entry)

    entry = lax.fori_loop(0, chains, advance, head_inflow[0], unroll=chains <= 16)

    branch_in = lax.dynamic_index_in_dim(branch_all, me, axis=0, keepdims=False)
    first_reach = (jnp.arange(reaches) == 0).astype(jnp.float32)
    fed = branch_in + entry[:, None] * first_reach[None, :]
    main_mixed = jnp.einsum("rc,tc->tr", operator, fed, precision=lax.Precision.HIGHEST)
    main_flows = route_series(main_mixed, keep_main, prev_main)
    return (water, trib_flows[:, sub_steps - 1], main_flows[None, None])


def cores_paired(mesh):
    try:
        grid = mesh.devices
        if grid.ndim != 2 or grid.shape[1] % 2:
            return False
        for row in grid:
            for m in range(0, len(row), 2):
                a, b = row[m], row[m + 1]
                if tuple(a.coords) != tuple(b.coords) or a.core_on_chip == b.core_on_chip:
                    return False
        return True
    except AttributeError:
        return False


PAIRED = False
BAND = "band"
GRID = ("basin", "band")


def solution(mesh):
    global PAIRED, BAND, GRID
    PAIRED = cores_paired(mesh)
    if PAIRED:
        grid = mesh.devices
        mesh = Mesh(grid.reshape(grid.shape[0], grid.shape[1] // 2, 2), ("basin", "x", "core"))
        BAND, GRID = ("x", "core"), ("basin", "x", "core")
    else:
        BAND, GRID = "band", ("basin", "band")
    return jax.shard_map(
        local,
        mesh=mesh,
        in_specs=(
            P(GRID, None, None),
            P(GRID, None),
            P(GRID, None),
            P(GRID, None),
            P(GRID),
            P(GRID),
            P(GRID, None, None),
            P(GRID, None),
            P(GRID, None),
            P(GRID),
            P(GRID),
            P(BAND, "basin", None, None),
            P(BAND, "basin", None),
            P(BAND, "basin", None),
            P(BAND, None),
        ),
        out_specs=(
            P(GRID, None),
            P(GRID, None),
            P(BAND, "basin", None, None),
        ),
        check_vma=False,
    )
```

```python
import jax
import jax.numpy as jnp
from jax import lax
from jax.sharding import Mesh, PartitionSpec as P


def land_update(precip, soil_water, capacity, evap_rate):
    water = soil_water
    runoff_steps = []
    for sub_step in range(precip.shape[1]):
        rain_now = precip[:, sub_step]
        runoff_now = rain_now * water / (water + capacity)
        water = (1.0 - evap_rate) * water + rain_now - runoff_now
        runoff_steps.append(runoff_now)
    return (jnp.stack(runoff_steps, axis=1), water)


def land_update_t(precip_t, soil_water, capacity, evap_rate):
    water = soil_water
    runoff_steps = []
    for sub_step in range(precip_t.shape[0]):
        rain_now = precip_t[sub_step]
        runoff_now = rain_now * water / (water + capacity)
        water = (1.0 - evap_rate) * water + rain_now - runoff_now
        runoff_steps.append(runoff_now)
    return (jnp.stack(runoff_steps, axis=0), water)


def route_series(mixed, keep, previous):
    flow = previous
    flows = []
    for sub_step in range(mixed.shape[-2]):
        flow = keep * flow + (1.0 - keep) * mixed[..., sub_step, :]
        flows.append(flow)
    return jnp.stack(flows, axis=-2)


def pack_slots(values, labels, targets, peer_count, slot_cap):
    entries = targets.shape[0]
    position = jnp.arange(entries, dtype=jnp.int32)
    earlier = (targets[:, None] == targets[None, :]) & (position[None, :] < position[:, None])
    ranking = jnp.sum(earlier.astype(jnp.int32), axis=1)
    target_slot = targets * slot_cap + ranking
    buffer = (
        jnp.zeros((peer_count * slot_cap, values.shape[1]), values.dtype)
        .at[target_slot]
        .set(values)
    )
    slot_labels = jnp.zeros((peer_count * slot_cap,), jnp.int32).at[target_slot].set(labels)
    return (buffer, slot_labels)


def gather_lateral(runoff_t, tile_dest, tile_block, blocks, shards):
    sub_steps, tile_count, reaches = runoff_t.shape
    width = sub_steps * reaches
    tile_cap = max(2, 2 * tile_count // shards)
    grid = GRID
    if tile_cap >= blocks:
        block_ids = tile_dest * blocks + tile_block
        pick = (
            block_ids[None, :] == jnp.arange(shards * blocks, dtype=jnp.int32)[:, None]
        ).astype(jnp.float32)
        dense = jnp.einsum(
            "gk,tkc->gtc", pick, runoff_t, precision=lax.Precision.HIGHEST
        ).reshape(shards * blocks, width)
        if not PAIRED or blocks % 2:
            arrived = lax.all_to_all(
                dense.reshape(shards, blocks, width), grid, split_axis=0, concat_axis=0, tiled=True
            )
            return jnp.sum(arrived, axis=0)
        return pair_exchange(dense, blocks, shards)
    runoff = jnp.transpose(runoff_t, (1, 0, 2)).reshape(tile_count, width)
    buffer, slot_labels = pack_slots(runoff, tile_block, tile_dest, shards, tile_cap)
    arrived = lax.all_to_all(
        buffer.reshape(shards, tile_cap, width), grid, split_axis=0, concat_axis=0, tiled=True
    )
    arrived_ids = lax.all_to_all(
        slot_labels.reshape(shards, tile_cap), grid, split_axis=0, concat_axis=0, tiled=True
    )
    block_pick = (
        arrived_ids.reshape(-1)[:, None] == jnp.arange(blocks, dtype=jnp.int32)[None, :]
    ).astype(jnp.float32)
    return jnp.einsum(
        "sk,sx->kx", block_pick, arrived.reshape(-1, width), precision=lax.Precision.HIGHEST
    )


def pair_exchange(dense, blocks, shards):
    chains = lax.axis_size("basin")
    across = lax.axis_size("x")
    width = dense.shape[1]
    core = lax.axis_index("core")
    parts = dense.reshape(chains, across, 2, blocks, width)
    keep_side = lax.dynamic_index_in_dim(parts, core, axis=2, keepdims=False)
    give_side = lax.dynamic_index_in_dim(parts, 1 - core, axis=2, keepdims=False)
    chip_sum = keep_side + lax.ppermute(give_side, "core", [(0, 1), (1, 0)])
    arrived = lax.all_to_all(
        chip_sum.reshape(chains * across, blocks, width), ("basin", "x"), split_axis=0, concat_axis=0, tiled=True
    )
    return jnp.sum(arrived, axis=0)


def local(
    precip,
    soil_water,
    capacity,
    evap_rate,
    tile_dest,
    tile_block,
    trib_op,
    trib_keep,
    trib_prev,
    trib_river,
    trib_reach,
    main_op,
    main_keep,
    main_prev,
    head_inflow,
):
    tile_count = precip.shape[0]
    sub_steps = precip.shape[1]
    reaches = precip.shape[2]
    blocks = trib_op.shape[0]
    chains = lax.axis_size("basin")
    rivers = lax.axis_size(BAND)
    shards = chains * rivers
    grid = GRID
    operator = main_op[0, 0]
    keep_main = main_keep[0, 0]
    prev_main = main_prev[0, 0]

    runoff_t, water = land_update_t(jnp.transpose(precip, (1, 0, 2)), soil_water, capacity, evap_rate)
    lateral = gather_lateral(runoff_t, tile_dest, tile_block, blocks, shards)
    exit_mixed = jnp.sum(
        lateral.reshape(blocks, sub_steps, reaches) * trib_op[:, reaches - 1][:, None, :], axis=2
    )
    outlet = route_series(
        exit_mixed[:, :, None], trib_keep[:, reaches - 1 :], trib_prev[:, reaches - 1 :]
    )[:, :, 0]

    mine = lax.axis_index(BAND)
    me = lax.axis_index("basin")
    spread_lanes = reaches // blocks
    if reaches % blocks == 0 and sub_steps + 4 + spread_lanes <= reaches:
        lane = lax.broadcasted_iota(jnp.int32, (blocks, reaches), 1)
        columns = (
            trib_river.astype(jnp.float32)[:, None],
            trib_reach.astype(jnp.float32)[:, None],
            keep_main[reaches - 1 :][None, :],
            prev_main[reaches - 1 :][None, :],
        )
        spread_row = operator[reaches - 1].reshape(blocks, spread_lanes)
        static_tile = jnp.pad(
            spread_row, ((0, 0), (sub_steps + 4, reaches - sub_steps - 4 - spread_lanes))
        )
        for offset, value in enumerate(columns):
            static_tile = static_tile + jnp.where(lane == sub_steps + offset, value, 0.0)
        tile = jnp.pad(outlet, ((0, 0), (0, reaches - sub_steps))) + static_tile
        outgoing = jnp.broadcast_to(tile[None], (shards,) + tile.shape)
        every = lax.all_to_all(outgoing, grid, split_axis=0, concat_axis=0, tiled=True)
        outlets = every[:, :, :sub_steps].reshape(chains, rivers * blocks, sub_steps)
        river_of = every[:, :, sub_steps].reshape(chains, rivers * blocks)
        reach_of = every[:, :, sub_steps + 1].reshape(chains, rivers * blocks)
        facts = lax.dynamic_index_in_dim(
            every.reshape(chains, rivers, blocks, reaches), mine, axis=1, keepdims=False
        )
        keeps = facts[:, 0, sub_steps + 2]
        starts = facts[:, 0, sub_steps + 3]
        exit_rows = facts[:, :, sub_steps + 4 : sub_steps + 4 + spread_lanes].reshape(chains, reaches)
    else:
        payload = jnp.concatenate(
            [
                outlet.reshape(-1),
                trib_river.astype(jnp.float32),
                trib_reach.astype(jnp.float32),
                operator[reaches - 1],
                keep_main[reaches - 1 :],
                prev_main[reaches - 1 :],
            ]
        )
        width = payload.shape[0]
        padded = -(-width // 128) * 128
        payload = jnp.pad(payload, (0, padded - width))
        outgoing = jnp.broadcast_to(payload[None], (shards, padded))
        every = lax.all_to_all(outgoing, grid, split_axis=0, concat_axis=0, tiled=True)
        at = 0
        outlets = every[:, at : at + blocks * sub_steps].reshape(chains, rivers * blocks, sub_steps)
        at += blocks * sub_steps
        river_of = every[:, at : at + blocks].reshape(chains, rivers * blocks)
        at += blocks
        reach_of = every[:, at : at + blocks].reshape(chains, rivers * blocks)
        at += blocks
        exit_rows = lax.dynamic_index_in_dim(
            every[:, at : at + reaches].reshape(chains, rivers, reaches), mine, axis=1, keepdims=False
        )
        at += reaches
        keeps = lax.dynamic_index_in_dim(
            every[:, at].reshape(chains, rivers), mine, axis=1, keepdims=False
        )
        starts = lax.dynamic_index_in_dim(
            every[:, at + 1].reshape(chains, rivers), mine, axis=1, keepdims=False
        )

    lateral_late, _ = lax.optimization_barrier((lateral, outgoing))
    trib_mixed = jnp.einsum(
        "brc,btc->btr",
        trib_op,
        lateral_late.reshape(blocks, sub_steps, reaches),
        precision=lax.Precision.HIGHEST,
    )
    trib_flows = route_series(trib_mixed, trib_keep, trib_prev)

    joins = (river_of == mine.astype(jnp.float32))[:, :, None] & (
        reach_of[:, :, None] == jnp.arange(reaches, dtype=jnp.float32)[None, None, :]
    )
    weight = joins.astype(jnp.float32)
    branch_all = jnp.sum(weight[:, :, None, :] * outlets[:, :, :, None], axis=1)
    branch_exit = jnp.sum(branch_all * exit_rows[:, None, :], axis=2)

    flow = starts
    free_exit = []
    for sub_step in range(sub_steps):
        flow = keeps * flow + (1.0 - keeps) * branch_exit[:, sub_step]
        free_exit.append(flow)
    free_exit = jnp.stack(free_exit, axis=1)
    lag = jnp.arange(sub_steps)[:, None] - jnp.arange(sub_steps)[None, :]
    lag_f = jnp.maximum(lag, 0).astype(jnp.float32)
    response = jnp.where(
        lag[None] >= 0,
        (exit_rows[:, 0] * (1.0 - keeps))[:, None, None] * keeps[:, None, None] ** lag_f[None],
        0.0,
    )

    def advance(section, entry):
        moved = jnp.sum(response[section] * entry[None, :], axis=1) + free_exit[section]
        return jnp.where(section < me, moved, entry)

    entry = lax.fori_loop(0, chains, advance, head_inflow[0], unroll=chains <= 16)

    branch_in = lax.dynamic_index_in_dim(branch_all, me, axis=0, keepdims=False)
    first_reach = (jnp.arange(reaches) == 0).astype(jnp.float32)
    fed = branch_in + entry[:, None] * first_reach[None, :]
    main_mixed = jnp.einsum("rc,tc->tr", operator, fed, precision=lax.Precision.HIGHEST)
    main_flows = route_series(main_mixed, keep_main, prev_main)
    return (water, trib_flows[:, sub_steps - 1], main_flows[None, None])


def cores_paired(mesh):
    try:
        grid = mesh.devices
        if grid.ndim != 2 or grid.shape[1] % 2:
            return False
        for row in grid:
            for m in range(0, len(row), 2):
                a, b = row[m], row[m + 1]
                if tuple(a.coords) != tuple(b.coords) or a.core_on_chip == b.core_on_chip:
                    return False
        return True
    except AttributeError:
        return False


PAIRED = False
BAND = "band"
GRID = ("basin", "band")


def solution(mesh):
    global PAIRED, BAND, GRID
    PAIRED = cores_paired(mesh)
    if PAIRED:
        grid = mesh.devices
        mesh = Mesh(grid.reshape(grid.shape[0], grid.shape[1] // 2, 2), ("basin", "x", "core"))
        BAND, GRID = ("x", "core"), ("basin", "x", "core")
    else:
        BAND, GRID = "band", ("basin", "band")
    return jax.shard_map(
        local,
        mesh=mesh,
        in_specs=(
            P(GRID, None, None),
            P(GRID, None),
            P(GRID, None),
            P(GRID, None),
            P(GRID),
            P(GRID),
            P(GRID, None, None),
            P(GRID, None),
            P(GRID, None),
            P(GRID),
            P(GRID),
            P(BAND, "basin", None, None),
            P(BAND, "basin", None),
            P(BAND, "basin", None),
            P(BAND, None),
        ),
        out_specs=(
            P(GRID, None),
            P(GRID, None),
            P(BAND, "basin", None, None),
        ),
        check_vma=False,
    )
```

```python
import jax
import jax.numpy as jnp
from jax import lax
from jax.sharding import Mesh, PartitionSpec as P


def land_update(precip, soil_water, capacity, evap_rate):
    water = soil_water
    runoff_steps = []
    for sub_step in range(precip.shape[1]):
        rain_now = precip[:, sub_step]
        runoff_now = rain_now * water / (water + capacity)
        water = (1.0 - evap_rate) * water + rain_now - runoff_now
        runoff_steps.append(runoff_now)
    return (jnp.stack(runoff_steps, axis=1), water)


def land_update_t(precip_t, soil_water, capacity, evap_rate):
    water = soil_water
    runoff_steps = []
    for sub_step in range(precip_t.shape[0]):
        rain_now = precip_t[sub_step]
        runoff_now = rain_now * water / (water + capacity)
        water = (1.0 - evap_rate) * water + rain_now - runoff_now
        runoff_steps.append(runoff_now)
    return (jnp.stack(runoff_steps, axis=0), water)


def route_series(mixed, keep, previous):
    flow = previous
    flows = []
    for sub_step in range(mixed.shape[-2]):
        flow = keep * flow + (1.0 - keep) * mixed[..., sub_step, :]
        flows.append(flow)
    return jnp.stack(flows, axis=-2)


def pack_slots(values, labels, targets, peer_count, slot_cap):
    entries = targets.shape[0]
    position = jnp.arange(entries, dtype=jnp.int32)
    earlier = (targets[:, None] == targets[None, :]) & (position[None, :] < position[:, None])
    ranking = jnp.sum(earlier.astype(jnp.int32), axis=1)
    target_slot = targets * slot_cap + ranking
    buffer = (
        jnp.zeros((peer_count * slot_cap, values.shape[1]), values.dtype)
        .at[target_slot]
        .set(values)
    )
    slot_labels = jnp.zeros((peer_count * slot_cap,), jnp.int32).at[target_slot].set(labels)
    return (buffer, slot_labels)


def gather_lateral(runoff_t, tile_dest, tile_block, blocks, shards):
    sub_steps, tile_count, reaches = runoff_t.shape
    width = sub_steps * reaches
    tile_cap = max(2, 2 * tile_count // shards)
    grid = GRID
    if tile_cap >= blocks:
        block_ids = tile_dest * blocks + tile_block
        pick = (
            block_ids[None, :] == jnp.arange(shards * blocks, dtype=jnp.int32)[:, None]
        ).astype(jnp.float32)
        dense = jnp.einsum("gk,tkc->gtc", pick, runoff_t, precision=lax.Precision.HIGHEST)
        if not PAIRED or blocks % 2:
            arrived = lax.all_to_all(
                dense.reshape(shards, blocks, width), grid, split_axis=0, concat_axis=0, tiled=True
            )
            return jnp.sum(arrived, axis=0)
        return pair_exchange(dense, blocks, shards).reshape(blocks, width)
    runoff = jnp.transpose(runoff_t, (1, 0, 2)).reshape(tile_count, width)
    buffer, slot_labels = pack_slots(runoff, tile_block, tile_dest, shards, tile_cap)
    arrived = lax.all_to_all(
        buffer.reshape(shards, tile_cap, width), grid, split_axis=0, concat_axis=0, tiled=True
    )
    arrived_ids = lax.all_to_all(
        slot_labels.reshape(shards, tile_cap), grid, split_axis=0, concat_axis=0, tiled=True
    )
    block_pick = (
        arrived_ids.reshape(-1)[:, None] == jnp.arange(blocks, dtype=jnp.int32)[None, :]
    ).astype(jnp.float32)
    return jnp.einsum(
        "sk,sx->kx", block_pick, arrived.reshape(-1, width), precision=lax.Precision.HIGHEST
    )


def pair_exchange(dense, blocks, shards):
    chains = lax.axis_size("basin")
    across = lax.axis_size("x")
    tail = dense.shape[1:]
    core = lax.axis_index("core")
    parts = dense.reshape((chains, across, 2, blocks) + tail)
    keep_side = lax.dynamic_index_in_dim(parts, core, axis=2, keepdims=False)
    give_side = lax.dynamic_index_in_dim(parts, 1 - core, axis=2, keepdims=False)
    chip_sum = keep_side + lax.ppermute(give_side, "core", [(0, 1), (1, 0)])
    arrived = lax.all_to_all(
        chip_sum.reshape((chains * across, blocks) + tail), ("basin", "x"), split_axis=0, concat_axis=0, tiled=True
    )
    return jnp.sum(arrived, axis=0)


def local(
    precip,
    soil_water,
    capacity,
    evap_rate,
    tile_dest,
    tile_block,
    trib_op,
    trib_keep,
    trib_prev,
    trib_river,
    trib_reach,
    main_op,
    main_keep,
    main_prev,
    head_inflow,
):
    tile_count = precip.shape[0]
    sub_steps = precip.shape[1]
    reaches = precip.shape[2]
    blocks = trib_op.shape[0]
    chains = lax.axis_size("basin")
    rivers = lax.axis_size(BAND)
    shards = chains * rivers
    grid = GRID
    operator = main_op[0, 0]
    keep_main = main_keep[0, 0]
    prev_main = main_prev[0, 0]

    runoff_t, water = land_update_t(jnp.transpose(precip, (1, 0, 2)), soil_water, capacity, evap_rate)
    lateral = gather_lateral(runoff_t, tile_dest, tile_block, blocks, shards)
    exit_mixed = jnp.sum(
        lateral.reshape(blocks, sub_steps, reaches) * trib_op[:, reaches - 1][:, None, :], axis=2
    )
    outlet = route_series(
        exit_mixed[:, :, None], trib_keep[:, reaches - 1 :], trib_prev[:, reaches - 1 :]
    )[:, :, 0]

    mine = lax.axis_index(BAND)
    me = lax.axis_index("basin")
    spread_lanes = reaches // blocks
    if reaches % blocks == 0 and sub_steps + 4 + spread_lanes <= reaches:
        lane = lax.broadcasted_iota(jnp.int32, (blocks, reaches), 1)
        columns = (
            trib_river.astype(jnp.float32)[:, None],
            trib_reach.astype(jnp.float32)[:, None],
            keep_main[reaches - 1 :][None, :],
            prev_main[reaches - 1 :][None, :],
        )
        spread_row = operator[reaches - 1].reshape(blocks, spread_lanes)
        static_tile = jnp.pad(
            spread_row, ((0, 0), (sub_steps + 4, reaches - sub_steps - 4 - spread_lanes))
        )
        for offset, value in enumerate(columns):
            static_tile = static_tile + jnp.where(lane == sub_steps + offset, value, 0.0)
        tile = jnp.pad(outlet, ((0, 0), (0, reaches - sub_steps))) + static_tile
        outgoing = jnp.broadcast_to(tile[None], (shards,) + tile.shape)
        every = lax.all_to_all(outgoing, grid, split_axis=0, concat_axis=0, tiled=True)
        outlets = every[:, :, :sub_steps].reshape(chains, rivers * blocks, sub_steps)
        river_of = every[:, :, sub_steps].reshape(chains, rivers * blocks)
        reach_of = every[:, :, sub_steps + 1].reshape(chains, rivers * blocks)
        facts = lax.dynamic_index_in_dim(
            every.reshape(chains, rivers, blocks, reaches), mine, axis=1, keepdims=False
        )
        keeps = facts[:, 0, sub_steps + 2]
        starts = facts[:, 0, sub_steps + 3]
        exit_rows = facts[:, :, sub_steps + 4 : sub_steps + 4 + spread_lanes].reshape(chains, reaches)
    else:
        payload = jnp.concatenate(
            [
                outlet.reshape(-1),
                trib_river.astype(jnp.float32),
                trib_reach.astype(jnp.float32),
                operator[reaches - 1],
                keep_main[reaches - 1 :],
                prev_main[reaches - 1 :],
            ]
        )
        width = payload.shape[0]
        padded = -(-width // 128) * 128
        payload = jnp.pad(payload, (0, padded - width))
        outgoing = jnp.broadcast_to(payload[None], (shards, padded))
        every = lax.all_to_all(outgoing, grid, split_axis=0, concat_axis=0, tiled=True)
        at = 0
        outlets = every[:, at : at + blocks * sub_steps].reshape(chains, rivers * blocks, sub_steps)
        at += blocks * sub_steps
        river_of = every[:, at : at + blocks].reshape(chains, rivers * blocks)
        at += blocks
        reach_of = every[:, at : at + blocks].reshape(chains, rivers * blocks)
        at += blocks
        exit_rows = lax.dynamic_index_in_dim(
            every[:, at : at + reaches].reshape(chains, rivers, reaches), mine, axis=1, keepdims=False
        )
        at += reaches
        keeps = lax.dynamic_index_in_dim(
            every[:, at].reshape(chains, rivers), mine, axis=1, keepdims=False
        )
        starts = lax.dynamic_index_in_dim(
            every[:, at + 1].reshape(chains, rivers), mine, axis=1, keepdims=False
        )

    lateral_late, _ = lax.optimization_barrier((lateral, outgoing))
    trib_mixed = jnp.einsum(
        "brc,btc->btr",
        trib_op,
        lateral_late.reshape(blocks, sub_steps, reaches),
        precision=lax.Precision.HIGHEST,
    )
    trib_flows = route_series(trib_mixed, trib_keep, trib_prev)

    joins = (river_of == mine.astype(jnp.float32))[:, :, None] & (
        reach_of[:, :, None] == jnp.arange(reaches, dtype=jnp.float32)[None, None, :]
    )
    weight = joins.astype(jnp.float32)
    branch_all = jnp.sum(weight[:, :, None, :] * outlets[:, :, :, None], axis=1)
    branch_exit = jnp.sum(branch_all * exit_rows[:, None, :], axis=2)

    flow = starts
    free_exit = []
    for sub_step in range(sub_steps):
        flow = keeps * flow + (1.0 - keeps) * branch_exit[:, sub_step]
        free_exit.append(flow)
    free_exit = jnp.stack(free_exit, axis=1)
    lag = jnp.arange(sub_steps)[:, None] - jnp.arange(sub_steps)[None, :]
    lag_f = jnp.maximum(lag, 0).astype(jnp.float32)
    response = jnp.where(
        lag[None] >= 0,
        (exit_rows[:, 0] * (1.0 - keeps))[:, None, None] * keeps[:, None, None] ** lag_f[None],
        0.0,
    )

    def advance(section, entry):
        moved = jnp.sum(response[section] * entry[None, :], axis=1) + free_exit[section]
        return jnp.where(section < me, moved, entry)

    entry = lax.fori_loop(0, chains, advance, head_inflow[0], unroll=chains <= 16)

    branch_in = lax.dynamic_index_in_dim(branch_all, me, axis=0, keepdims=False)
    first_reach = (jnp.arange(reaches) == 0).astype(jnp.float32)
    fed = branch_in + entry[:, None] * first_reach[None, :]
    main_mixed = jnp.einsum("rc,tc->tr", operator, fed, precision=lax.Precision.HIGHEST)
    main_flows = route_series(main_mixed, keep_main, prev_main)
    return (water, trib_flows[:, sub_steps - 1], main_flows[None, None])


def cores_paired(mesh):
    try:
        grid = mesh.devices
        if grid.ndim != 2 or grid.shape[1] % 2:
            return False
        for row in grid:
            for m in range(0, len(row), 2):
                a, b = row[m], row[m + 1]
                if tuple(a.coords) != tuple(b.coords) or a.core_on_chip == b.core_on_chip:
                    return False
        return True
    except AttributeError:
        return False


PAIRED = False
BAND = "band"
GRID = ("basin", "band")


def solution(mesh):
    global PAIRED, BAND, GRID
    PAIRED = cores_paired(mesh)
    if PAIRED:
        grid = mesh.devices
        mesh = Mesh(grid.reshape(grid.shape[0], grid.shape[1] // 2, 2), ("basin", "x", "core"))
        BAND, GRID = ("x", "core"), ("basin", "x", "core")
    else:
        BAND, GRID = "band", ("basin", "band")
    return jax.shard_map(
        local,
        mesh=mesh,
        in_specs=(
            P(GRID, None, None),
            P(GRID, None),
            P(GRID, None),
            P(GRID, None),
            P(GRID),
            P(GRID),
            P(GRID, None, None),
            P(GRID, None),
            P(GRID, None),
            P(GRID),
            P(GRID),
            P(BAND, "basin", None, None),
            P(BAND, "basin", None),
            P(BAND, "basin", None),
            P(BAND, None),
        ),
        out_specs=(
            P(GRID, None),
            P(GRID, None),
            P(BAND, "basin", None, None),
        ),
        check_vma=False,
    )
```

```python
import jax
import jax.numpy as jnp
from jax import lax
from jax.sharding import Mesh, PartitionSpec as P


def land_update(precip, soil_water, capacity, evap_rate):
    water = soil_water
    runoff_steps = []
    for sub_step in range(precip.shape[1]):
        rain_now = precip[:, sub_step]
        runoff_now = rain_now * water / (water + capacity)
        water = (1.0 - evap_rate) * water + rain_now - runoff_now
        runoff_steps.append(runoff_now)
    return (jnp.stack(runoff_steps, axis=1), water)


def land_update_t(precip_t, soil_water, capacity, evap_rate):
    water = soil_water
    runoff_steps = []
    for sub_step in range(precip_t.shape[0]):
        rain_now = precip_t[sub_step]
        runoff_now = rain_now * water / (water + capacity)
        water = (1.0 - evap_rate) * water + rain_now - runoff_now
        runoff_steps.append(runoff_now)
    return (jnp.stack(runoff_steps, axis=0), water)


def route_series(mixed, keep, previous):
    flow = previous
    flows = []
    for sub_step in range(mixed.shape[-2]):
        flow = keep * flow + (1.0 - keep) * mixed[..., sub_step, :]
        flows.append(flow)
    return jnp.stack(flows, axis=-2)


def pack_slots(values, labels, targets, peer_count, slot_cap):
    entries = targets.shape[0]
    position = jnp.arange(entries, dtype=jnp.int32)
    earlier = (targets[:, None] == targets[None, :]) & (position[None, :] < position[:, None])
    ranking = jnp.sum(earlier.astype(jnp.int32), axis=1)
    target_slot = targets * slot_cap + ranking
    buffer = (
        jnp.zeros((peer_count * slot_cap, values.shape[1]), values.dtype)
        .at[target_slot]
        .set(values)
    )
    slot_labels = jnp.zeros((peer_count * slot_cap,), jnp.int32).at[target_slot].set(labels)
    return (buffer, slot_labels)


def gather_lateral(runoff_t, tile_dest, tile_block, blocks, shards):
    sub_steps, tile_count, reaches = runoff_t.shape
    width = sub_steps * reaches
    tile_cap = max(2, 2 * tile_count // shards)
    grid = GRID
    if tile_cap >= blocks:
        block_ids = tile_dest * blocks + tile_block
        pick = (
            block_ids[None, :] == jnp.arange(shards * blocks, dtype=jnp.int32)[:, None]
        ).astype(jnp.float32)
        dense = jnp.einsum(
            "gk,tkc->gtc", pick, runoff_t, precision=lax.Precision.HIGH
        ).reshape(shards * blocks, width)
        if not PAIRED or blocks % 2:
            arrived = lax.all_to_all(
                dense.reshape(shards, blocks, width), grid, split_axis=0, concat_axis=0, tiled=True
            )
            return jnp.sum(arrived, axis=0)
        return pair_exchange(dense, blocks, shards)
    runoff = jnp.transpose(runoff_t, (1, 0, 2)).reshape(tile_count, width)
    buffer, slot_labels = pack_slots(runoff, tile_block, tile_dest, shards, tile_cap)
    arrived = lax.all_to_all(
        buffer.reshape(shards, tile_cap, width), grid, split_axis=0, concat_axis=0, tiled=True
    )
    arrived_ids = lax.all_to_all(
        slot_labels.reshape(shards, tile_cap), grid, split_axis=0, concat_axis=0, tiled=True
    )
    block_pick = (
        arrived_ids.reshape(-1)[:, None] == jnp.arange(blocks, dtype=jnp.int32)[None, :]
    ).astype(jnp.float32)
    return jnp.einsum(
        "sk,sx->kx", block_pick, arrived.reshape(-1, width), precision=lax.Precision.HIGHEST
    )


def pair_exchange(dense, blocks, shards):
    chains = lax.axis_size("basin")
    across = lax.axis_size("x")
    width = dense.shape[1]
    core = lax.axis_index("core")
    parts = dense.reshape(chains, across, 2, blocks, width)
    keep_side = lax.dynamic_index_in_dim(parts, core, axis=2, keepdims=False)
    give_side = lax.dynamic_index_in_dim(parts, 1 - core, axis=2, keepdims=False)
    chip_sum = keep_side + lax.ppermute(give_side, "core", [(0, 1), (1, 0)])
    arrived = lax.all_to_all(
        chip_sum.reshape(chains * across, blocks, width), ("basin", "x"), split_axis=0, concat_axis=0, tiled=True
    )
    return jnp.sum(arrived, axis=0)


def local(
    precip,
    soil_water,
    capacity,
    evap_rate,
    tile_dest,
    tile_block,
    trib_op,
    trib_keep,
    trib_prev,
    trib_river,
    trib_reach,
    main_op,
    main_keep,
    main_prev,
    head_inflow,
):
    tile_count = precip.shape[0]
    sub_steps = precip.shape[1]
    reaches = precip.shape[2]
    blocks = trib_op.shape[0]
    chains = lax.axis_size("basin")
    rivers = lax.axis_size(BAND)
    shards = chains * rivers
    grid = GRID
    operator = main_op[0, 0]
    keep_main = main_keep[0, 0]
    prev_main = main_prev[0, 0]

    runoff_t, water = land_update_t(jnp.transpose(precip, (1, 0, 2)), soil_water, capacity, evap_rate)
    lateral = gather_lateral(runoff_t, tile_dest, tile_block, blocks, shards)
    exit_mixed = jnp.sum(
        lateral.reshape(blocks, sub_steps, reaches) * trib_op[:, reaches - 1][:, None, :], axis=2
    )
    outlet = route_series(
        exit_mixed[:, :, None], trib_keep[:, reaches - 1 :], trib_prev[:, reaches - 1 :]
    )[:, :, 0]

    mine = lax.axis_index(BAND)
    me = lax.axis_index("basin")
    spread_lanes = reaches // blocks
    if reaches % blocks == 0 and sub_steps + 4 + spread_lanes <= reaches:
        lane = lax.broadcasted_iota(jnp.int32, (blocks, reaches), 1)
        columns = (
            trib_river.astype(jnp.float32)[:, None],
            trib_reach.astype(jnp.float32)[:, None],
            keep_main[reaches - 1 :][None, :],
            prev_main[reaches - 1 :][None, :],
        )
        spread_row = operator[reaches - 1].reshape(blocks, spread_lanes)
        static_tile = jnp.pad(
            spread_row, ((0, 0), (sub_steps + 4, reaches - sub_steps - 4 - spread_lanes))
        )
        for offset, value in enumerate(columns):
            static_tile = static_tile + jnp.where(lane == sub_steps + offset, value, 0.0)
        tile = jnp.pad(outlet, ((0, 0), (0, reaches - sub_steps))) + static_tile
        outgoing = jnp.broadcast_to(tile[None], (shards,) + tile.shape)
        every = lax.all_to_all(outgoing, grid, split_axis=0, concat_axis=0, tiled=True)
        outlets = every[:, :, :sub_steps].reshape(chains, rivers * blocks, sub_steps)
        river_of = every[:, :, sub_steps].reshape(chains, rivers * blocks)
        reach_of = every[:, :, sub_steps + 1].reshape(chains, rivers * blocks)
        facts = lax.dynamic_index_in_dim(
            every.reshape(chains, rivers, blocks, reaches), mine, axis=1, keepdims=False
        )
        keeps = facts[:, 0, sub_steps + 2]
        starts = facts[:, 0, sub_steps + 3]
        exit_rows = facts[:, :, sub_steps + 4 : sub_steps + 4 + spread_lanes].reshape(chains, reaches)
    else:
        payload = jnp.concatenate(
            [
                outlet.reshape(-1),
                trib_river.astype(jnp.float32),
                trib_reach.astype(jnp.float32),
                operator[reaches - 1],
                keep_main[reaches - 1 :],
                prev_main[reaches - 1 :],
            ]
        )
        width = payload.shape[0]
        padded = -(-width // 128) * 128
        payload = jnp.pad(payload, (0, padded - width))
        outgoing = jnp.broadcast_to(payload[None], (shards, padded))
        every = lax.all_to_all(outgoing, grid, split_axis=0, concat_axis=0, tiled=True)
        at = 0
        outlets = every[:, at : at + blocks * sub_steps].reshape(chains, rivers * blocks, sub_steps)
        at += blocks * sub_steps
        river_of = every[:, at : at + blocks].reshape(chains, rivers * blocks)
        at += blocks
        reach_of = every[:, at : at + blocks].reshape(chains, rivers * blocks)
        at += blocks
        exit_rows = lax.dynamic_index_in_dim(
            every[:, at : at + reaches].reshape(chains, rivers, reaches), mine, axis=1, keepdims=False
        )
        at += reaches
        keeps = lax.dynamic_index_in_dim(
            every[:, at].reshape(chains, rivers), mine, axis=1, keepdims=False
        )
        starts = lax.dynamic_index_in_dim(
            every[:, at + 1].reshape(chains, rivers), mine, axis=1, keepdims=False
        )

    lateral_late, _ = lax.optimization_barrier((lateral, outgoing))
    trib_mixed = jnp.einsum(
        "brc,btc->btr",
        trib_op,
        lateral_late.reshape(blocks, sub_steps, reaches),
        precision=lax.Precision.HIGHEST,
    )
    trib_flows = route_series(trib_mixed, trib_keep, trib_prev)

    joins = (river_of == mine.astype(jnp.float32))[:, :, None] & (
        reach_of[:, :, None] == jnp.arange(reaches, dtype=jnp.float32)[None, None, :]
    )
    weight = joins.astype(jnp.float32)
    branch_all = jnp.sum(weight[:, :, None, :] * outlets[:, :, :, None], axis=1)
    branch_exit = jnp.sum(branch_all * exit_rows[:, None, :], axis=2)

    flow = starts
    free_exit = []
    for sub_step in range(sub_steps):
        flow = keeps * flow + (1.0 - keeps) * branch_exit[:, sub_step]
        free_exit.append(flow)
    free_exit = jnp.stack(free_exit, axis=1)
    lag = jnp.arange(sub_steps)[:, None] - jnp.arange(sub_steps)[None, :]
    lag_f = jnp.maximum(lag, 0).astype(jnp.float32)
    response = jnp.where(
        lag[None] >= 0,
        (exit_rows[:, 0] * (1.0 - keeps))[:, None, None] * keeps[:, None, None] ** lag_f[None],
        0.0,
    )

    def advance(section, entry):
        moved = jnp.sum(response[section] * entry[None, :], axis=1) + free_exit[section]
        return jnp.where(section < me, moved, entry)

    entry = lax.fori_loop(0, chains, advance, head_inflow[0], unroll=chains <= 16)

    branch_in = lax.dynamic_index_in_dim(branch_all, me, axis=0, keepdims=False)
    first_reach = (jnp.arange(reaches) == 0).astype(jnp.float32)
    fed = branch_in + entry[:, None] * first_reach[None, :]
    main_mixed = jnp.einsum("rc,tc->tr", operator, fed, precision=lax.Precision.HIGHEST)
    main_flows = route_series(main_mixed, keep_main, prev_main)
    return (water, trib_flows[:, sub_steps - 1], main_flows[None, None])


def cores_paired(mesh):
    try:
        grid = mesh.devices
        if grid.ndim != 2 or grid.shape[1] % 2:
            return False
        for row in grid:
            for m in range(0, len(row), 2):
                a, b = row[m], row[m + 1]
                if tuple(a.coords) != tuple(b.coords) or a.core_on_chip == b.core_on_chip:
                    return False
        return True
    except AttributeError:
        return False


PAIRED = False
BAND = "band"
GRID = ("basin", "band")


def solution(mesh):
    global PAIRED, BAND, GRID
    PAIRED = cores_paired(mesh)
    if PAIRED:
        grid = mesh.devices
        mesh = Mesh(grid.reshape(grid.shape[0], grid.shape[1] // 2, 2), ("basin", "x", "core"))
        BAND, GRID = ("x", "core"), ("basin", "x", "core")
    else:
        BAND, GRID = "band", ("basin", "band")
    return jax.shard_map(
        local,
        mesh=mesh,
        in_specs=(
            P(GRID, None, None),
            P(GRID, None),
            P(GRID, None),
            P(GRID, None),
            P(GRID),
            P(GRID),
            P(GRID, None, None),
            P(GRID, None),
            P(GRID, None),
            P(GRID),
            P(GRID),
            P(BAND, "basin", None, None),
            P(BAND, "basin", None),
            P(BAND, "basin", None),
            P(BAND, None),
        ),
        out_specs=(
            P(GRID, None),
            P(GRID, None),
            P(BAND, "basin", None, None),
        ),
        check_vma=False,
    )
```
